32 devices in a mesh: heads: 4 (over y, core), seq: 8 (over z, x).
Axes of the slice: x: 2, y: 2, z: 4, core: 2. Of those that a mesh axis runs over, the one named last changes fastest.
Arguments:
- hidden: bfloat16 [8, 256, 2048], P('seq', 'heads'), may hold values from -6 to 6
- norm_gain: bfloat16 [2048], replicated, may hold values from 0.099609375 to 1.8984375
- router_weight: bfloat16 [2048, 4], replicated, may hold values from -0.125 to 0.125
- att_experts: int32 [8, 256, 2], P('seq'), may hold values from 0 to 3, all different within a row
- q_weight: bfloat16 [4, 2048, 1024], P(None, None, 'heads'), may hold values from -0.125 to 0.125
- kv_weight: bfloat16 [2, 2048, 1024], P(None, None, 'heads'), may hold values from -0.125 to 0.125
- o_weight: bfloat16 [4, 1024, 2048], P(None, 'heads'), may hold values from -1 to 1
- kv_cache: bfloat16 [2, 128, 128, 1024], P(None, 'seq', None, 'heads'), may hold values from -200 to 200
- cached_blocks: int32 [8], replicated, may hold values from 1 to 32, 128 in all
- tail_trim: int32 [8], replicated, may hold values from 0 to 127
- block_pool: int32 [128], replicated, may hold values from 0 to 127, each once
Outputs:
- attn_out: bfloat16 [8, 256, 2048], P('seq', 'heads')
The draws below stay inside these ranges and needn't reach their ends.
Inputs may be any that keep to these rules, and one draw needn't show every extreme that they name: `block_pool`: the cached_blocks sum to 128, so every block belongs to one request.
All inputs are finite; a program needn't handle non-finite values.
Results may differ from the reference program's by a relative error of at most 0.019.
The reference program's roundings to bfloat16 on the way count: a program that leaves them out, or rounds other values in their place, can miss the bound.
Values may be sent and summed in bfloat16 or wider, within the bound.
No kernel may reach another device: no remote copies, remote signals or barrier semaphores. Data moves between devices by JAX's collectives and lax.ppermute only.
A program may use at most 128 MiB of HBM per device.

```python
import math
import jax
import jax.numpy as jnp
import numpy as np
from jax import lax

D = 2048
HD = 128
ATT_EXP = 4
NEW = 256
BLOCK = 128
KVH = 8
REQS = 8
NBLK = 128
LONGB = 32


def draw_kv_cache(key, part):
    shape = (2, NBLK, BLOCK, KVH * HD)
    values = jax.random.normal(key, shape, jnp.float32)
    return values.astype(jnp.bfloat16)


def with_ends(drawn, rng, low, top_value):
    spot = [jax.random.randint(jax.random.fold_in(rng, axis), (), 0, length) for axis, length in enumerate(drawn.shape)]
    main_axis = drawn.shape.index(max(drawn.shape))
    next_to = spot[:main_axis] + [(spot[main_axis] + 1) % drawn.shape[main_axis]] + spot[main_axis + 1:]
    return drawn.at[tuple(spot)].set(low).at[tuple(next_to)].set(top_value)


def shard_levels(own_key, extent, pieces, least, high):
    loudness, own = 1.0, jax.random.fold_in(own_key, 6)
    for axis_at, shards_of in pieces:
        draws = jnp.exp(jax.random.uniform(jax.random.fold_in(own, axis_at), (shards_of,), jnp.float32, least / len(pieces), high / len(pieces)))
        loudness = loudness * jnp.repeat(draws, extent[axis_at] // shards_of).reshape([-1 if axis == axis_at else 1 for axis in range(len(extent))])
    return loudness


def picks_of(stream_key, rows, number_of, top, lift):
    ranking = jax.random.permutation(jax.random.fold_in(stream_key, 1), number_of)
    pull = ranking
    for power in range(3):
        pull = pull * pull // number_of
    pull = pull * lift // number_of
    chance = jax.random.randint(jax.random.fold_in(stream_key, 2), (rows, number_of), 0, 4096) + pull
    holders = jax.random.permutation(jax.random.fold_in(stream_key, 3), rows)[jnp.arange(number_of) % rows]
    chance = jnp.where(jnp.arange(rows)[:, None] == holders[None, :], 1 << 14, chance)
    merit = chance * number_of + jnp.arange(number_of)
    return lax.top_k(merit.astype(jnp.int32), top)[1].astype(jnp.int32)


def length_profile(amount, total, reach, skew):
    portions = [(1 << 20) // math.isqrt(grade ** skew) + 1 for grade in range(2, amount + 1)]
    surplus, counts = total - reach - (amount - 1), [1] * (amount - 1)
    while surplus > 0:
        movable = [i for i in range(amount - 1) if counts[i] < reach]
        whole, budget = sum([portions[i] for i in movable]), surplus
        for i in movable:
            more = min(reach - counts[i], max(1, budget * portions[i] // whole), surplus)
            counts[i] = counts[i] + more
            surplus = surplus - more
    return np.array([reach] + counts)


def uneven(key, amount, total, most, lean):
    if amount == 2:
        one = jax.random.randint(key, (), max(1, total - most), min(most, total - 1) + 1)
        return jnp.stack([one, total - one])
    sizes = jnp.asarray(length_profile(amount, total, most, lean), jnp.int32)
    pairs = (amount - 1) // 2
    giver, taker = sizes[1:1 + 2 * pairs:2], sizes[2:2 + 2 * pairs:2]
    margin = jnp.minimum(giver - 1, most - taker)
    shifted = jax.random.randint(jax.random.fold_in(key, 1), (pairs,), 0, 1 << 20) % (margin + 1)
    sizes = sizes.at[1:1 + 2 * pairs:2].set(giver - shifted).at[2:2 + 2 * pairs:2].set(taker + shifted)
    return sizes[jax.random.permutation(jax.random.fold_in(key, 2), amount)]


def scatter_about(rng, extent, deviation, most, cuts=(), kind=jnp.bfloat16):
    drawn = deviation * jax.random.normal(rng, extent, jnp.float32)
    if cuts:
        drawn = drawn * shard_levels(rng, extent, cuts, -0.22, 0.18)
    return jnp.clip(drawn, -most, most).astype(kind)


def setup_inputs(seed: int = 0) -> dict:
    splits = jax.random.split(jax.random.key(seed), 12)
    hidden = scatter_about(splits[0], (REQS, NEW, D), 1.0, 6.0, ((0, 8), (1, 4)))
    norm_gain = jnp.clip(1.0 + 0.18 * jax.random.normal(splits[1], (D,), jnp.float32), 0.099609375, 1.8984375).astype(jnp.bfloat16)
    router_weight = scatter_about(splits[2], (D, ATT_EXP), D ** -0.5, 0.125)
    att_experts = picks_of(splits[3], REQS * NEW, ATT_EXP, 2, 4096).reshape((REQS, NEW, 2))
    q_weight = scatter_about(splits[4], (ATT_EXP, D, KVH * HD), D ** -0.5, 0.125, ((2, 4),))
    kv_weight = scatter_about(splits[5], (2, D, KVH * HD), D ** -0.5, 0.125, ((2, 4),))
    o_weight = scatter_about(splits[6], (ATT_EXP, KVH * HD, D), (HD // 4) ** -0.5, 1.0, ((1, 4),))
    kv_cache = draw_kv_cache(jax.random.fold_in(splits[11], 71), 0)
    cached_blocks = uneven(splits[8], REQS, NBLK, LONGB, 2).astype(jnp.int32)
    tail_trim = with_ends(jax.random.randint(splits[9], (REQS,), 0, BLOCK), jax.random.fold_in(splits[9], 1), 0, BLOCK - 1).astype(jnp.int32)
    block_pool = jax.random.permutation(splits[10], NBLK).astype(jnp.int32)
    return {"hidden": hidden, "norm_gain": norm_gain, "router_weight": router_weight, "att_experts": att_experts, "q_weight": q_weight, "kv_weight": kv_weight, "o_weight": o_weight, "kv_cache": kv_cache, "cached_blocks": cached_blocks, "tail_trim": tail_trim, "block_pool": block_pool}


NEG_FILL = -1e+30

def rotate(values, positions):
    half_dim = values.shape[-1] // 2
    inverse = 10000.0 ** (-2.0 * jnp.arange(half_dim, dtype=jnp.float32) / values.shape[-1])
    angles = positions.astype(jnp.float32)[:, None] * inverse[None, :]
    target = (values.shape[0],) + (1,) * (values.ndim - 2) + (half_dim,)
    cosine = jnp.cos(angles).reshape(target)
    sine_part = jnp.sin(angles).reshape(target)
    leading_part = values[..., :half_dim]
    trailing_part = values[..., half_dim:]
    return jnp.concatenate([leading_part * cosine - trailing_part * sine_part, trailing_part * cosine + leading_part * sine_part], axis=-1)

def normalize(rows, norm_gain):
    wide_rows = rows.astype(jnp.float32)
    scaled = wide_rows * lax.rsqrt(lax.optimization_barrier(jnp.mean(wide_rows * wide_rows, axis=-1, keepdims=True)) + 1e-05)
    return (scaled * norm_gain.astype(jnp.float32)).astype(jnp.bfloat16)

def route(normed, router_weight, chosen):
    logits = jnp.dot(normed, router_weight, preferred_element_type=jnp.float32)
    experts_all = router_weight.shape[1]
    onehot = (chosen[:, :, None] == jnp.arange(experts_all, dtype=jnp.int32)[None, None, :]).astype(jnp.float32)
    picked = lax.optimization_barrier(jnp.sum(onehot * logits[:, None, :], axis=-1))
    return (onehot, jax.nn.softmax(picked, axis=-1))

def reference(hidden, norm_gain, router_weight, att_experts, q_weight, kv_weight, o_weight, kv_cache, cached_blocks, tail_trim, block_pool):
    cached_len = (cached_blocks * BLOCK - tail_trim).astype(jnp.int32)
    starts = (jnp.cumsum(cached_blocks) - cached_blocks).astype(jnp.int32)
    scale_q = HD ** (-0.5)
    span_len = LONGB * BLOCK

    def one_request(request):
        chosen = att_experts[request]
        normed = normalize(hidden[request], norm_gain)
        onehot, gates = route(normed, router_weight, chosen)
        positions = cached_len[request] + jnp.arange(NEW, dtype=jnp.int32)
        every_q = jnp.einsum('nd,edc->nec', normed.astype(jnp.float32), q_weight.astype(jnp.float32))
        chosen_q = lax.optimization_barrier(jnp.sum(onehot[:, :, :, None] * every_q[:, None, :, :], axis=2)).reshape(NEW, 2, KVH, HD)
        queries = rotate(chosen_q, positions).astype(jnp.bfloat16)
        fresh = jnp.einsum('nd,sdc->snc', normed.astype(jnp.float32), kv_weight.astype(jnp.float32))
        new_keys = rotate(fresh[0].reshape(NEW, KVH, HD), positions).astype(jnp.bfloat16)
        new_values = fresh[1].reshape(NEW, KVH, HD).astype(jnp.bfloat16)
        slots = jnp.clip(starts[request] + jnp.arange(LONGB, dtype=jnp.int32), 0, NBLK - 1).astype(jnp.int32)
        blocks = block_pool[slots]
        cache_keys = kv_cache[0][blocks].reshape(span_len, KVH, HD)
        cache_values = kv_cache[1][blocks].reshape(span_len, KVH, HD)
        key_valid = jnp.arange(span_len, dtype=jnp.int32) < cached_len[request]
        causal = jnp.arange(NEW, dtype=jnp.int32)[None, :] <= jnp.arange(NEW, dtype=jnp.int32)[:, None]

        def one_head(head):
            query_head = lax.dynamic_index_in_dim(queries, head, 2, keepdims=False).astype(jnp.float32)
            key_old = lax.dynamic_index_in_dim(cache_keys, head, 1, keepdims=False).astype(jnp.float32)
            value_old = lax.dynamic_index_in_dim(cache_values, head, 1, keepdims=False).astype(jnp.float32)
            key_new = lax.dynamic_index_in_dim(new_keys, head, 1, keepdims=False).astype(jnp.float32)
            value_new = lax.dynamic_index_in_dim(new_values, head, 1, keepdims=False).astype(jnp.float32)
            old_scores = jnp.einsum('nkc,tc->nkt', query_head, key_old) * scale_q
            old_scores = jnp.where(key_valid[None, None, :], old_scores, NEG_FILL)
            new_scores = jnp.einsum('nkc,tc->nkt', query_head, key_new) * scale_q
            new_scores = jnp.where(causal[:, None, :], new_scores, NEG_FILL)
            peak = jnp.maximum(lax.optimization_barrier(jnp.max(old_scores, axis=-1)), lax.optimization_barrier(jnp.max(new_scores, axis=-1)))
            old_weights = jnp.exp(old_scores - peak[..., None])
            new_weights = jnp.exp(new_scores - peak[..., None])
            total = lax.optimization_barrier(jnp.sum(old_weights, axis=-1)) + lax.optimization_barrier(jnp.sum(new_weights, axis=-1))
            old_probs = lax.optimization_barrier(old_weights.astype(jnp.bfloat16)).astype(jnp.float32)
            new_probs = lax.optimization_barrier(new_weights.astype(jnp.bfloat16)).astype(jnp.float32)
            mixed = jnp.einsum('nkt,tc->nkc', old_probs, value_old) + jnp.einsum('nkt,tc->nkc', new_probs, value_new)
            return (mixed / total[..., None]).astype(jnp.bfloat16)
        per_head = lax.map(one_head, jnp.arange(KVH, dtype=jnp.int32))
        attended = jnp.transpose(per_head, (1, 2, 0, 3)).reshape(NEW, 2, KVH * HD)
        output = jnp.zeros((NEW, D), jnp.float32)
        for expert in range(ATT_EXP):
            weight_expert = lax.optimization_barrier(jnp.sum(onehot[:, :, expert] * gates, axis=1))
            picked = jnp.where(chosen[:, 0:1] == expert, attended[:, 0], jnp.where(chosen[:, 1:2] == expert, attended[:, 1], jnp.zeros_like(attended[:, 0])))
            output = output + weight_expert[:, None] * jnp.dot(picked, o_weight[expert], preferred_element_type=jnp.float32)
        return output.astype(jnp.bfloat16)
    return lax.map(one_request, jnp.arange(REQS, dtype=jnp.int32))
```

```python
import jax
import jax.numpy as jnp
from jax import lax
from jax.sharding import PartitionSpec as P

HD = 128


NEG_FILL = -1e30


def rotate(values, positions):
    half_dim = values.shape[-1] // 2
    inverse = 10000.0 ** (-2.0 * jnp.arange(half_dim, dtype=jnp.float32) / values.shape[-1])
    angles = positions.astype(jnp.float32)[:, None] * inverse[None, :]
    target = (values.shape[0],) + (1,) * (values.ndim - 2) + (half_dim,)
    cosine = jnp.cos(angles).reshape(target)
    sine_part = jnp.sin(angles).reshape(target)
    leading_part = values[..., :half_dim]
    trailing_part = values[..., half_dim:]
    return jnp.concatenate(
        [
            leading_part * cosine - trailing_part * sine_part,
            trailing_part * cosine + leading_part * sine_part,
        ],
        axis=-1,
    )


def normalize(rows, norm_gain):
    wide_rows = rows.astype(jnp.float32)
    scaled = wide_rows * lax.rsqrt(jnp.mean(wide_rows * wide_rows, axis=-1, keepdims=True) + 1e-05)
    return (scaled * norm_gain.astype(jnp.float32)).astype(jnp.bfloat16)


def route(normed, router_weight, chosen):
    logits = jnp.dot(normed, router_weight, preferred_element_type=jnp.float32)
    experts_all = router_weight.shape[1]
    onehot = (chosen[:, :, None] == jnp.arange(experts_all, dtype=jnp.int32)[None, None, :]).astype(
        jnp.float32
    )
    picked = jnp.sum(onehot * logits[:, None, :], axis=-1)
    return (onehot, jax.nn.softmax(picked, axis=-1))


def split_bf16(x):
    hi = lax.reduce_precision(x, exponent_bits=8, mantissa_bits=7)
    lo = lax.reduce_precision(x - hi, exponent_bits=8, mantissa_bits=7)
    return hi, lo


def per_device(
    hidden,
    norm_gain,
    router_weight,
    att_experts,
    q_weight,
    kv_weight,
    o_weight,
    kv_cache,
    cached_blocks,
    tail_trim,
    block_pool,
):
    head_count = lax.axis_size("heads")
    seq_rank = lax.axis_index("seq")
    block_size = kv_cache.shape[2]
    local_blocks = kv_cache.shape[1]
    local_heads = q_weight.shape[2] // HD
    scale_q = HD ** (-0.5)
    normed = normalize(hidden[0], norm_gain)
    gathered = lax.all_gather(normed, "heads", axis=0, tiled=True)
    new_count = gathered.shape[0]
    chosen = att_experts[0]
    cached_len = cached_blocks * block_size - tail_trim
    positions = cached_len[seq_rank] + jnp.arange(new_count, dtype=jnp.int32)
    onehot, gates = route(gathered, router_weight, chosen)
    every_q = jnp.einsum("nd,edc->nec", gathered, q_weight, preferred_element_type=jnp.float32)
    chosen_q = jnp.sum(onehot[:, :, :, None] * every_q[:, None, :, :], axis=2).reshape(
        new_count, 2, local_heads, HD
    )
    queries = rotate(chosen_q, positions).astype(jnp.bfloat16)
    fresh = jnp.einsum("nd,sdc->snc", gathered, kv_weight, preferred_element_type=jnp.float32)
    new_keys = rotate(fresh[0].reshape(new_count, local_heads, HD), positions).astype(jnp.bfloat16)
    new_values = fresh[1].reshape(new_count, local_heads, HD).astype(jnp.bfloat16)
    all_queries = lax.all_gather(queries[None], "seq", axis=0, tiled=True)
    request_count = all_queries.shape[0]
    pool_size = block_pool.shape[0]

    global_ids = seq_rank * local_blocks + jnp.arange(local_blocks, dtype=jnp.int32)
    matches = block_pool[None, :] == global_ids[:, None]
    slot_of = jnp.sum(
        jnp.where(matches, jnp.arange(pool_size, dtype=jnp.int32)[None, :], 0), axis=1
    )
    starts = jnp.cumsum(cached_blocks) - cached_blocks
    owner = jnp.sum((starts[None, :] <= slot_of[:, None]).astype(jnp.int32), axis=1) - 1
    ordinal = slot_of - starts[owner]
    owns = owner[None, :] == jnp.arange(request_count, dtype=jnp.int32)[:, None]

    block_queries = jnp.take(all_queries, owner, axis=0)
    keys_here = kv_cache[0].reshape(local_blocks, block_size, local_heads, HD)
    values_here = kv_cache[1].reshape(local_blocks, block_size, local_heads, HD)
    scores = (
        jnp.einsum(
            "bnkhc,bthc->bhnkt", block_queries, keys_here, preferred_element_type=jnp.float32
        )
        * scale_q
    )
    key_pos = ordinal[:, None] * block_size + jnp.arange(block_size, dtype=jnp.int32)[None, :]
    key_ok = key_pos < cached_len[owner][:, None]
    scores = jnp.where(key_ok[:, None, None, None, :], scores, NEG_FILL)
    block_best = jnp.max(scores, axis=-1)
    request_best = jnp.max(
        jnp.where(owns[:, :, None, None, None], block_best[None], NEG_FILL), axis=1
    )
    best_hi, best_lo = split_bf16(request_best)
    request_ref = best_hi + best_lo
    weights = jnp.exp(scores - jnp.take(request_ref, owner, axis=0)[..., None])
    block_totals = jnp.sum(weights, axis=-1)
    block_accum = jnp.einsum(
        "bhnkt,bthc->bhnkc",
        weights.astype(jnp.bfloat16),
        values_here,
        preferred_element_type=jnp.float32,
    )
    owns_f = owns.astype(jnp.float32)
    accum = jnp.einsum("rb,bhnkc->rhnkc", owns_f, block_accum, precision=lax.Precision.HIGHEST)
    totals = jnp.einsum("rb,bhnk->rhnk", owns_f, block_totals, precision=lax.Precision.HIGHEST)
    totals_hi, totals_lo = split_bf16(totals)
    stats = jnp.stack([best_hi, best_lo, totals_hi, totals_lo], axis=1).astype(jnp.bfloat16)
    stat_rows = stats.size // (request_count * HD)
    payload = jnp.concatenate(
        [
            accum.astype(jnp.bfloat16).reshape(request_count, -1, HD),
            stats.reshape(request_count, stat_rows, HD),
        ],
        axis=1,
    )
    received = lax.all_to_all(payload, "seq", 0, 0, tiled=True)
    acc_rows = local_heads * new_count * 2
    sources = received.shape[0]
    part_accum = received[:, :acc_rows].astype(jnp.float32).reshape(
        sources, local_heads, new_count, 2, HD
    )
    part_stats = received[:, acc_rows:].astype(jnp.float32).reshape(
        sources, 4, local_heads, new_count, 2
    )
    part_best = part_stats[:, 0] + part_stats[:, 1]
    part_totals = part_stats[:, 2] + part_stats[:, 3]
    cache_best = jnp.max(part_best, axis=0)
    factor = jnp.exp(part_best - cache_best[None])
    cache_total = jnp.sum(part_totals * factor, axis=0)
    cache_accum = jnp.sum(part_accum * factor[..., None], axis=0)

    self_scores = (
        jnp.einsum("nkhc,thc->hnkt", queries, new_keys, preferred_element_type=jnp.float32)
        * scale_q
    )
    causal = (
        jnp.arange(new_count, dtype=jnp.int32)[None, :]
        <= jnp.arange(new_count, dtype=jnp.int32)[:, None]
    )
    self_scores = jnp.where(causal[None, :, None, :], self_scores, NEG_FILL)
    self_best = jnp.max(self_scores, axis=-1)
    self_weights = jnp.exp(self_scores - self_best[..., None])
    self_total = jnp.sum(self_weights, axis=-1)
    self_accum = jnp.einsum(
        "hnkt,thc->hnkc",
        self_weights.astype(jnp.bfloat16),
        new_values,
        preferred_element_type=jnp.float32,
    )
    peak = jnp.maximum(cache_best, self_best)
    cache_share = jnp.exp(cache_best - peak)
    self_share = jnp.exp(self_best - peak)
    numerator = cache_accum * cache_share[..., None] + self_accum * self_share[..., None]
    denominator = cache_total * cache_share + self_total * self_share
    attended = (
        jnp.transpose((numerator / denominator[..., None]).astype(jnp.bfloat16), (1, 2, 0, 3))
        .reshape(new_count, 2, local_heads * HD)
    )
    rows_each = new_count // head_count
    output = jnp.zeros((rows_each * lax.axis_size("heads"), o_weight.shape[2]), jnp.float32)
    for expert in range(o_weight.shape[0]):
        weight_expert = jnp.sum(onehot[:, :, expert] * gates, axis=1)
        picked = jnp.where(
            chosen[:, 0:1] == expert,
            attended[:, 0],
            jnp.where(chosen[:, 1:2] == expert, attended[:, 1], jnp.zeros_like(attended[:, 0])),
        )
        output = output + weight_expert[:, None] * jnp.dot(
            picked, o_weight[expert], preferred_element_type=jnp.float32
        )
    summed = lax.psum_scatter(
        output.astype(jnp.bfloat16), "heads", scatter_dimension=0, tiled=True
    ).astype(jnp.float32)
    return summed[None].astype(jnp.bfloat16)


def solution(mesh):
    return jax.shard_map(
        per_device,
        mesh=mesh,
        in_specs=(
            P("seq", "heads", None),
            P(),
            P(),
            P("seq", None, None),
            P(None, None, "heads"),
            P(None, None, "heads"),
            P(None, "heads", None),
            P(None, "seq", None, "heads"),
            P(),
            P(),
            P(),
        ),
        out_specs=P("seq", "heads", None),
        check_vma=False,
    )
```

```python
import jax
import jax.numpy as jnp
from jax import lax
from jax.sharding import PartitionSpec as P

HD = 128


NEG_FILL = -1e30


def rotate(values, positions):
    half_dim = values.shape[-1] // 2
    inverse = 10000.0 ** (-2.0 * jnp.arange(half_dim, dtype=jnp.float32) / values.shape[-1])
    angles = positions.astype(jnp.float32)[:, None] * inverse[None, :]
    target = (values.shape[0],) + (1,) * (values.ndim - 2) + (half_dim,)
    cosine = jnp.cos(angles).reshape(target)
    sine_part = jnp.sin(angles).reshape(target)
    leading_part = values[..., :half_dim]
    trailing_part = values[..., half_dim:]
    return jnp.concatenate(
        [
            leading_part * cosine - trailing_part * sine_part,
            trailing_part * cosine + leading_part * sine_part,
        ],
        axis=-1,
    )


def normalize(rows, norm_gain):
    wide_rows = rows.astype(jnp.float32)
    scaled = wide_rows * lax.rsqrt(jnp.mean(wide_rows * wide_rows, axis=-1, keepdims=True) + 1e-05)
    return (scaled * norm_gain.astype(jnp.float32)).astype(jnp.bfloat16)


def route(normed, router_weight, chosen):
    logits = jnp.dot(normed, router_weight, preferred_element_type=jnp.float32)
    experts_all = router_weight.shape[1]
    onehot = (chosen[:, :, None] == jnp.arange(experts_all, dtype=jnp.int32)[None, None, :]).astype(
        jnp.float32
    )
    picked = jnp.sum(onehot * logits[:, None, :], axis=-1)
    return (onehot, jax.nn.softmax(picked, axis=-1))


def split_bf16(x):
    hi = lax.reduce_precision(x, exponent_bits=8, mantissa_bits=7)
    lo = lax.reduce_precision(x - hi, exponent_bits=8, mantissa_bits=7)
    return hi, lo


def per_device(
    hidden,
    norm_gain,
    router_weight,
    att_experts,
    q_weight,
    kv_weight,
    o_weight,
    kv_cache,
    cached_blocks,
    tail_trim,
    block_pool,
):
    head_count = lax.axis_size("heads")
    seq_rank = lax.axis_index("seq")
    block_size = kv_cache.shape[2]
    local_blocks = kv_cache.shape[1]
    local_heads = q_weight.shape[2] // HD
    scale_q = HD ** (-0.5)
    normed = normalize(hidden[0], norm_gain)
    gathered = lax.all_gather(normed, "heads", axis=0, tiled=True)
    new_count = gathered.shape[0]
    chosen = att_experts[0]
    cached_len = cached_blocks * block_size - tail_trim
    positions = cached_len[seq_rank] + jnp.arange(new_count, dtype=jnp.int32)
    onehot, gates = route(gathered, router_weight, chosen)
    every_q = jnp.einsum("nd,edc->nec", gathered, q_weight, preferred_element_type=jnp.float32)
    chosen_q = jnp.sum(onehot[:, :, :, None] * every_q[:, None, :, :], axis=2).reshape(
        new_count, 2, local_heads, HD
    )
    queries = rotate(chosen_q, positions).astype(jnp.bfloat16)
    fresh = jnp.einsum("nd,sdc->snc", gathered, kv_weight, preferred_element_type=jnp.float32)
    new_keys = rotate(fresh[0].reshape(new_count, local_heads, HD), positions).astype(jnp.bfloat16)
    new_values = fresh[1].reshape(new_count, local_heads, HD).astype(jnp.bfloat16)
    pool_size = block_pool.shape[0]

    global_ids = seq_rank * local_blocks + jnp.arange(local_blocks, dtype=jnp.int32)
    matches = block_pool[None, :] == global_ids[:, None]
    slot_of = jnp.sum(
        jnp.where(matches, jnp.arange(pool_size, dtype=jnp.int32)[None, :], 0), axis=1
    )
    starts = jnp.cumsum(cached_blocks) - cached_blocks
    owner = jnp.sum((starts[None, :] <= slot_of[:, None]).astype(jnp.int32), axis=1) - 1
    ordinal = slot_of - starts[owner]
    request_count = cached_blocks.shape[0]
    owns = owner[None, :] == jnp.arange(request_count, dtype=jnp.int32)[:, None]
    owns_f = owns.astype(jnp.float32)
    key_pos = ordinal[:, None] * block_size + jnp.arange(block_size, dtype=jnp.int32)[None, :]
    key_ok = key_pos < cached_len[owner][:, None]
    keys_here = kv_cache[0].reshape(local_blocks, block_size, local_heads, HD)
    values_here = kv_cache[1].reshape(local_blocks, block_size, local_heads, HD)
    slots = queries.shape[1]

    gathered_q = [
        lax.all_gather(queries[None, :, slot], "seq", axis=0, tiled=True) for slot in range(slots)
    ]

    self_scores = (
        jnp.einsum("nkhc,thc->khnt", queries, new_keys, preferred_element_type=jnp.float32)
        * scale_q
    )
    causal = (
        jnp.arange(new_count, dtype=jnp.int32)[None, :]
        <= jnp.arange(new_count, dtype=jnp.int32)[:, None]
    )
    self_scores = jnp.where(causal[None, None], self_scores, NEG_FILL)
    self_best = jnp.max(self_scores, axis=-1)
    self_weights = jnp.exp(self_scores - self_best[..., None])
    self_total = jnp.sum(self_weights, axis=-1)
    self_accum = jnp.einsum(
        "khnt,thc->khnc",
        self_weights.astype(jnp.bfloat16),
        new_values,
        preferred_element_type=jnp.float32,
    )
    self_parts = (self_best, self_total, self_accum)

    def cache_payload(slot_queries):
        block_queries = jnp.take(slot_queries, owner, axis=0)
        scores = (
            jnp.einsum(
                "bnhc,bthc->bhnt", block_queries, keys_here, preferred_element_type=jnp.float32
            )
            * scale_q
        )
        scores = jnp.where(key_ok[:, None, None, :], scores, NEG_FILL)
        block_best = jnp.max(scores, axis=-1)
        request_best = jnp.max(
            jnp.where(owns[:, :, None, None], block_best[None], NEG_FILL), axis=1
        )
        best_hi, best_lo = split_bf16(request_best)
        request_ref = best_hi + best_lo
        weights = jnp.exp(scores - jnp.take(request_ref, owner, axis=0)[..., None])
        block_totals = jnp.sum(weights, axis=-1)
        block_accum = jnp.einsum(
            "bhnt,bthc->bhnc",
            weights.astype(jnp.bfloat16),
            values_here,
            preferred_element_type=jnp.float32,
        )
        accum = jnp.einsum("rb,bhnc->rhnc", owns_f, block_accum, precision=lax.Precision.HIGHEST)
        totals = jnp.einsum("rb,bhn->rhn", owns_f, block_totals, precision=lax.Precision.HIGHEST)
        totals_hi, totals_lo = split_bf16(totals)
        stats = jnp.stack([best_hi, best_lo, totals_hi, totals_lo], axis=1).astype(jnp.bfloat16)
        stat_rows = stats.size // (request_count * HD)
        return jnp.concatenate(
            [
                accum.astype(jnp.bfloat16).reshape(request_count, -1, HD),
                stats.reshape(request_count, stat_rows, HD),
            ],
            axis=1,
        )

    def finish(received, slot):
        acc_rows = local_heads * new_count
        sources = received.shape[0]
        part_accum = received[:, :acc_rows].astype(jnp.float32).reshape(
            sources, local_heads, new_count, HD
        )
        part_stats = received[:, acc_rows:].astype(jnp.float32).reshape(
            sources, 4, local_heads, new_count
        )
        part_best = part_stats[:, 0] + part_stats[:, 1]
        part_totals = part_stats[:, 2] + part_stats[:, 3]
        cache_best = jnp.max(part_best, axis=0)
        factor = jnp.exp(part_best - cache_best[None])
        cache_total = jnp.sum(part_totals * factor, axis=0)
        cache_accum = jnp.sum(part_accum * factor[..., None], axis=0)
        slot_best, slot_total, slot_accum = (part[slot] for part in self_parts)
        peak = jnp.maximum(cache_best, slot_best)
        cache_share = jnp.exp(cache_best - peak)
        self_share = jnp.exp(slot_best - peak)
        numerator = cache_accum * cache_share[..., None] + slot_accum * self_share[..., None]
        denominator = cache_total * cache_share + slot_total * self_share
        attended = jnp.transpose(
            (numerator / denominator[..., None]).astype(jnp.bfloat16), (1, 0, 2)
        ).reshape(new_count, local_heads * HD)
        experts_all = o_weight.shape[0]
        picked = jnp.where(
            chosen[:, slot, None, None] == jnp.arange(experts_all, dtype=jnp.int32)[None, :, None],
            attended[:, None, :],
            jnp.zeros_like(attended[:, None, :]),
        )
        projected = jnp.einsum(
            "nec,ecd->nd", picked, o_weight, preferred_element_type=jnp.float32
        )
        return gates[:, slot, None] * projected

    first_queries, self_parts = lax.optimization_barrier((gathered_q[0], self_parts))
    payloads = [cache_payload(first_queries)]
    second_queries, first_payload = lax.optimization_barrier((gathered_q[1], payloads[0]))
    first_received = lax.all_to_all(first_payload, "seq", 0, 0, tiled=True)
    second_payload = cache_payload(second_queries)
    second_received = lax.all_to_all(second_payload, "seq", 0, 0, tiled=True)
    first_out = finish(first_received, 0)
    second_received, first_out = lax.optimization_barrier((second_received, first_out))
    output = first_out + finish(second_received, 1)
    summed = lax.psum_scatter(
        output.astype(jnp.bfloat16), "heads", scatter_dimension=0, tiled=True
    ).astype(jnp.float32)
    return summed[None].astype(jnp.bfloat16)


def solution(mesh):
    return jax.shard_map(
        per_device,
        mesh=mesh,
        in_specs=(
            P("seq", "heads", None),
            P(),
            P(),
            P("seq", None, None),
            P(None, None, "heads"),
            P(None, None, "heads"),
            P(None, "heads", None),
            P(None, "seq", None, "heads"),
            P(),
            P(),
            P(),
        ),
        out_specs=P("seq", "heads", None),
        check_vma=False,
    )
```

```python
import functools

import numpy as np
import jax
import jax.numpy as jnp
from jax import lax
from jax.sharding import PartitionSpec as P

HD = 128


NEG_FILL = -1e30


def rotate(values, positions):
    half_dim = values.shape[-1] // 2
    inverse = 10000.0 ** (-2.0 * jnp.arange(half_dim, dtype=jnp.float32) / values.shape[-1])
    angles = positions.astype(jnp.float32)[:, None] * inverse[None, :]
    target = (values.shape[0],) + (1,) * (values.ndim - 2) + (half_dim,)
    cosine = jnp.cos(angles).reshape(target)
    sine_part = jnp.sin(angles).reshape(target)
    leading_part = values[..., :half_dim]
    trailing_part = values[..., half_dim:]
    return jnp.concatenate(
        [
            leading_part * cosine - trailing_part * sine_part,
            trailing_part * cosine + leading_part * sine_part,
        ],
        axis=-1,
    )


def normalize(rows, norm_gain):
    wide_rows = rows.astype(jnp.float32)
    scaled = wide_rows * lax.rsqrt(jnp.mean(wide_rows * wide_rows, axis=-1, keepdims=True) + 1e-05)
    return (scaled * norm_gain.astype(jnp.float32)).astype(jnp.bfloat16)


def route(normed, router_weight, chosen):
    logits = jnp.dot(normed, router_weight, preferred_element_type=jnp.float32)
    experts_all = router_weight.shape[1]
    onehot = (chosen[:, :, None] == jnp.arange(experts_all, dtype=jnp.int32)[None, None, :]).astype(
        jnp.float32
    )
    picked = jnp.sum(onehot * logits[:, None, :], axis=-1)
    return (onehot, jax.nn.softmax(picked, axis=-1))


def seq_cycle(mesh):
    size = mesh.shape["seq"]
    plain = list(range(size))
    try:
        devices = np.moveaxis(np.asarray(mesh.devices), mesh.axis_names.index("seq"), -1)
        line = devices.reshape(-1, size)[0]
        coords = np.array([list(d.coords) for d in line])
    except Exception:
        return plain
    varying = [k for k in range(coords.shape[1]) if len(set(coords[:, k])) > 1]
    if len(varying) == 1:
        order = sorted(plain, key=lambda j: coords[j, varying[0]])
        return order[0::2] + order[1::2][::-1]
    if len(varying) != 2:
        return plain
    dim_a, dim_b = varying
    values_a = sorted(set(coords[:, dim_a]))
    values_b = sorted(set(coords[:, dim_b]))
    if len(values_a) % 2:
        dim_a, dim_b, values_a, values_b = dim_b, dim_a, values_b, values_a
    if len(values_a) % 2 or len(values_a) * len(values_b) != size:
        return plain
    at = {(coords[j, dim_a], coords[j, dim_b]): j for j in plain}
    cycle = [at[(a, values_b[0])] for a in values_a]
    for row, a in enumerate(reversed(values_a)):
        columns = values_b[1:] if row % 2 == 0 else values_b[1:][::-1]
        cycle += [at[(a, b)] for b in columns]
    if sorted(cycle) != plain:
        return plain
    return cycle


def shift_all_gather(piece, axis_name):
    size = lax.axis_size(axis_name)
    rank = lax.axis_index(axis_name)
    by_offset = [piece] + [
        lax.ppermute(piece, axis_name, [(i, (i + s) % size) for i in range(size)])
        for s in range(1, size)
    ]
    by_offset = jnp.stack(by_offset[:1] + by_offset[1:][::-1], axis=0)
    return jnp.take(by_offset, (jnp.arange(size, dtype=jnp.int32) - rank) % size, axis=0)


def shift_reduce_scatter(rows, axis_name):
    size = lax.axis_size(axis_name)
    rank = lax.axis_index(axis_name)
    share = rows.shape[0] // size
    total = lax.dynamic_slice_in_dim(rows, rank * share, share, 0).astype(jnp.float32)
    for s in range(1, size):
        piece = lax.dynamic_slice_in_dim(rows, ((rank + s) % size) * share, share, 0)
        moved = lax.ppermute(piece, axis_name, [(i, (i + s) % size) for i in range(size)])
        total = total + moved.astype(jnp.float32)
    return total


def ring_all_gather(piece, axis_name, cycle):
    size = len(cycle)
    forward = [(cycle[i], cycle[(i + 1) % size]) for i in range(size)]
    backward = [(cycle[(i + 1) % size], cycle[i]) for i in range(size)]
    ahead = size // 2
    behind = size - 1 - ahead
    from_behind, from_ahead = [], []
    moving = piece
    for _ in range(ahead):
        moving = lax.ppermute(moving, axis_name, forward)
        from_behind.append(moving)
    moving = piece
    for _ in range(behind):
        moving = lax.ppermute(moving, axis_name, backward)
        from_ahead.append(moving)
    return jnp.stack([piece] + from_ahead + from_behind[::-1], axis=0)


def merge_parts(first, second):
    best_a, total_a, accum_a = first
    best_b, total_b, accum_b = second
    best = jnp.maximum(best_a, best_b)
    share_a = jnp.exp(best_a - best)
    share_b = jnp.exp(best_b - best)
    return (
        best,
        total_a * share_a + total_b * share_b,
        accum_a * share_a[..., None] + accum_b * share_b[..., None],
    )


def ring_reduce_scatter(parts, axis_name, cycle, position, forward_dir):
    size = len(cycle)
    cycle_arr = jnp.asarray(cycle, dtype=jnp.int32)
    step_sign = 1 if forward_dir else -1
    if forward_dir:
        pairs = [(cycle[i], cycle[(i + 1) % size]) for i in range(size)]
    else:
        pairs = [(cycle[(i + 1) % size], cycle[i]) for i in range(size)]

    def own(step):
        request = cycle_arr[(position - step_sign * (1 + step)) % size]
        return tuple(lax.dynamic_index_in_dim(p, request, 0, keepdims=False) for p in parts)

    carried = own(0)
    for step in range(1, size):
        arrived = lax.ppermute(carried, axis_name, pairs)
        carried = merge_parts(arrived, own(step))
    return carried


def per_device(
    cycle,
    hidden,
    norm_gain,
    router_weight,
    att_experts,
    q_weight,
    kv_weight,
    o_weight,
    kv_cache,
    cached_blocks,
    tail_trim,
    block_pool,
):
    head_count = lax.axis_size("heads")
    seq_rank = lax.axis_index("seq")
    block_size = kv_cache.shape[2]
    local_blocks = kv_cache.shape[1]
    local_heads = q_weight.shape[2] // HD
    scale_q = HD ** (-0.5)
    normed = normalize(hidden[0], norm_gain)
    gathered = shift_all_gather(normed, "heads").reshape(-1, normed.shape[1])
    new_count = gathered.shape[0]
    chosen = att_experts[0]
    cached_len = cached_blocks * block_size - tail_trim
    positions = cached_len[seq_rank] + jnp.arange(new_count, dtype=jnp.int32)
    onehot, gates = route(gathered, router_weight, chosen)
    every_q = jnp.einsum("nd,edc->nec", gathered, q_weight, preferred_element_type=jnp.float32)
    chosen_q = jnp.sum(onehot[:, :, :, None] * every_q[:, None, :, :], axis=2).reshape(
        new_count, 2, local_heads, HD
    )
    queries = rotate(chosen_q, positions).astype(jnp.bfloat16)
    fresh = jnp.einsum("nd,sdc->snc", gathered, kv_weight, preferred_element_type=jnp.float32)
    new_keys = rotate(fresh[0].reshape(new_count, local_heads, HD), positions).astype(jnp.bfloat16)
    new_values = fresh[1].reshape(new_count, local_heads, HD).astype(jnp.bfloat16)
    ring_queries = ring_all_gather(queries, "seq", cycle)
    request_count = ring_queries.shape[0]
    ring_size = len(cycle)
    position_of = np.argsort(np.asarray(cycle))
    position = jnp.asarray(position_of, dtype=jnp.int32)[seq_rank]
    pool_size = block_pool.shape[0]

    global_ids = seq_rank * local_blocks + jnp.arange(local_blocks, dtype=jnp.int32)
    matches = block_pool[None, :] == global_ids[:, None]
    slot_of = jnp.sum(
        jnp.where(matches, jnp.arange(pool_size, dtype=jnp.int32)[None, :], 0), axis=1
    )
    starts = jnp.cumsum(cached_blocks) - cached_blocks
    owner = jnp.sum((starts[None, :] <= slot_of[:, None]).astype(jnp.int32), axis=1) - 1
    ordinal = slot_of - starts[owner]
    owns = owner[None, :] == jnp.arange(request_count, dtype=jnp.int32)[:, None]

    owner_offset = (jnp.asarray(position_of, dtype=jnp.int32)[owner] - position) % ring_size
    block_queries = jnp.take(ring_queries, owner_offset, axis=0)
    keys_here = kv_cache[0].reshape(local_blocks, block_size, local_heads, HD)
    values_here = kv_cache[1].reshape(local_blocks, block_size, local_heads, HD)
    scores = (
        jnp.einsum(
            "bnkhc,bthc->bhnkt", block_queries, keys_here, preferred_element_type=jnp.float32
        )
        * scale_q
    )
    key_pos = ordinal[:, None] * block_size + jnp.arange(block_size, dtype=jnp.int32)[None, :]
    key_ok = key_pos < cached_len[owner][:, None]
    scores = jnp.where(key_ok[:, None, None, None, :], scores, NEG_FILL)
    block_best = jnp.max(scores, axis=-1)
    request_best = jnp.max(
        jnp.where(owns[:, :, None, None, None], block_best[None], NEG_FILL), axis=1
    )
    weights = jnp.exp(scores - jnp.take(request_best, owner, axis=0)[..., None])
    block_totals = jnp.sum(weights, axis=-1)
    block_accum = jnp.einsum(
        "bhnkt,bthc->bhnkc",
        weights.astype(jnp.bfloat16),
        values_here,
        preferred_element_type=jnp.float32,
    )
    owns_f = owns.astype(jnp.float32)
    accum = jnp.einsum("rb,bhnkc->rhnkc", owns_f, block_accum, precision=lax.Precision.HIGHEST)
    totals = jnp.einsum("rb,bhnk->rhnk", owns_f, block_totals, precision=lax.Precision.HIGHEST)
    half = new_count // 2
    halves = []
    for index, forward_dir in enumerate((True, False)):
        cut = slice(index * half, (index + 1) * half)
        parts = (request_best[:, :, cut], totals[:, :, cut], accum[:, :, cut])
        halves.append(ring_reduce_scatter(parts, "seq", cycle, position, forward_dir))
    cache_best, cache_total, cache_accum = (
        jnp.concatenate([first, second], axis=1) for first, second in zip(*halves)
    )

    self_scores = (
        jnp.einsum("nkhc,thc->hnkt", queries, new_keys, preferred_element_type=jnp.float32)
        * scale_q
    )
    causal = (
        jnp.arange(new_count, dtype=jnp.int32)[None, :]
        <= jnp.arange(new_count, dtype=jnp.int32)[:, None]
    )
    self_scores = jnp.where(causal[None, :, None, :], self_scores, NEG_FILL)
    self_best = jnp.max(self_scores, axis=-1)
    self_weights = jnp.exp(self_scores - self_best[..., None])
    self_total = jnp.sum(self_weights, axis=-1)
    self_accum = jnp.einsum(
        "hnkt,thc->hnkc",
        self_weights.astype(jnp.bfloat16),
        new_values,
        preferred_element_type=jnp.float32,
    )
    peak = jnp.maximum(cache_best, self_best)
    cache_share = jnp.exp(cache_best - peak)
    self_share = jnp.exp(self_best - peak)
    numerator = cache_accum * cache_share[..., None] + self_accum * self_share[..., None]
    denominator = cache_total * cache_share + self_total * self_share
    attended = (
        jnp.transpose((numerator / denominator[..., None]).astype(jnp.bfloat16), (1, 2, 0, 3))
        .reshape(new_count, 2, local_heads * HD)
    )
    rows_each = new_count // head_count
    output = jnp.zeros((rows_each * lax.axis_size("heads"), o_weight.shape[2]), jnp.float32)
    for expert in range(o_weight.shape[0]):
        weight_expert = jnp.sum(onehot[:, :, expert] * gates, axis=1)
        picked = jnp.where(
            chosen[:, 0:1] == expert,
            attended[:, 0],
            jnp.where(chosen[:, 1:2] == expert, attended[:, 1], jnp.zeros_like(attended[:, 0])),
        )
        output = output + weight_expert[:, None] * jnp.dot(
            picked, o_weight[expert], preferred_element_type=jnp.float32
        )
    summed = shift_reduce_scatter(output.astype(jnp.bfloat16), "heads")
    return summed[None].astype(jnp.bfloat16)


def solution(mesh):
    return jax.shard_map(
        functools.partial(per_device, tuple(seq_cycle(mesh))),
        mesh=mesh,
        in_specs=(
            P("seq", "heads", None),
            P(),
            P(),
            P("seq", None, None),
            P(None, None, "heads"),
            P(None, None, "heads"),
            P(None, "heads", None),
            P(None, "seq", None, "heads"),
            P(),
            P(),
            P(),
        ),
        out_specs=P("seq", "heads", None),
        check_vma=False,
    )
```

```python
import functools

import numpy as np
import jax
import jax.numpy as jnp
from jax import lax
from jax.sharding import PartitionSpec as P

HD = 128


NEG_FILL = -1e30


def rotate(values, positions):
    half_dim = values.shape[-1] // 2
    inverse = 10000.0 ** (-2.0 * jnp.arange(half_dim, dtype=jnp.float32) / values.shape[-1])
    angles = positions.astype(jnp.float32)[:, None] * inverse[None, :]
    target = (values.shape[0],) + (1,) * (values.ndim - 2) + (half_dim,)
    cosine = jnp.cos(angles).reshape(target)
    sine_part = jnp.sin(angles).reshape(target)
    leading_part = values[..., :half_dim]
    trailing_part = values[..., half_dim:]
    return jnp.concatenate(
        [
            leading_part * cosine - trailing_part * sine_part,
            trailing_part * cosine + leading_part * sine_part,
        ],
        axis=-1,
    )


def normalize(rows, norm_gain):
    wide_rows = rows.astype(jnp.float32)
    scaled = wide_rows * lax.rsqrt(jnp.mean(wide_rows * wide_rows, axis=-1, keepdims=True) + 1e-05)
    return (scaled * norm_gain.astype(jnp.float32)).astype(jnp.bfloat16)


def route(normed, router_weight, chosen):
    logits = jnp.dot(normed, router_weight, preferred_element_type=jnp.float32)
    experts_all = router_weight.shape[1]
    onehot = (chosen[:, :, None] == jnp.arange(experts_all, dtype=jnp.int32)[None, None, :]).astype(
        jnp.float32
    )
    picked = jnp.sum(onehot * logits[:, None, :], axis=-1)
    return (onehot, jax.nn.softmax(picked, axis=-1))


def split_bf16(x):
    hi = lax.reduce_precision(x, exponent_bits=8, mantissa_bits=7)
    lo = lax.reduce_precision(x - hi, exponent_bits=8, mantissa_bits=7)
    return hi, lo


def seq_cycle(mesh):
    size = mesh.shape["seq"]
    plain = list(range(size))
    try:
        devices = np.moveaxis(np.asarray(mesh.devices), mesh.axis_names.index("seq"), -1)
        line = devices.reshape(-1, size)[0]
        coords = np.array([list(d.coords) for d in line])
    except Exception:
        return plain
    varying = [k for k in range(coords.shape[1]) if len(set(coords[:, k])) > 1]
    if len(varying) == 1:
        order = sorted(plain, key=lambda j: coords[j, varying[0]])
        return order[0::2] + order[1::2][::-1]
    if len(varying) != 2:
        return plain
    dim_a, dim_b = varying
    values_a = sorted(set(coords[:, dim_a]))
    values_b = sorted(set(coords[:, dim_b]))
    if len(values_a) % 2:
        dim_a, dim_b, values_a, values_b = dim_b, dim_a, values_b, values_a
    if len(values_a) % 2 or len(values_a) * len(values_b) != size:
        return plain
    at = {(coords[j, dim_a], coords[j, dim_b]): j for j in plain}
    cycle = [at[(a, values_b[0])] for a in values_a]
    for row, a in enumerate(reversed(values_a)):
        columns = values_b[1:] if row % 2 == 0 else values_b[1:][::-1]
        cycle += [at[(a, b)] for b in columns]
    if sorted(cycle) != plain:
        return plain
    return cycle


def shift_all_gather(piece, axis_name):
    size = lax.axis_size(axis_name)
    rank = lax.axis_index(axis_name)
    by_offset = [piece] + [
        lax.ppermute(piece, axis_name, [(i, (i + s) % size) for i in range(size)])
        for s in range(1, size)
    ]
    by_offset = jnp.stack(by_offset[:1] + by_offset[1:][::-1], axis=0)
    return jnp.take(by_offset, (jnp.arange(size, dtype=jnp.int32) - rank) % size, axis=0)


def shift_reduce_scatter(rows, axis_name):
    size = lax.axis_size(axis_name)
    rank = lax.axis_index(axis_name)
    share = rows.shape[0] // size
    total = lax.dynamic_slice_in_dim(rows, rank * share, share, 0).astype(jnp.float32)
    for s in range(1, size):
        piece = lax.dynamic_slice_in_dim(rows, ((rank + s) % size) * share, share, 0)
        moved = lax.ppermute(piece, axis_name, [(i, (i + s) % size) for i in range(size)])
        total = total + moved.astype(jnp.float32)
    return total


def ring_all_gather(piece, axis_name, cycle):
    size = len(cycle)
    forward = [(cycle[i], cycle[(i + 1) % size]) for i in range(size)]
    backward = [(cycle[(i + 1) % size], cycle[i]) for i in range(size)]
    ahead = size // 2
    behind = size - 1 - ahead
    from_behind, from_ahead = [], []
    moving = piece
    for _ in range(ahead):
        moving = lax.ppermute(moving, axis_name, forward)
        from_behind.append(moving)
    moving = piece
    for _ in range(behind):
        moving = lax.ppermute(moving, axis_name, backward)
        from_ahead.append(moving)
    return jnp.stack([piece] + from_ahead + from_behind[::-1], axis=0)


def per_device(
    cycle,
    hidden,
    norm_gain,
    router_weight,
    att_experts,
    q_weight,
    kv_weight,
    o_weight,
    kv_cache,
    cached_blocks,
    tail_trim,
    block_pool,
):
    head_count = lax.axis_size("heads")
    seq_rank = lax.axis_index("seq")
    block_size = kv_cache.shape[2]
    local_blocks = kv_cache.shape[1]
    local_heads = q_weight.shape[2] // HD
    scale_q = HD ** (-0.5)
    normed = normalize(hidden[0], norm_gain)
    gathered = lax.all_gather(normed, "heads", axis=0, tiled=True)
    new_count = gathered.shape[0]
    chosen = att_experts[0]
    cached_len = cached_blocks * block_size - tail_trim
    positions = cached_len[seq_rank] + jnp.arange(new_count, dtype=jnp.int32)
    onehot, gates = route(gathered, router_weight, chosen)
    every_q = jnp.einsum("nd,edc->nec", gathered, q_weight, preferred_element_type=jnp.float32)
    chosen_q = jnp.sum(onehot[:, :, :, None] * every_q[:, None, :, :], axis=2).reshape(
        new_count, 2, local_heads, HD
    )
    queries = rotate(chosen_q, positions).astype(jnp.bfloat16)
    fresh = jnp.einsum("nd,sdc->snc", gathered, kv_weight, preferred_element_type=jnp.float32)
    new_keys = rotate(fresh[0].reshape(new_count, local_heads, HD), positions).astype(jnp.bfloat16)
    new_values = fresh[1].reshape(new_count, local_heads, HD).astype(jnp.bfloat16)
    ring_queries = ring_all_gather(queries, "seq", cycle)
    request_count = ring_queries.shape[0]
    ring_size = len(cycle)
    position_of = np.argsort(np.asarray(cycle))
    position = jnp.asarray(position_of, dtype=jnp.int32)[seq_rank]
    pool_size = block_pool.shape[0]

    global_ids = seq_rank * local_blocks + jnp.arange(local_blocks, dtype=jnp.int32)
    matches = block_pool[None, :] == global_ids[:, None]
    slot_of = jnp.sum(
        jnp.where(matches, jnp.arange(pool_size, dtype=jnp.int32)[None, :], 0), axis=1
    )
    starts = jnp.cumsum(cached_blocks) - cached_blocks
    owner = jnp.sum((starts[None, :] <= slot_of[:, None]).astype(jnp.int32), axis=1) - 1
    ordinal = slot_of - starts[owner]
    owns = owner[None, :] == jnp.arange(request_count, dtype=jnp.int32)[:, None]

    self_scores = (
        jnp.einsum("nkhc,thc->hnkt", queries, new_keys, preferred_element_type=jnp.float32)
        * scale_q
    )
    causal = (
        jnp.arange(new_count, dtype=jnp.int32)[None, :]
        <= jnp.arange(new_count, dtype=jnp.int32)[:, None]
    )
    self_scores = jnp.where(causal[None, :, None, :], self_scores, NEG_FILL)
    self_best = jnp.max(self_scores, axis=-1)
    self_weights = jnp.exp(self_scores - self_best[..., None])
    self_total = jnp.sum(self_weights, axis=-1)
    self_accum = jnp.einsum(
        "hnkt,thc->hnkc",
        self_weights.astype(jnp.bfloat16),
        new_values,
        preferred_element_type=jnp.float32,
    )
    ring_queries, self_best, self_total, self_accum = lax.optimization_barrier(
        (ring_queries, self_best, self_total, self_accum)
    )
    owner_offset = (jnp.asarray(position_of, dtype=jnp.int32)[owner] - position) % ring_size
    block_queries = jnp.take(ring_queries, owner_offset, axis=0)
    keys_here = kv_cache[0].reshape(local_blocks, block_size, local_heads, HD)
    values_here = kv_cache[1].reshape(local_blocks, block_size, local_heads, HD)
    scores = (
        jnp.einsum(
            "bnkhc,bthc->bhnkt", block_queries, keys_here, preferred_element_type=jnp.float32
        )
        * scale_q
    )
    key_pos = ordinal[:, None] * block_size + jnp.arange(block_size, dtype=jnp.int32)[None, :]
    key_ok = key_pos < cached_len[owner][:, None]
    scores = jnp.where(key_ok[:, None, None, None, :], scores, NEG_FILL)
    block_best = jnp.max(scores, axis=-1)
    request_best = jnp.max(
        jnp.where(owns[:, :, None, None, None], block_best[None], NEG_FILL), axis=1
    )
    best_hi, best_lo = split_bf16(request_best)
    request_ref = best_hi + best_lo
    weights = jnp.exp(scores - jnp.take(request_ref, owner, axis=0)[..., None])
    block_totals = jnp.sum(weights, axis=-1)
    block_accum = jnp.einsum(
        "bhnkt,bthc->bhnkc",
        weights.astype(jnp.bfloat16),
        values_here,
        preferred_element_type=jnp.float32,
    )
    owns_f = owns.astype(jnp.float32)
    accum = jnp.einsum("rb,bhnkc->rhnkc", owns_f, block_accum, precision=lax.Precision.HIGHEST)
    totals = jnp.einsum("rb,bhnk->rhnk", owns_f, block_totals, precision=lax.Precision.HIGHEST)
    totals_hi, totals_lo = split_bf16(totals)
    stats = jnp.stack([best_hi, best_lo, totals_hi, totals_lo], axis=1).astype(jnp.bfloat16)
    stat_rows = stats.size // (request_count * HD)
    payload = jnp.concatenate(
        [
            accum.astype(jnp.bfloat16).reshape(request_count, -1, HD),
            stats.reshape(request_count, stat_rows, HD),
        ],
        axis=1,
    )
    received = lax.all_to_all(payload, "seq", 0, 0, tiled=True)
    acc_rows = local_heads * new_count * 2
    sources = received.shape[0]
    part_accum = received[:, :acc_rows].astype(jnp.float32).reshape(
        sources, local_heads, new_count, 2, HD
    )
    part_stats = received[:, acc_rows:].astype(jnp.float32).reshape(
        sources, 4, local_heads, new_count, 2
    )
    part_best = part_stats[:, 0] + part_stats[:, 1]
    part_totals = part_stats[:, 2] + part_stats[:, 3]
    cache_best = jnp.max(part_best, axis=0)
    factor = jnp.exp(part_best - cache_best[None])
    cache_total = jnp.sum(part_totals * factor, axis=0)
    cache_accum = jnp.sum(part_accum * factor[..., None], axis=0)

    peak = jnp.maximum(cache_best, self_best)
    cache_share = jnp.exp(cache_best - peak)
    self_share = jnp.exp(self_best - peak)
    numerator = cache_accum * cache_share[..., None] + self_accum * self_share[..., None]
    denominator = cache_total * cache_share + self_total * self_share
    attended = (
        jnp.transpose((numerator / denominator[..., None]).astype(jnp.bfloat16), (1, 2, 0, 3))
        .reshape(new_count, 2, local_heads * HD)
    )
    rows_each = new_count // head_count
    output = jnp.zeros((rows_each * lax.axis_size("heads"), o_weight.shape[2]), jnp.float32)
    for expert in range(o_weight.shape[0]):
        weight_expert = jnp.sum(onehot[:, :, expert] * gates, axis=1)
        picked = jnp.where(
            chosen[:, 0:1] == expert,
            attended[:, 0],
            jnp.where(chosen[:, 1:2] == expert, attended[:, 1], jnp.zeros_like(attended[:, 0])),
        )
        output = output + weight_expert[:, None] * jnp.dot(
            picked, o_weight[expert], preferred_element_type=jnp.float32
        )
    summed = shift_reduce_scatter(output.astype(jnp.bfloat16), "heads")
    return summed[None].astype(jnp.bfloat16)


def solution(mesh):
    return jax.shard_map(
        functools.partial(per_device, tuple(seq_cycle(mesh))),
        mesh=mesh,
        in_specs=(
            P("seq", "heads", None),
            P(),
            P(),
            P("seq", None, None),
            P(None, None, "heads"),
            P(None, None, "heads"),
            P(None, "heads", None),
            P(None, "seq", None, "heads"),
            P(),
            P(),
            P(),
        ),
        out_specs=P("seq", "heads", None),
        check_vma=False,
    )
```

```python
import functools

import numpy as np
import jax
import jax.numpy as jnp
from jax import lax
from jax.sharding import PartitionSpec as P

HD = 128


NEG_FILL = -1e30


def rotate(values, positions):
    half_dim = values.shape[-1] // 2
    inverse = 10000.0 ** (-2.0 * jnp.arange(half_dim, dtype=jnp.float32) / values.shape[-1])
    angles = positions.astype(jnp.float32)[:, None] * inverse[None, :]
    target = (values.shape[0],) + (1,) * (values.ndim - 2) + (half_dim,)
    cosine = jnp.cos(angles).reshape(target)
    sine_part = jnp.sin(angles).reshape(target)
    leading_part = values[..., :half_dim]
    trailing_part = values[..., half_dim:]
    return jnp.concatenate(
        [
            leading_part * cosine - trailing_part * sine_part,
            trailing_part * cosine + leading_part * sine_part,
        ],
        axis=-1,
    )


def normalize(rows, norm_gain):
    wide_rows = rows.astype(jnp.float32)
    scaled = wide_rows * lax.rsqrt(jnp.mean(wide_rows * wide_rows, axis=-1, keepdims=True) + 1e-05)
    return (scaled * norm_gain.astype(jnp.float32)).astype(jnp.bfloat16)


def route(normed, router_weight, chosen):
    logits = jnp.dot(normed, router_weight, preferred_element_type=jnp.float32)
    experts_all = router_weight.shape[1]
    onehot = (chosen[:, :, None] == jnp.arange(experts_all, dtype=jnp.int32)[None, None, :]).astype(
        jnp.float32
    )
    picked = jnp.sum(onehot * logits[:, None, :], axis=-1)
    return (onehot, jax.nn.softmax(picked, axis=-1))


def split_bf16(x):
    hi = lax.reduce_precision(x, exponent_bits=8, mantissa_bits=7)
    lo = lax.reduce_precision(x - hi, exponent_bits=8, mantissa_bits=7)
    return hi, lo


def seq_cycle(mesh):
    size = mesh.shape["seq"]
    plain = list(range(size))
    try:
        devices = np.moveaxis(np.asarray(mesh.devices), mesh.axis_names.index("seq"), -1)
        line = devices.reshape(-1, size)[0]
        coords = np.array([list(d.coords) for d in line])
    except Exception:
        return plain
    varying = [k for k in range(coords.shape[1]) if len(set(coords[:, k])) > 1]
    if len(varying) == 1:
        order = sorted(plain, key=lambda j: coords[j, varying[0]])
        return order[0::2] + order[1::2][::-1]
    if len(varying) != 2:
        return plain
    dim_a, dim_b = varying
    values_a = sorted(set(coords[:, dim_a]))
    values_b = sorted(set(coords[:, dim_b]))
    if len(values_a) % 2:
        dim_a, dim_b, values_a, values_b = dim_b, dim_a, values_b, values_a
    if len(values_a) % 2 or len(values_a) * len(values_b) != size:
        return plain
    at = {(coords[j, dim_a], coords[j, dim_b]): j for j in plain}
    cycle = [at[(a, values_b[0])] for a in values_a]
    for row, a in enumerate(reversed(values_a)):
        columns = values_b[1:] if row % 2 == 0 else values_b[1:][::-1]
        cycle += [at[(a, b)] for b in columns]
    if sorted(cycle) != plain:
        return plain
    return cycle


def shift_all_gather(piece, axis_name):
    size = lax.axis_size(axis_name)
    rank = lax.axis_index(axis_name)
    by_offset = [piece] + [
        lax.ppermute(piece, axis_name, [(i, (i + s) % size) for i in range(size)])
        for s in range(1, size)
    ]
    by_offset = jnp.stack(by_offset[:1] + by_offset[1:][::-1], axis=0)
    return jnp.take(by_offset, (jnp.arange(size, dtype=jnp.int32) - rank) % size, axis=0)


def shift_reduce_scatter(rows, axis_name):
    size = lax.axis_size(axis_name)
    rank = lax.axis_index(axis_name)
    share = rows.shape[0] // size
    total = lax.dynamic_slice_in_dim(rows, rank * share, share, 0).astype(jnp.float32)
    for s in range(1, size):
        piece = lax.dynamic_slice_in_dim(rows, ((rank + s) % size) * share, share, 0)
        moved = lax.ppermute(piece, axis_name, [(i, (i + s) % size) for i in range(size)])
        total = total + moved.astype(jnp.float32)
    return total


def ring_all_gather(piece, axis_name, cycle):
    size = len(cycle)
    forward = [(cycle[i], cycle[(i + 1) % size]) for i in range(size)]
    backward = [(cycle[(i + 1) % size], cycle[i]) for i in range(size)]
    ahead = size // 2
    behind = size - 1 - ahead
    from_behind, from_ahead = [], []
    moving = piece
    for _ in range(ahead):
        moving = lax.ppermute(moving, axis_name, forward)
        from_behind.append(moving)
    moving = piece
    for _ in range(behind):
        moving = lax.ppermute(moving, axis_name, backward)
        from_ahead.append(moving)
    return jnp.stack([piece] + from_ahead + from_behind[::-1], axis=0)


def per_device(
    cycle,
    hidden,
    norm_gain,
    router_weight,
    att_experts,
    q_weight,
    kv_weight,
    o_weight,
    kv_cache,
    cached_blocks,
    tail_trim,
    block_pool,
):
    head_count = lax.axis_size("heads")
    seq_rank = lax.axis_index("seq")
    block_size = kv_cache.shape[2]
    local_blocks = kv_cache.shape[1]
    local_heads = q_weight.shape[2] // HD
    scale_q = HD ** (-0.5)
    normed = normalize(hidden[0], norm_gain)
    gathered = shift_all_gather(normed, "heads").reshape(-1, normed.shape[1])
    new_count = gathered.shape[0]
    chosen = att_experts[0]
    cached_len = cached_blocks * block_size - tail_trim
    positions = cached_len[seq_rank] + jnp.arange(new_count, dtype=jnp.int32)
    onehot, gates = route(gathered, router_weight, chosen)
    every_q = jnp.einsum("nd,edc->nec", gathered, q_weight, preferred_element_type=jnp.float32)
    chosen_q = jnp.sum(onehot[:, :, :, None] * every_q[:, None, :, :], axis=2).reshape(
        new_count, 2, local_heads, HD
    )
    queries = rotate(chosen_q, positions).astype(jnp.bfloat16)
    fresh = jnp.einsum("nd,sdc->snc", gathered, kv_weight, preferred_element_type=jnp.float32)
    new_keys = rotate(fresh[0].reshape(new_count, local_heads, HD), positions).astype(jnp.bfloat16)
    new_values = fresh[1].reshape(new_count, local_heads, HD).astype(jnp.bfloat16)
    ring_queries = ring_all_gather(queries, "seq", cycle)
    request_count = ring_queries.shape[0]
    ring_size = len(cycle)
    position_of = np.argsort(np.asarray(cycle))
    position = jnp.asarray(position_of, dtype=jnp.int32)[seq_rank]
    pool_size = block_pool.shape[0]

    global_ids = seq_rank * local_blocks + jnp.arange(local_blocks, dtype=jnp.int32)
    matches = block_pool[None, :] == global_ids[:, None]
    slot_of = jnp.sum(
        jnp.where(matches, jnp.arange(pool_size, dtype=jnp.int32)[None, :], 0), axis=1
    )
    starts = jnp.cumsum(cached_blocks) - cached_blocks
    owner = jnp.sum((starts[None, :] <= slot_of[:, None]).astype(jnp.int32), axis=1) - 1
    ordinal = slot_of - starts[owner]
    owns = owner[None, :] == jnp.arange(request_count, dtype=jnp.int32)[:, None]

    self_scores = (
        jnp.einsum("nkhc,thc->hnkt", queries, new_keys, preferred_element_type=jnp.float32)
        * scale_q
    )
    causal = (
        jnp.arange(new_count, dtype=jnp.int32)[None, :]
        <= jnp.arange(new_count, dtype=jnp.int32)[:, None]
    )
    self_scores = jnp.where(causal[None, :, None, :], self_scores, NEG_FILL)
    self_best = jnp.max(self_scores, axis=-1)
    self_weights = jnp.exp(self_scores - self_best[..., None])
    self_total = jnp.sum(self_weights, axis=-1)
    self_accum = jnp.einsum(
        "hnkt,thc->hnkc",
        self_weights.astype(jnp.bfloat16),
        new_values,
        preferred_element_type=jnp.float32,
    )
    ring_queries, self_best, self_total, self_accum = lax.optimization_barrier(
        (ring_queries, self_best, self_total, self_accum)
    )
    owner_offset = (jnp.asarray(position_of, dtype=jnp.int32)[owner] - position) % ring_size
    block_queries = jnp.take(ring_queries, owner_offset, axis=0)
    keys_here = kv_cache[0].reshape(local_blocks, block_size, local_heads, HD)
    values_here = kv_cache[1].reshape(local_blocks, block_size, local_heads, HD)
    scores = (
        jnp.einsum(
            "bnkhc,bthc->bhnkt", block_queries, keys_here, preferred_element_type=jnp.float32
        )
        * scale_q
    )
    key_pos = ordinal[:, None] * block_size + jnp.arange(block_size, dtype=jnp.int32)[None, :]
    key_ok = key_pos < cached_len[owner][:, None]
    scores = jnp.where(key_ok[:, None, None, None, :], scores, NEG_FILL)
    block_best = jnp.max(scores, axis=-1)
    request_best = jnp.max(
        jnp.where(owns[:, :, None, None, None], block_best[None], NEG_FILL), axis=1
    )
    best_hi, best_lo = split_bf16(request_best)
    request_ref = best_hi + best_lo
    weights = jnp.exp(scores - jnp.take(request_ref, owner, axis=0)[..., None])
    block_totals = jnp.sum(weights, axis=-1)
    block_accum = jnp.einsum(
        "bhnkt,bthc->bhnkc",
        weights.astype(jnp.bfloat16),
        values_here,
        preferred_element_type=jnp.float32,
    )
    owns_f = owns.astype(jnp.float32)
    accum = jnp.einsum("rb,bhnkc->rhnkc", owns_f, block_accum, precision=lax.Precision.HIGHEST)
    totals = jnp.einsum("rb,bhnk->rhnk", owns_f, block_totals, precision=lax.Precision.HIGHEST)
    totals_hi, totals_lo = split_bf16(totals)
    stats = jnp.stack([best_hi, best_lo, totals_hi, totals_lo], axis=1).astype(jnp.bfloat16)
    stat_rows = stats.size // (request_count * HD)
    payload = jnp.concatenate(
        [
            accum.astype(jnp.bfloat16).reshape(request_count, -1, HD),
            stats.reshape(request_count, stat_rows, HD),
        ],
        axis=1,
    )
    received = lax.all_to_all(payload, "seq", 0, 0, tiled=True)
    acc_rows = local_heads * new_count * 2
    sources = received.shape[0]
    part_accum = received[:, :acc_rows].astype(jnp.float32).reshape(
        sources, local_heads, new_count, 2, HD
    )
    part_stats = received[:, acc_rows:].astype(jnp.float32).reshape(
        sources, 4, local_heads, new_count, 2
    )
    part_best = part_stats[:, 0] + part_stats[:, 1]
    part_totals = part_stats[:, 2] + part_stats[:, 3]
    cache_best = jnp.max(part_best, axis=0)
    factor = jnp.exp(part_best - cache_best[None])
    cache_total = jnp.sum(part_totals * factor, axis=0)
    cache_accum = jnp.sum(part_accum * factor[..., None], axis=0)

    peak = jnp.maximum(cache_best, self_best)
    cache_share = jnp.exp(cache_best - peak)
    self_share = jnp.exp(self_best - peak)
    numerator = cache_accum * cache_share[..., None] + self_accum * self_share[..., None]
    denominator = cache_total * cache_share + self_total * self_share
    attended = (
        jnp.transpose((numerator / denominator[..., None]).astype(jnp.bfloat16), (1, 2, 0, 3))
        .reshape(new_count, 2, local_heads * HD)
    )
    rows_each = new_count // head_count
    output = jnp.zeros((rows_each * lax.axis_size("heads"), o_weight.shape[2]), jnp.float32)
    for expert in range(o_weight.shape[0]):
        weight_expert = jnp.sum(onehot[:, :, expert] * gates, axis=1)
        picked = jnp.where(
            chosen[:, 0:1] == expert,
            attended[:, 0],
            jnp.where(chosen[:, 1:2] == expert, attended[:, 1], jnp.zeros_like(attended[:, 0])),
        )
        output = output + weight_expert[:, None] * jnp.dot(
            picked, o_weight[expert], preferred_element_type=jnp.float32
        )
    summed = shift_reduce_scatter(output.astype(jnp.bfloat16), "heads")
    return summed[None].astype(jnp.bfloat16)


def solution(mesh):
    return jax.shard_map(
        functools.partial(per_device, tuple(seq_cycle(mesh))),
        mesh=mesh,
        in_specs=(
            P("seq", "heads", None),
            P(),
            P(),
            P("seq", None, None),
            P(None, None, "heads"),
            P(None, None, "heads"),
            P(None, "heads", None),
            P(None, "seq", None, "heads"),
            P(),
            P(),
            P(),
        ),
        out_specs=P("seq", "heads", None),
        check_vma=False,
    )
```

```python
import functools

import numpy as np
import jax
import jax.numpy as jnp
from jax import lax
from jax.experimental import pallas as pl
from jax.experimental.pallas import tpu as pltpu
from jax.sharding import PartitionSpec as P

HD = 128


NEG_FILL = -1e30


def rotate(values, positions):
    half_dim = values.shape[-1] // 2
    inverse = 10000.0 ** (-2.0 * jnp.arange(half_dim, dtype=jnp.float32) / values.shape[-1])
    angles = positions.astype(jnp.float32)[:, None] * inverse[None, :]
    target = (values.shape[0],) + (1,) * (values.ndim - 2) + (half_dim,)
    cosine = jnp.cos(angles).reshape(target)
    sine_part = jnp.sin(angles).reshape(target)
    leading_part = values[..., :half_dim]
    trailing_part = values[..., half_dim:]
    return jnp.concatenate(
        [
            leading_part * cosine - trailing_part * sine_part,
            trailing_part * cosine + leading_part * sine_part,
        ],
        axis=-1,
    )


def normalize(rows, norm_gain):
    wide_rows = rows.astype(jnp.float32)
    scaled = wide_rows * lax.rsqrt(jnp.mean(wide_rows * wide_rows, axis=-1, keepdims=True) + 1e-05)
    return (scaled * norm_gain.astype(jnp.float32)).astype(jnp.bfloat16)


def route(normed, router_weight, chosen):
    logits = jnp.dot(normed, router_weight, preferred_element_type=jnp.float32)
    experts_all = router_weight.shape[1]
    onehot = (chosen[:, :, None] == jnp.arange(experts_all, dtype=jnp.int32)[None, None, :]).astype(
        jnp.float32
    )
    picked = jnp.sum(onehot * logits[:, None, :], axis=-1)
    return (onehot, jax.nn.softmax(picked, axis=-1))


def split_bf16(x):
    hi = lax.reduce_precision(x, exponent_bits=8, mantissa_bits=7)
    lo = lax.reduce_precision(x - hi, exponent_bits=8, mantissa_bits=7)
    return hi, lo


def seq_cycle(mesh):
    size = mesh.shape["seq"]
    plain = list(range(size))
    try:
        devices = np.moveaxis(np.asarray(mesh.devices), mesh.axis_names.index("seq"), -1)
        line = devices.reshape(-1, size)[0]
        coords = np.array([list(d.coords) for d in line])
    except Exception:
        return plain
    varying = [k for k in range(coords.shape[1]) if len(set(coords[:, k])) > 1]
    if len(varying) == 1:
        order = sorted(plain, key=lambda j: coords[j, varying[0]])
        return order[0::2] + order[1::2][::-1]
    if len(varying) != 2:
        return plain
    dim_a, dim_b = varying
    values_a = sorted(set(coords[:, dim_a]))
    values_b = sorted(set(coords[:, dim_b]))
    if len(values_a) % 2:
        dim_a, dim_b, values_a, values_b = dim_b, dim_a, values_b, values_a
    if len(values_a) % 2 or len(values_a) * len(values_b) != size:
        return plain
    at = {(coords[j, dim_a], coords[j, dim_b]): j for j in plain}
    cycle = [at[(a, values_b[0])] for a in values_a]
    for row, a in enumerate(reversed(values_a)):
        columns = values_b[1:] if row % 2 == 0 else values_b[1:][::-1]
        cycle += [at[(a, b)] for b in columns]
    if sorted(cycle) != plain:
        return plain
    return cycle


def shift_all_gather(piece, axis_name):
    size = lax.axis_size(axis_name)
    rank = lax.axis_index(axis_name)
    by_offset = [piece] + [
        lax.ppermute(piece, axis_name, [(i, (i + s) % size) for i in range(size)])
        for s in range(1, size)
    ]
    by_offset = jnp.stack(by_offset[:1] + by_offset[1:][::-1], axis=0)
    return jnp.take(by_offset, (jnp.arange(size, dtype=jnp.int32) - rank) % size, axis=0)


def shift_reduce_scatter(rows, axis_name):
    size = lax.axis_size(axis_name)
    rank = lax.axis_index(axis_name)
    share = rows.shape[0] // size
    total = lax.dynamic_slice_in_dim(rows, rank * share, share, 0).astype(jnp.float32)
    for s in range(1, size):
        piece = lax.dynamic_slice_in_dim(rows, ((rank + s) % size) * share, share, 0)
        moved = lax.ppermute(piece, axis_name, [(i, (i + s) % size) for i in range(size)])
        total = total + moved.astype(jnp.float32)
    return total


def ring_all_gather(piece, axis_name, cycle):
    size = len(cycle)
    forward = [(cycle[i], cycle[(i + 1) % size]) for i in range(size)]
    backward = [(cycle[(i + 1) % size], cycle[i]) for i in range(size)]
    ahead = size // 2
    behind = size - 1 - ahead
    from_behind, from_ahead = [], []
    moving = piece
    for _ in range(ahead):
        moving = lax.ppermute(moving, axis_name, forward)
        from_behind.append(moving)
    moving = piece
    for _ in range(behind):
        moving = lax.ppermute(moving, axis_name, backward)
        from_ahead.append(moving)
    return jnp.stack([piece] + from_ahead + from_behind[::-1], axis=0)


def block_attention(ring_queries, keys, values_t, owner_offset, valid):
    blocks, block_size, width = keys.shape
    query_rows = ring_queries.shape[1]
    heads = width // HD
    scale = HD ** (-0.5)

    def kernel(offset_ref, valid_ref, q_ref, k_ref, v_ref, best_ref, total_ref, accum_ref):
        b = pl.program_id(0)
        limit = valid_ref[b]
        row = lax.broadcasted_iota(jnp.int32, (block_size, query_rows), 0)
        for h in range(heads):
            q = q_ref[0, :, h * HD:(h + 1) * HD]
            k = k_ref[0, :, h * HD:(h + 1) * HD]
            scores = lax.dot_general(
                k, q, (((1,), (1,)), ((), ())), preferred_element_type=jnp.float32
            ) * scale
            scores = jnp.where(row < limit, scores, NEG_FILL)
            best = jnp.max(scores, axis=0, keepdims=True)
            weights = jnp.exp(scores - best)
            best_ref[0, h] = best
            total_ref[0, h] = jnp.sum(weights, axis=0, keepdims=True)
            v_t = v_ref[0, h * HD:(h + 1) * HD, :]
            accum_ref[0, h] = jnp.dot(
                v_t, weights.astype(jnp.bfloat16), preferred_element_type=jnp.float32
            )

    grid_spec = pltpu.PrefetchScalarGridSpec(
        num_scalar_prefetch=2,
        grid=(blocks,),
        in_specs=[
            pl.BlockSpec((1, query_rows, width), lambda b, off, val: (off[b], 0, 0)),
            pl.BlockSpec((1, block_size, width), lambda b, off, val: (b, 0, 0)),
            pl.BlockSpec((1, width, block_size), lambda b, off, val: (b, 0, 0)),
        ],
        out_specs=[
            pl.BlockSpec((1, heads, 1, query_rows), lambda b, off, val: (b, 0, 0, 0)),
            pl.BlockSpec((1, heads, 1, query_rows), lambda b, off, val: (b, 0, 0, 0)),
            pl.BlockSpec((1, heads, HD, query_rows), lambda b, off, val: (b, 0, 0, 0)),
        ],
    )
    return pl.pallas_call(
        kernel,
        grid_spec=grid_spec,
        out_shape=[
            jax.ShapeDtypeStruct((blocks, heads, 1, query_rows), jnp.float32),
            jax.ShapeDtypeStruct((blocks, heads, 1, query_rows), jnp.float32),
            jax.ShapeDtypeStruct((blocks, heads, HD, query_rows), jnp.float32),
        ],
    )(owner_offset, valid, ring_queries, keys, values_t)


def per_device(
    cycle,
    hidden,
    norm_gain,
    router_weight,
    att_experts,
    q_weight,
    kv_weight,
    o_weight,
    kv_cache,
    cached_blocks,
    tail_trim,
    block_pool,
):
    head_count = lax.axis_size("heads")
    seq_rank = lax.axis_index("seq")
    block_size = kv_cache.shape[2]
    local_blocks = kv_cache.shape[1]
    local_heads = q_weight.shape[2] // HD
    scale_q = HD ** (-0.5)
    normed = normalize(hidden[0], norm_gain)
    gathered = shift_all_gather(normed, "heads").reshape(-1, normed.shape[1])
    new_count = gathered.shape[0]
    chosen = att_experts[0]
    cached_len = cached_blocks * block_size - tail_trim
    positions = cached_len[seq_rank] + jnp.arange(new_count, dtype=jnp.int32)
    onehot, gates = route(gathered, router_weight, chosen)
    every_q = jnp.einsum("nd,edc->nec", gathered, q_weight, preferred_element_type=jnp.float32)
    chosen_q = jnp.sum(onehot[:, :, :, None] * every_q[:, None, :, :], axis=2).reshape(
        new_count, 2, local_heads, HD
    )
    queries = rotate(chosen_q, positions).astype(jnp.bfloat16)
    fresh = jnp.einsum("nd,sdc->snc", gathered, kv_weight, preferred_element_type=jnp.float32)
    new_keys = rotate(fresh[0].reshape(new_count, local_heads, HD), positions).astype(jnp.bfloat16)
    new_values = fresh[1].reshape(new_count, local_heads, HD).astype(jnp.bfloat16)
    ring_queries = ring_all_gather(queries, "seq", cycle)
    request_count = ring_queries.shape[0]
    ring_size = len(cycle)
    position_of = np.argsort(np.asarray(cycle))
    position = jnp.asarray(position_of, dtype=jnp.int32)[seq_rank]
    pool_size = block_pool.shape[0]

    global_ids = seq_rank * local_blocks + jnp.arange(local_blocks, dtype=jnp.int32)
    matches = block_pool[None, :] == global_ids[:, None]
    slot_of = jnp.sum(
        jnp.where(matches, jnp.arange(pool_size, dtype=jnp.int32)[None, :], 0), axis=1
    )
    starts = jnp.cumsum(cached_blocks) - cached_blocks
    owner = jnp.sum((starts[None, :] <= slot_of[:, None]).astype(jnp.int32), axis=1) - 1
    ordinal = slot_of - starts[owner]
    owns = owner[None, :] == jnp.arange(request_count, dtype=jnp.int32)[:, None]

    self_scores = (
        jnp.einsum("nkhc,thc->hnkt", queries, new_keys, preferred_element_type=jnp.float32)
        * scale_q
    )
    causal = (
        jnp.arange(new_count, dtype=jnp.int32)[None, :]
        <= jnp.arange(new_count, dtype=jnp.int32)[:, None]
    )
    self_scores = jnp.where(causal[None, :, None, :], self_scores, NEG_FILL)
    self_best = jnp.max(self_scores, axis=-1)
    self_weights = jnp.exp(self_scores - self_best[..., None])
    self_total = jnp.sum(self_weights, axis=-1)
    self_accum = jnp.einsum(
        "hnkt,thc->hnkc",
        self_weights.astype(jnp.bfloat16),
        new_values,
        preferred_element_type=jnp.float32,
    )
    ring_queries, self_best, self_total, self_accum = lax.optimization_barrier(
        (ring_queries, self_best, self_total, self_accum)
    )
    owner_offset = (jnp.asarray(position_of, dtype=jnp.int32)[owner] - position) % ring_size
    valid = jnp.clip(cached_len[owner] - ordinal * block_size, 0, block_size).astype(jnp.int32)
    query_rows = new_count * 2
    block_best, block_totals, block_accum = block_attention(
        ring_queries.reshape(request_count, query_rows, local_heads * HD),
        kv_cache[0],
        jnp.swapaxes(kv_cache[1], 1, 2),
        owner_offset,
        valid,
    )
    block_best = block_best[:, :, 0]
    block_totals = block_totals[:, :, 0]
    request_best = jnp.max(jnp.where(owns[:, :, None, None], block_best[None], NEG_FILL), axis=1)
    best_hi, best_lo = split_bf16(request_best)
    request_ref = best_hi + best_lo
    factor = jnp.exp(block_best - jnp.take(request_ref, owner, axis=0))
    owns_f = owns.astype(jnp.float32)
    totals = jnp.einsum(
        "rb,bhq->rhq", owns_f, block_totals * factor, precision=lax.Precision.HIGHEST
    )
    accum = jnp.einsum(
        "rb,bhcq->rhcq",
        owns_f,
        block_accum * factor[:, :, None, :],
        precision=lax.Precision.HIGHEST,
    )
    totals_hi, totals_lo = split_bf16(totals)
    stats = jnp.stack([best_hi, best_lo, totals_hi, totals_lo], axis=1).astype(jnp.bfloat16)
    payload = jnp.concatenate(
        [
            accum.astype(jnp.bfloat16).reshape(request_count, -1, query_rows),
            stats.reshape(request_count, -1, query_rows),
        ],
        axis=1,
    )
    received = lax.all_to_all(payload, "seq", 0, 0, tiled=True)
    acc_rows = local_heads * HD
    sources = received.shape[0]
    part_accum = received[:, :acc_rows].astype(jnp.float32).reshape(
        sources, local_heads, HD, query_rows
    )
    part_stats = received[:, acc_rows:].astype(jnp.float32).reshape(
        sources, 4, local_heads, query_rows
    )
    part_best = part_stats[:, 0] + part_stats[:, 1]
    part_totals = part_stats[:, 2] + part_stats[:, 3]
    cache_best = jnp.max(part_best, axis=0)
    share = jnp.exp(part_best - cache_best[None])
    cache_total = jnp.sum(part_totals * share, axis=0).reshape(local_heads, new_count, 2)
    cache_accum = jnp.transpose(
        jnp.sum(part_accum * share[:, :, None, :], axis=0), (0, 2, 1)
    ).reshape(local_heads, new_count, 2, HD)
    cache_best = cache_best.reshape(local_heads, new_count, 2)

    peak = jnp.maximum(cache_best, self_best)
    cache_share = jnp.exp(cache_best - peak)
    self_share = jnp.exp(self_best - peak)
    numerator = cache_accum * cache_share[..., None] + self_accum * self_share[..., None]
    denominator = cache_total * cache_share + self_total * self_share
    attended = (
        jnp.transpose((numerator / denominator[..., None]).astype(jnp.bfloat16), (1, 2, 0, 3))
        .reshape(new_count, 2, local_heads * HD)
    )
    rows_each = new_count // head_count
    output = jnp.zeros((rows_each * lax.axis_size("heads"), o_weight.shape[2]), jnp.float32)
    for expert in range(o_weight.shape[0]):
        weight_expert = jnp.sum(onehot[:, :, expert] * gates, axis=1)
        picked = jnp.where(
            chosen[:, 0:1] == expert,
            attended[:, 0],
            jnp.where(chosen[:, 1:2] == expert, attended[:, 1], jnp.zeros_like(attended[:, 0])),
        )
        output = output + weight_expert[:, None] * jnp.dot(
            picked, o_weight[expert], preferred_element_type=jnp.float32
        )
    summed = shift_reduce_scatter(output.astype(jnp.bfloat16), "heads")
    return summed[None].astype(jnp.bfloat16)


def solution(mesh):
    return jax.shard_map(
        functools.partial(per_device, tuple(seq_cycle(mesh))),
        mesh=mesh,
        in_specs=(
            P("seq", "heads", None),
            P(),
            P(),
            P("seq", None, None),
            P(None, None, "heads"),
            P(None, None, "heads"),
            P(None, "heads", None),
            P(None, "seq", None, "heads"),
            P(),
            P(),
            P(),
        ),
        out_specs=P("seq", "heads", None),
        check_vma=False,
    )
```

```python
import functools

import numpy as np
import jax
import jax.numpy as jnp
from jax import lax
from jax.experimental import pallas as pl
from jax.experimental.pallas import tpu as pltpu
from jax.sharding import PartitionSpec as P

HD = 128


NEG_FILL = -1e30


def rotate(values, positions):
    half_dim = values.shape[-1] // 2
    inverse = 10000.0 ** (-2.0 * jnp.arange(half_dim, dtype=jnp.float32) / values.shape[-1])
    angles = positions.astype(jnp.float32)[:, None] * inverse[None, :]
    target = (values.shape[0],) + (1,) * (values.ndim - 2) + (half_dim,)
    cosine = jnp.cos(angles).reshape(target)
    sine_part = jnp.sin(angles).reshape(target)
    leading_part = values[..., :half_dim]
    trailing_part = values[..., half_dim:]
    return jnp.concatenate(
        [
            leading_part * cosine - trailing_part * sine_part,
            trailing_part * cosine + leading_part * sine_part,
        ],
        axis=-1,
    )


def normalize(rows, norm_gain):
    wide_rows = rows.astype(jnp.float32)
    scaled = wide_rows * lax.rsqrt(jnp.mean(wide_rows * wide_rows, axis=-1, keepdims=True) + 1e-05)
    return (scaled * norm_gain.astype(jnp.float32)).astype(jnp.bfloat16)


def route(normed, router_weight, chosen):
    logits = jnp.dot(normed, router_weight, preferred_element_type=jnp.float32)
    experts_all = router_weight.shape[1]
    onehot = (chosen[:, :, None] == jnp.arange(experts_all, dtype=jnp.int32)[None, None, :]).astype(
        jnp.float32
    )
    picked = jnp.sum(onehot * logits[:, None, :], axis=-1)
    return (onehot, jax.nn.softmax(picked, axis=-1))


def split_bf16(x):
    hi = lax.reduce_precision(x, exponent_bits=8, mantissa_bits=7)
    lo = lax.reduce_precision(x - hi, exponent_bits=8, mantissa_bits=7)
    return hi, lo


def seq_cycle(mesh):
    size = mesh.shape["seq"]
    plain = list(range(size))
    try:
        devices = np.moveaxis(np.asarray(mesh.devices), mesh.axis_names.index("seq"), -1)
        line = devices.reshape(-1, size)[0]
        coords = np.array([list(d.coords) for d in line])
    except Exception:
        return plain
    varying = [k for k in range(coords.shape[1]) if len(set(coords[:, k])) > 1]
    if len(varying) == 1:
        order = sorted(plain, key=lambda j: coords[j, varying[0]])
        return order[0::2] + order[1::2][::-1]
    if len(varying) != 2:
        return plain
    dim_a, dim_b = varying
    values_a = sorted(set(coords[:, dim_a]))
    values_b = sorted(set(coords[:, dim_b]))
    if len(values_a) % 2:
        dim_a, dim_b, values_a, values_b = dim_b, dim_a, values_b, values_a
    if len(values_a) % 2 or len(values_a) * len(values_b) != size:
        return plain
    at = {(coords[j, dim_a], coords[j, dim_b]): j for j in plain}
    cycle = [at[(a, values_b[0])] for a in values_a]
    for row, a in enumerate(reversed(values_a)):
        columns = values_b[1:] if row % 2 == 0 else values_b[1:][::-1]
        cycle += [at[(a, b)] for b in columns]
    if sorted(cycle) != plain:
        return plain
    return cycle


def shift_all_gather(piece, axis_name):
    size = lax.axis_size(axis_name)
    rank = lax.axis_index(axis_name)
    by_offset = [piece] + [
        lax.ppermute(piece, axis_name, [(i, (i + s) % size) for i in range(size)])
        for s in range(1, size)
    ]
    by_offset = jnp.stack(by_offset[:1] + by_offset[1:][::-1], axis=0)
    return jnp.take(by_offset, (jnp.arange(size, dtype=jnp.int32) - rank) % size, axis=0)


def shift_reduce_scatter(rows, axis_name):
    size = lax.axis_size(axis_name)
    rank = lax.axis_index(axis_name)
    share = rows.shape[0] // size
    total = lax.dynamic_slice_in_dim(rows, rank * share, share, 0).astype(jnp.float32)
    for s in range(1, size):
        piece = lax.dynamic_slice_in_dim(rows, ((rank + s) % size) * share, share, 0)
        moved = lax.ppermute(piece, axis_name, [(i, (i + s) % size) for i in range(size)])
        total = total + moved.astype(jnp.float32)
    return total


def ring_all_gather(piece, axis_name, cycle):
    size = len(cycle)
    forward = [(cycle[i], cycle[(i + 1) % size]) for i in range(size)]
    backward = [(cycle[(i + 1) % size], cycle[i]) for i in range(size)]
    ahead = size // 2
    behind = size - 1 - ahead
    from_behind, from_ahead = [], []
    moving = piece
    for _ in range(ahead):
        moving = lax.ppermute(moving, axis_name, forward)
        from_behind.append(moving)
    moving = piece
    for _ in range(behind):
        moving = lax.ppermute(moving, axis_name, backward)
        from_ahead.append(moving)
    return jnp.stack([piece] + from_ahead + from_behind[::-1], axis=0)


def block_attention(ring_queries, keys, values_t, owner_offset, owner, valid, requests):
    blocks, block_size, width = keys.shape
    query_rows = ring_queries.shape[1]
    heads = width // HD
    scale = HD ** (-0.5)

    def kernel(offset_ref, owner_ref, valid_ref, q_ref, k_ref, v_ref, best_ref, total_ref, accum_ref):
        b = pl.program_id(0)

        @pl.when(b == 0)
        def _():
            best_ref[...] = jnp.full(best_ref.shape, NEG_FILL, jnp.float32)
            total_ref[...] = jnp.zeros(total_ref.shape, jnp.float32)
            accum_ref[...] = jnp.zeros(accum_ref.shape, jnp.float32)

        request = owner_ref[b]
        limit = valid_ref[b]
        row = lax.broadcasted_iota(jnp.int32, (block_size, query_rows), 0)
        for h in range(heads):
            q = q_ref[0, :, h * HD:(h + 1) * HD]
            k = k_ref[0, :, h * HD:(h + 1) * HD]
            scores = lax.dot_general(
                k, q, (((1,), (1,)), ((), ())), preferred_element_type=jnp.float32
            ) * scale
            scores = jnp.where(row < limit, scores, NEG_FILL)
            old_best = best_ref[request, h]
            new_best = jnp.maximum(old_best, jnp.max(scores, axis=0, keepdims=True))
            rescale = jnp.exp(old_best - new_best)
            weights = jnp.exp(scores - new_best)
            best_ref[request, h] = new_best
            total_ref[request, h] = total_ref[request, h] * rescale + jnp.sum(
                weights, axis=0, keepdims=True
            )
            v_t = v_ref[0, h * HD:(h + 1) * HD, :]
            accum_ref[request, h] = accum_ref[request, h] * rescale + jnp.dot(
                v_t, weights.astype(jnp.bfloat16), preferred_element_type=jnp.float32
            )

    grid_spec = pltpu.PrefetchScalarGridSpec(
        num_scalar_prefetch=3,
        grid=(blocks,),
        in_specs=[
            pl.BlockSpec((1, query_rows, width), lambda b, off, own, val: (off[b], 0, 0)),
            pl.BlockSpec((1, block_size, width), lambda b, off, own, val: (b, 0, 0)),
            pl.BlockSpec((1, width, block_size), lambda b, off, own, val: (b, 0, 0)),
        ],
        out_specs=[
            pl.BlockSpec((requests, heads, 1, query_rows), lambda b, off, own, val: (0, 0, 0, 0)),
            pl.BlockSpec((requests, heads, 1, query_rows), lambda b, off, own, val: (0, 0, 0, 0)),
            pl.BlockSpec((requests, heads, HD, query_rows), lambda b, off, own, val: (0, 0, 0, 0)),
        ],
    )
    resident = 2 * requests * heads * (HD + 16) * query_rows * 4
    return pl.pallas_call(
        kernel,
        grid_spec=grid_spec,
        out_shape=[
            jax.ShapeDtypeStruct((requests, heads, 1, query_rows), jnp.float32),
            jax.ShapeDtypeStruct((requests, heads, 1, query_rows), jnp.float32),
            jax.ShapeDtypeStruct((requests, heads, HD, query_rows), jnp.float32),
        ],
        compiler_params=pltpu.CompilerParams(
            dimension_semantics=("arbitrary",),
            vmem_limit_bytes=resident + 24 * 1024 * 1024,
        ),
    )(owner_offset, owner, valid, ring_queries, keys, values_t)


def per_device(
    cycle,
    hidden,
    norm_gain,
    router_weight,
    att_experts,
    q_weight,
    kv_weight,
    o_weight,
    kv_cache,
    cached_blocks,
    tail_trim,
    block_pool,
):
    head_count = lax.axis_size("heads")
    seq_rank = lax.axis_index("seq")
    block_size = kv_cache.shape[2]
    local_blocks = kv_cache.shape[1]
    local_heads = q_weight.shape[2] // HD
    scale_q = HD ** (-0.5)
    normed = normalize(hidden[0], norm_gain)
    gathered = shift_all_gather(normed, "heads").reshape(-1, normed.shape[1])
    new_count = gathered.shape[0]
    chosen = att_experts[0]
    cached_len = cached_blocks * block_size - tail_trim
    positions = cached_len[seq_rank] + jnp.arange(new_count, dtype=jnp.int32)
    onehot, gates = route(gathered, router_weight, chosen)
    every_q = jnp.einsum("nd,edc->nec", gathered, q_weight, preferred_element_type=jnp.float32)
    chosen_q = jnp.sum(onehot[:, :, :, None] * every_q[:, None, :, :], axis=2).reshape(
        new_count, 2, local_heads, HD
    )
    queries = rotate(chosen_q, positions).astype(jnp.bfloat16)
    fresh = jnp.einsum("nd,sdc->snc", gathered, kv_weight, preferred_element_type=jnp.float32)
    new_keys = rotate(fresh[0].reshape(new_count, local_heads, HD), positions).astype(jnp.bfloat16)
    new_values = fresh[1].reshape(new_count, local_heads, HD).astype(jnp.bfloat16)
    ring_queries = ring_all_gather(
        queries.reshape(new_count * 2, local_heads * HD), "seq", cycle
    )
    request_count = ring_queries.shape[0]
    ring_size = len(cycle)
    position_of = np.argsort(np.asarray(cycle))
    position = jnp.asarray(position_of, dtype=jnp.int32)[seq_rank]
    pool_size = block_pool.shape[0]

    global_ids = seq_rank * local_blocks + jnp.arange(local_blocks, dtype=jnp.int32)
    matches = block_pool[None, :] == global_ids[:, None]
    slot_of = jnp.sum(
        jnp.where(matches, jnp.arange(pool_size, dtype=jnp.int32)[None, :], 0), axis=1
    )
    starts = jnp.cumsum(cached_blocks) - cached_blocks
    owner = jnp.sum((starts[None, :] <= slot_of[:, None]).astype(jnp.int32), axis=1) - 1
    ordinal = slot_of - starts[owner]
    owns = owner[None, :] == jnp.arange(request_count, dtype=jnp.int32)[:, None]

    self_scores = (
        jnp.einsum("nkhc,thc->hnkt", queries, new_keys, preferred_element_type=jnp.float32)
        * scale_q
    )
    causal = (
        jnp.arange(new_count, dtype=jnp.int32)[None, :]
        <= jnp.arange(new_count, dtype=jnp.int32)[:, None]
    )
    self_scores = jnp.where(causal[None, :, None, :], self_scores, NEG_FILL)
    self_best = jnp.max(self_scores, axis=-1)
    self_weights = jnp.exp(self_scores - self_best[..., None])
    self_total = jnp.sum(self_weights, axis=-1)
    self_accum = jnp.einsum(
        "hnkt,thc->hnkc",
        self_weights.astype(jnp.bfloat16),
        new_values,
        preferred_element_type=jnp.float32,
    )
    ring_queries, self_best, self_total, self_accum = lax.optimization_barrier(
        (ring_queries, self_best, self_total, self_accum)
    )
    owner_offset = (jnp.asarray(position_of, dtype=jnp.int32)[owner] - position) % ring_size
    valid = jnp.clip(cached_len[owner] - ordinal * block_size, 0, block_size).astype(jnp.int32)
    query_rows = new_count * 2
    request_best, totals, accum = block_attention(
        ring_queries,
        kv_cache[0],
        jnp.swapaxes(kv_cache[1], 1, 2),
        owner_offset,
        owner,
        valid,
        request_count,
    )
    request_best = request_best[:, :, 0]
    best_hi, best_lo = split_bf16(request_best)
    request_ref = best_hi + best_lo
    present = request_best > 0.5 * NEG_FILL
    adjust = jnp.exp(jnp.where(present, request_best - request_ref, 0.0))
    totals = totals[:, :, 0] * adjust
    accum = accum * adjust[:, :, None, :]
    totals_hi, totals_lo = split_bf16(totals)
    stats = jnp.stack([best_hi, best_lo, totals_hi, totals_lo], axis=1).astype(jnp.bfloat16)
    payload = jnp.concatenate(
        [
            accum.astype(jnp.bfloat16).reshape(request_count, -1, query_rows),
            stats.reshape(request_count, -1, query_rows),
        ],
        axis=1,
    )
    received = lax.all_to_all(payload, "seq", 0, 0, tiled=True)
    acc_rows = local_heads * HD
    sources = received.shape[0]
    part_accum = received[:, :acc_rows].astype(jnp.float32).reshape(
        sources, local_heads, HD, query_rows
    )
    part_stats = received[:, acc_rows:].astype(jnp.float32).reshape(
        sources, 4, local_heads, query_rows
    )
    part_best = part_stats[:, 0] + part_stats[:, 1]
    part_totals = part_stats[:, 2] + part_stats[:, 3]
    cache_best = jnp.max(part_best, axis=0)
    share = jnp.exp(part_best - cache_best[None])
    cache_total = jnp.sum(part_totals * share, axis=0).reshape(local_heads, new_count, 2)
    cache_accum = jnp.transpose(
        jnp.sum(part_accum * share[:, :, None, :], axis=0), (0, 2, 1)
    ).reshape(local_heads, new_count, 2, HD)
    cache_best = cache_best.reshape(local_heads, new_count, 2)

    peak = jnp.maximum(cache_best, self_best)
    cache_share = jnp.exp(cache_best - peak)
    self_share = jnp.exp(self_best - peak)
    numerator = cache_accum * cache_share[..., None] + self_accum * self_share[..., None]
    denominator = cache_total * cache_share + self_total * self_share
    attended = (
        jnp.transpose((numerator / denominator[..., None]).astype(jnp.bfloat16), (1, 2, 0, 3))
        .reshape(new_count, 2, local_heads * HD)
    )
    rows_each = new_count // head_count
    output = jnp.zeros((rows_each * lax.axis_size("heads"), o_weight.shape[2]), jnp.float32)
    for expert in range(o_weight.shape[0]):
        weight_expert = jnp.sum(onehot[:, :, expert] * gates, axis=1)
        picked = jnp.where(
            chosen[:, 0:1] == expert,
            attended[:, 0],
            jnp.where(chosen[:, 1:2] == expert, attended[:, 1], jnp.zeros_like(attended[:, 0])),
        )
        output = output + weight_expert[:, None] * jnp.dot(
            picked, o_weight[expert], preferred_element_type=jnp.float32
        )
    summed = shift_reduce_scatter(output.astype(jnp.bfloat16), "heads")
    return summed[None].astype(jnp.bfloat16)


def solution(mesh):
    return jax.shard_map(
        functools.partial(per_device, tuple(seq_cycle(mesh))),
        mesh=mesh,
        in_specs=(
            P("seq", "heads", None),
            P(),
            P(),
            P("seq", None, None),
            P(None, None, "heads"),
            P(None, None, "heads"),
            P(None, "heads", None),
            P(None, "seq", None, "heads"),
            P(),
            P(),
            P(),
        ),
        out_specs=P("seq", "heads", None),
        check_vma=False,
    )
```

```python
import functools

import numpy as np
import jax
import jax.numpy as jnp
from jax import lax
from jax.experimental import pallas as pl
from jax.experimental.pallas import tpu as pltpu
from jax.sharding import PartitionSpec as P

HD = 128


NEG_FILL = -1e30


def rotate(values, positions):
    half_dim = values.shape[-1] // 2
    inverse = 10000.0 ** (-2.0 * jnp.arange(half_dim, dtype=jnp.float32) / values.shape[-1])
    angles = positions.astype(jnp.float32)[:, None] * inverse[None, :]
    target = (values.shape[0],) + (1,) * (values.ndim - 2) + (half_dim,)
    cosine = jnp.cos(angles).reshape(target)
    sine_part = jnp.sin(angles).reshape(target)
    leading_part = values[..., :half_dim]
    trailing_part = values[..., half_dim:]
    return jnp.concatenate(
        [
            leading_part * cosine - trailing_part * sine_part,
            trailing_part * cosine + leading_part * sine_part,
        ],
        axis=-1,
    )


def normalize(rows, norm_gain):
    wide_rows = rows.astype(jnp.float32)
    scaled = wide_rows * lax.rsqrt(jnp.mean(wide_rows * wide_rows, axis=-1, keepdims=True) + 1e-05)
    return (scaled * norm_gain.astype(jnp.float32)).astype(jnp.bfloat16)


def route(normed, router_weight, chosen):
    logits = jnp.dot(normed, router_weight, preferred_element_type=jnp.float32)
    experts_all = router_weight.shape[1]
    onehot = (chosen[:, :, None] == jnp.arange(experts_all, dtype=jnp.int32)[None, None, :]).astype(
        jnp.float32
    )
    picked = jnp.sum(onehot * logits[:, None, :], axis=-1)
    return (onehot, jax.nn.softmax(picked, axis=-1))


def split_bf16(x):
    hi = lax.reduce_precision(x, exponent_bits=8, mantissa_bits=7)
    lo = lax.reduce_precision(x - hi, exponent_bits=8, mantissa_bits=7)
    return hi, lo


def seq_cycle(mesh):
    size = mesh.shape["seq"]
    plain = list(range(size))
    try:
        devices = np.moveaxis(np.asarray(mesh.devices), mesh.axis_names.index("seq"), -1)
        line = devices.reshape(-1, size)[0]
        coords = np.array([list(d.coords) for d in line])
    except Exception:
        return plain
    varying = [k for k in range(coords.shape[1]) if len(set(coords[:, k])) > 1]
    if len(varying) == 1:
        order = sorted(plain, key=lambda j: coords[j, varying[0]])
        return order[0::2] + order[1::2][::-1]
    if len(varying) != 2:
        return plain
    dim_a, dim_b = varying
    values_a = sorted(set(coords[:, dim_a]))
    values_b = sorted(set(coords[:, dim_b]))
    if len(values_a) % 2:
        dim_a, dim_b, values_a, values_b = dim_b, dim_a, values_b, values_a
    if len(values_a) % 2 or len(values_a) * len(values_b) != size:
        return plain
    at = {(coords[j, dim_a], coords[j, dim_b]): j for j in plain}
    cycle = [at[(a, values_b[0])] for a in values_a]
    for row, a in enumerate(reversed(values_a)):
        columns = values_b[1:] if row % 2 == 0 else values_b[1:][::-1]
        cycle += [at[(a, b)] for b in columns]
    if sorted(cycle) != plain:
        return plain
    return cycle


def shift_all_gather(piece, axis_name):
    size = lax.axis_size(axis_name)
    rank = lax.axis_index(axis_name)
    by_offset = [piece] + [
        lax.ppermute(piece, axis_name, [(i, (i + s) % size) for i in range(size)])
        for s in range(1, size)
    ]
    return jnp.stack(by_offset[:1] + by_offset[1:][::-1], axis=0)


def shift_reduce_scatter(blocks, axis_name):
    size = lax.axis_size(axis_name)
    total = blocks[0].astype(jnp.float32)
    for s in range(1, size):
        moved = lax.ppermute(blocks[s], axis_name, [(i, (i + s) % size) for i in range(size)])
        total = total + moved.astype(jnp.float32)
    return total


def ring_all_gather(piece, axis_name, cycle):
    size = len(cycle)
    forward = [(cycle[i], cycle[(i + 1) % size]) for i in range(size)]
    backward = [(cycle[(i + 1) % size], cycle[i]) for i in range(size)]
    ahead = size // 2
    behind = size - 1 - ahead
    from_behind, from_ahead = [], []
    moving = piece
    for _ in range(ahead):
        moving = lax.ppermute(moving, axis_name, forward)
        from_behind.append(moving)
    moving = piece
    for _ in range(behind):
        moving = lax.ppermute(moving, axis_name, backward)
        from_ahead.append(moving)
    return jnp.stack([piece] + from_ahead + from_behind[::-1], axis=0)


def block_attention(ring_queries, keys, values_t, owner_offset, owner, valid, requests):
    blocks, block_size, width = keys.shape
    query_rows = ring_queries.shape[1]
    heads = width // HD
    scale = HD ** (-0.5)

    def kernel(offset_ref, owner_ref, valid_ref, q_ref, k_ref, v_ref, best_ref, total_ref, accum_ref):
        b = pl.program_id(0)

        @pl.when(b == 0)
        def _():
            best_ref[...] = jnp.full(best_ref.shape, NEG_FILL, jnp.float32)
            total_ref[...] = jnp.zeros(total_ref.shape, jnp.float32)
            accum_ref[...] = jnp.zeros(accum_ref.shape, jnp.float32)

        request = owner_ref[b]
        limit = valid_ref[b]
        row = lax.broadcasted_iota(jnp.int32, (block_size, query_rows), 0)
        for h in range(heads):
            q = q_ref[0, :, h * HD:(h + 1) * HD]
            k = k_ref[0, :, h * HD:(h + 1) * HD]
            scores = lax.dot_general(
                k, q, (((1,), (1,)), ((), ())), preferred_element_type=jnp.float32
            ) * scale
            scores = jnp.where(row < limit, scores, NEG_FILL)
            old_best = best_ref[request, h]
            new_best = jnp.maximum(old_best, jnp.max(scores, axis=0, keepdims=True))
            rescale = jnp.exp(old_best - new_best)
            weights = jnp.exp(scores - new_best)
            best_ref[request, h] = new_best
            total_ref[request, h] = total_ref[request, h] * rescale + jnp.sum(
                weights, axis=0, keepdims=True
            )
            v_t = v_ref[0, h * HD:(h + 1) * HD, :]
            accum_ref[request, h] = accum_ref[request, h] * rescale + jnp.dot(
                v_t, weights.astype(jnp.bfloat16), preferred_element_type=jnp.float32
            )

    grid_spec = pltpu.PrefetchScalarGridSpec(
        num_scalar_prefetch=3,
        grid=(blocks,),
        in_specs=[
            pl.BlockSpec((1, query_rows, width), lambda b, off, own, val: (off[b], 0, 0)),
            pl.BlockSpec((1, block_size, width), lambda b, off, own, val: (b, 0, 0)),
            pl.BlockSpec((1, width, block_size), lambda b, off, own, val: (b, 0, 0)),
        ],
        out_specs=[
            pl.BlockSpec((requests, heads, 1, query_rows), lambda b, off, own, val: (0, 0, 0, 0)),
            pl.BlockSpec((requests, heads, 1, query_rows), lambda b, off, own, val: (0, 0, 0, 0)),
            pl.BlockSpec((requests, heads, HD, query_rows), lambda b, off, own, val: (0, 0, 0, 0)),
        ],
    )
    resident = 2 * requests * heads * (HD + 16) * query_rows * 4
    return pl.pallas_call(
        kernel,
        grid_spec=grid_spec,
        out_shape=[
            jax.ShapeDtypeStruct((requests, heads, 1, query_rows), jnp.float32),
            jax.ShapeDtypeStruct((requests, heads, 1, query_rows), jnp.float32),
            jax.ShapeDtypeStruct((requests, heads, HD, query_rows), jnp.float32),
        ],
        compiler_params=pltpu.CompilerParams(
            dimension_semantics=("arbitrary",),
            vmem_limit_bytes=resident + 24 * 1024 * 1024,
        ),
    )(owner_offset, owner, valid, ring_queries, keys, values_t)


def per_device(
    cycle,
    hidden,
    norm_gain,
    router_weight,
    att_experts,
    q_weight,
    kv_weight,
    o_weight,
    kv_cache,
    cached_blocks,
    tail_trim,
    block_pool,
):
    head_count = lax.axis_size("heads")
    seq_rank = lax.axis_index("seq")
    block_size = kv_cache.shape[2]
    local_blocks = kv_cache.shape[1]
    local_heads = q_weight.shape[2] // HD
    scale_q = HD ** (-0.5)
    normed = normalize(hidden[0], norm_gain)
    gathered = shift_all_gather(normed, "heads").reshape(-1, normed.shape[1])
    new_count = gathered.shape[0]
    rows_each = new_count // head_count
    head_rank = lax.axis_index("heads")
    token_ids = (
        ((head_rank + jnp.arange(head_count, dtype=jnp.int32)[:, None]) % head_count) * rows_each
        + jnp.arange(rows_each, dtype=jnp.int32)[None, :]
    ).reshape(new_count)
    chosen = jnp.take(att_experts[0], token_ids, axis=0)
    cached_len = cached_blocks * block_size - tail_trim
    positions = cached_len[seq_rank] + token_ids
    onehot, gates = route(gathered, router_weight, chosen)
    every_q = jnp.einsum("nd,edc->nec", gathered, q_weight, preferred_element_type=jnp.float32)
    chosen_q = jnp.sum(onehot[:, :, :, None] * every_q[:, None, :, :], axis=2).reshape(
        new_count, 2, local_heads, HD
    )
    queries = rotate(chosen_q, positions).astype(jnp.bfloat16)
    fresh = jnp.einsum("nd,sdc->snc", gathered, kv_weight, preferred_element_type=jnp.float32)
    new_keys = rotate(fresh[0].reshape(new_count, local_heads, HD), positions).astype(jnp.bfloat16)
    new_values = fresh[1].reshape(new_count, local_heads, HD).astype(jnp.bfloat16)
    ring_queries = ring_all_gather(
        queries.reshape(new_count * 2, local_heads * HD), "seq", cycle
    )
    request_count = ring_queries.shape[0]
    ring_size = len(cycle)
    position_of = np.argsort(np.asarray(cycle))
    position = jnp.asarray(position_of, dtype=jnp.int32)[seq_rank]
    pool_size = block_pool.shape[0]

    global_ids = seq_rank * local_blocks + jnp.arange(local_blocks, dtype=jnp.int32)
    matches = block_pool[None, :] == global_ids[:, None]
    slot_of = jnp.sum(
        jnp.where(matches, jnp.arange(pool_size, dtype=jnp.int32)[None, :], 0), axis=1
    )
    starts = jnp.cumsum(cached_blocks) - cached_blocks
    owner = jnp.sum((starts[None, :] <= slot_of[:, None]).astype(jnp.int32), axis=1) - 1
    ordinal = slot_of - starts[owner]
    owns = owner[None, :] == jnp.arange(request_count, dtype=jnp.int32)[:, None]

    self_scores = (
        jnp.einsum("nkhc,thc->hnkt", queries, new_keys, preferred_element_type=jnp.float32)
        * scale_q
    )
    causal = token_ids[None, :] <= token_ids[:, None]
    self_scores = jnp.where(causal[None, :, None, :], self_scores, NEG_FILL)
    self_best = jnp.max(self_scores, axis=-1)
    self_weights = jnp.exp(self_scores - self_best[..., None])
    self_total = jnp.sum(self_weights, axis=-1)
    self_accum = jnp.einsum(
        "hnkt,thc->hnkc",
        self_weights.astype(jnp.bfloat16),
        new_values,
        preferred_element_type=jnp.float32,
    )
    ring_queries, self_best, self_total, self_accum = lax.optimization_barrier(
        (ring_queries, self_best, self_total, self_accum)
    )
    owner_offset = (jnp.asarray(position_of, dtype=jnp.int32)[owner] - position) % ring_size
    valid = jnp.clip(cached_len[owner] - ordinal * block_size, 0, block_size).astype(jnp.int32)
    query_rows = new_count * 2
    request_best, totals, accum = block_attention(
        ring_queries,
        kv_cache[0],
        jnp.swapaxes(kv_cache[1], 1, 2),
        owner_offset,
        owner,
        valid,
        request_count,
    )
    request_best = request_best[:, :, 0]
    best_hi, best_lo = split_bf16(request_best)
    request_ref = best_hi + best_lo
    present = request_best > 0.5 * NEG_FILL
    adjust = jnp.exp(jnp.where(present, request_best - request_ref, 0.0))
    totals = totals[:, :, 0] * adjust
    accum = accum * adjust[:, :, None, :]
    totals_hi, totals_lo = split_bf16(totals)
    stats = jnp.stack([best_hi, best_lo, totals_hi, totals_lo], axis=1).astype(jnp.bfloat16)
    payload = jnp.concatenate(
        [
            accum.astype(jnp.bfloat16).reshape(request_count, -1, query_rows),
            stats.reshape(request_count, -1, query_rows),
        ],
        axis=1,
    )
    received = lax.all_to_all(payload, "seq", 0, 0, tiled=True)
    acc_rows = local_heads * HD
    sources = received.shape[0]
    part_accum = received[:, :acc_rows].astype(jnp.float32).reshape(
        sources, local_heads, HD, query_rows
    )
    part_stats = received[:, acc_rows:].astype(jnp.float32).reshape(
        sources, 4, local_heads, query_rows
    )
    part_best = part_stats[:, 0] + part_stats[:, 1]
    part_totals = part_stats[:, 2] + part_stats[:, 3]
    cache_best = jnp.max(part_best, axis=0)
    share = jnp.exp(part_best - cache_best[None])
    cache_total = jnp.sum(part_totals * share, axis=0).reshape(local_heads, new_count, 2)
    cache_accum = jnp.transpose(
        jnp.sum(part_accum * share[:, :, None, :], axis=0), (0, 2, 1)
    ).reshape(local_heads, new_count, 2, HD)
    cache_best = cache_best.reshape(local_heads, new_count, 2)

    peak = jnp.maximum(cache_best, self_best)
    cache_share = jnp.exp(cache_best - peak)
    self_share = jnp.exp(self_best - peak)
    numerator = cache_accum * cache_share[..., None] + self_accum * self_share[..., None]
    denominator = cache_total * cache_share + self_total * self_share
    attended = (
        jnp.transpose((numerator / denominator[..., None]).astype(jnp.bfloat16), (1, 2, 0, 3))
        .reshape(new_count, 2, local_heads * HD)
    )
    output_blocks = []
    for block in range(head_count):
        rows = slice(block * rows_each, (block + 1) * rows_each)
        block_out = jnp.zeros((rows_each, o_weight.shape[2]), jnp.float32)
        for expert in range(o_weight.shape[0]):
            weight_expert = jnp.sum(onehot[rows, :, expert] * gates[rows], axis=1)
            picked = jnp.where(
                chosen[rows, 0:1] == expert,
                attended[rows, 0],
                jnp.where(
                    chosen[rows, 1:2] == expert, attended[rows, 1], jnp.zeros_like(attended[rows, 0])
                ),
            )
            block_out = block_out + weight_expert[:, None] * jnp.dot(
                picked, o_weight[expert], preferred_element_type=jnp.float32
            )
        output_blocks.append(block_out.astype(jnp.bfloat16))
    summed = shift_reduce_scatter(output_blocks, "heads")
    return summed[None].astype(jnp.bfloat16)


def solution(mesh):
    return jax.shard_map(
        functools.partial(per_device, tuple(seq_cycle(mesh))),
        mesh=mesh,
        in_specs=(
            P("seq", "heads", None),
            P(),
            P(),
            P("seq", None, None),
            P(None, None, "heads"),
            P(None, None, "heads"),
            P(None, "heads", None),
            P(None, "seq", None, "heads"),
            P(),
            P(),
            P(),
        ),
        out_specs=P("seq", "heads", None),
        check_vma=False,
    )
```

```python
import functools

import numpy as np
import jax
import jax.numpy as jnp
from jax import lax
from jax.experimental import pallas as pl
from jax.experimental.pallas import tpu as pltpu
from jax.sharding import PartitionSpec as P

HD = 128


NEG_FILL = -1e30


def rotate(values, positions):
    half_dim = values.shape[-1] // 2
    inverse = 10000.0 ** (-2.0 * jnp.arange(half_dim, dtype=jnp.float32) / values.shape[-1])
    angles = positions.astype(jnp.float32)[:, None] * inverse[None, :]
    target = (values.shape[0],) + (1,) * (values.ndim - 2) + (2 * half_dim,)
    cosine = jnp.cos(angles)
    sine_part = jnp.sin(angles)
    cosine = jnp.concatenate([cosine, cosine], axis=-1).reshape(target)
    signed_sine = jnp.concatenate([-sine_part, sine_part], axis=-1).reshape(target)
    swapped = jnp.concatenate([values[..., half_dim:], values[..., :half_dim]], axis=-1)
    return values * cosine + swapped * signed_sine


def normalize(rows, norm_gain):
    wide_rows = rows.astype(jnp.float32)
    scaled = wide_rows * lax.rsqrt(jnp.mean(wide_rows * wide_rows, axis=-1, keepdims=True) + 1e-05)
    return (scaled * norm_gain.astype(jnp.float32)).astype(jnp.bfloat16)


def route(normed, router_weight, chosen):
    logits = jnp.dot(normed, router_weight, preferred_element_type=jnp.float32)
    experts_all = router_weight.shape[1]
    onehot = (chosen[:, :, None] == jnp.arange(experts_all, dtype=jnp.int32)[None, None, :]).astype(
        jnp.float32
    )
    picked = jnp.sum(onehot * logits[:, None, :], axis=-1)
    return (onehot, jax.nn.softmax(picked, axis=-1))


def split_bf16(x):
    hi = lax.reduce_precision(x, exponent_bits=8, mantissa_bits=7)
    lo = lax.reduce_precision(x - hi, exponent_bits=8, mantissa_bits=7)
    return hi, lo


def seq_cycle(mesh):
    size = mesh.shape["seq"]
    plain = list(range(size))
    try:
        devices = np.moveaxis(np.asarray(mesh.devices), mesh.axis_names.index("seq"), -1)
        line = devices.reshape(-1, size)[0]
        coords = np.array([list(d.coords) for d in line])
    except Exception:
        return plain
    varying = [k for k in range(coords.shape[1]) if len(set(coords[:, k])) > 1]
    if len(varying) == 1:
        order = sorted(plain, key=lambda j: coords[j, varying[0]])
        return order[0::2] + order[1::2][::-1]
    if len(varying) != 2:
        return plain
    dim_a, dim_b = varying
    values_a = sorted(set(coords[:, dim_a]))
    values_b = sorted(set(coords[:, dim_b]))
    if len(values_a) % 2:
        dim_a, dim_b, values_a, values_b = dim_b, dim_a, values_b, values_a
    if len(values_a) % 2 or len(values_a) * len(values_b) != size:
        return plain
    at = {(coords[j, dim_a], coords[j, dim_b]): j for j in plain}
    cycle = [at[(a, values_b[0])] for a in values_a]
    for row, a in enumerate(reversed(values_a)):
        columns = values_b[1:] if row % 2 == 0 else values_b[1:][::-1]
        cycle += [at[(a, b)] for b in columns]
    if sorted(cycle) != plain:
        return plain
    return cycle


def shift_all_gather(piece, axis_name):
    size = lax.axis_size(axis_name)
    rank = lax.axis_index(axis_name)
    by_offset = [piece] + [
        lax.ppermute(piece, axis_name, [(i, (i + s) % size) for i in range(size)])
        for s in range(1, size)
    ]
    return jnp.stack(by_offset[:1] + by_offset[1:][::-1], axis=0)


def shift_reduce_scatter(blocks, axis_name):
    size = lax.axis_size(axis_name)
    total = blocks[0].astype(jnp.float32)
    for s in range(1, size):
        moved = lax.ppermute(blocks[s], axis_name, [(i, (i + s) % size) for i in range(size)])
        total = total + moved.astype(jnp.float32)
    return total


def ring_all_gather(piece, axis_name, cycle):
    size = len(cycle)
    forward = [(cycle[i], cycle[(i + 1) % size]) for i in range(size)]
    backward = [(cycle[(i + 1) % size], cycle[i]) for i in range(size)]
    ahead = size // 2
    behind = size - 1 - ahead
    from_behind, from_ahead = [], []
    moving = piece
    for _ in range(ahead):
        moving = lax.ppermute(moving, axis_name, forward)
        from_behind.append(moving)
    moving = piece
    for _ in range(behind):
        moving = lax.ppermute(moving, axis_name, backward)
        from_ahead.append(moving)
    return jnp.stack([piece] + from_ahead + from_behind[::-1], axis=0)


def block_attention(ring_queries, keys, values_t, owner_offset, owner, valid, requests):
    blocks, block_size, width = keys.shape
    query_rows = ring_queries.shape[1]
    heads = width // HD
    scale = HD ** (-0.5)

    def kernel(offset_ref, owner_ref, valid_ref, q_ref, k_ref, v_ref, best_ref, total_ref, accum_ref):
        b = pl.program_id(0)

        @pl.when(b == 0)
        def _():
            best_ref[...] = jnp.full(best_ref.shape, NEG_FILL, jnp.float32)
            total_ref[...] = jnp.zeros(total_ref.shape, jnp.float32)
            accum_ref[...] = jnp.zeros(accum_ref.shape, jnp.float32)

        request = owner_ref[b]
        limit = valid_ref[b]
        row = lax.broadcasted_iota(jnp.int32, (block_size, query_rows), 0)
        for h in range(heads):
            q = q_ref[0, :, h * HD:(h + 1) * HD]
            k = k_ref[0, :, h * HD:(h + 1) * HD]
            scores = lax.dot_general(
                k, q, (((1,), (1,)), ((), ())), preferred_element_type=jnp.float32
            ) * scale
            scores = jnp.where(row < limit, scores, NEG_FILL)
            old_best = best_ref[request, h]
            new_best = jnp.maximum(old_best, jnp.max(scores, axis=0, keepdims=True))
            rescale = jnp.exp(old_best - new_best)
            weights = jnp.exp(scores - new_best)
            best_ref[request, h] = new_best
            total_ref[request, h] = total_ref[request, h] * rescale + jnp.sum(
                weights, axis=0, keepdims=True
            )
            v_t = v_ref[0, h * HD:(h + 1) * HD, :]
            accum_ref[request, h] = accum_ref[request, h] * rescale + jnp.dot(
                v_t, weights.astype(jnp.bfloat16), preferred_element_type=jnp.float32
            )

    grid_spec = pltpu.PrefetchScalarGridSpec(
        num_scalar_prefetch=3,
        grid=(blocks,),
        in_specs=[
            pl.BlockSpec((1, query_rows, width), lambda b, off, own, val: (off[b], 0, 0)),
            pl.BlockSpec((1, block_size, width), lambda b, off, own, val: (b, 0, 0)),
            pl.BlockSpec((1, width, block_size), lambda b, off, own, val: (b, 0, 0)),
        ],
        out_specs=[
            pl.BlockSpec((requests, heads, 1, query_rows), lambda b, off, own, val: (0, 0, 0, 0)),
            pl.BlockSpec((requests, heads, 1, query_rows), lambda b, off, own, val: (0, 0, 0, 0)),
            pl.BlockSpec((requests, heads, HD, query_rows), lambda b, off, own, val: (0, 0, 0, 0)),
        ],
    )
    resident = 2 * requests * heads * (HD + 16) * query_rows * 4
    return pl.pallas_call(
        kernel,
        grid_spec=grid_spec,
        out_shape=[
            jax.ShapeDtypeStruct((requests, heads, 1, query_rows), jnp.float32),
            jax.ShapeDtypeStruct((requests, heads, 1, query_rows), jnp.float32),
            jax.ShapeDtypeStruct((requests, heads, HD, query_rows), jnp.float32),
        ],
        compiler_params=pltpu.CompilerParams(
            dimension_semantics=("arbitrary",),
            vmem_limit_bytes=resident + 24 * 1024 * 1024,
        ),
    )(owner_offset, owner, valid, ring_queries, keys, values_t)


def per_device(
    cycle,
    hidden,
    norm_gain,
    router_weight,
    att_experts,
    q_weight,
    kv_weight,
    o_weight,
    kv_cache,
    cached_blocks,
    tail_trim,
    block_pool,
):
    head_count = lax.axis_size("heads")
    seq_rank = lax.axis_index("seq")
    block_size = kv_cache.shape[2]
    local_blocks = kv_cache.shape[1]
    local_heads = q_weight.shape[2] // HD
    scale_q = HD ** (-0.5)
    normed = normalize(hidden[0], norm_gain)
    gathered = shift_all_gather(normed, "heads").reshape(-1, normed.shape[1])
    new_count = gathered.shape[0]
    rows_each = new_count // head_count
    head_rank = lax.axis_index("heads")
    token_ids = (
        ((head_rank + jnp.arange(head_count, dtype=jnp.int32)[:, None]) % head_count) * rows_each
        + jnp.arange(rows_each, dtype=jnp.int32)[None, :]
    ).reshape(new_count)
    chosen = jnp.take(att_experts[0], token_ids, axis=0)
    cached_len = cached_blocks * block_size - tail_trim
    positions = cached_len[seq_rank] + token_ids
    onehot, gates = route(gathered, router_weight, chosen)
    every_q = jnp.einsum("nd,edc->nec", gathered, q_weight, preferred_element_type=jnp.float32)
    chosen_q = jnp.sum(onehot[:, :, :, None] * every_q[:, None, :, :], axis=2).reshape(
        new_count, 2, local_heads, HD
    )
    queries = rotate(chosen_q, positions).astype(jnp.bfloat16)
    fresh = jnp.einsum("nd,sdc->snc", gathered, kv_weight, preferred_element_type=jnp.float32)
    new_keys = rotate(fresh[0].reshape(new_count, local_heads, HD), positions).astype(jnp.bfloat16)
    new_values = fresh[1].reshape(new_count, local_heads, HD).astype(jnp.bfloat16)
    ring_queries = ring_all_gather(
        queries.reshape(new_count * 2, local_heads * HD), "seq", cycle
    )
    request_count = ring_queries.shape[0]
    ring_size = len(cycle)
    position_of = np.argsort(np.asarray(cycle))
    position = jnp.asarray(position_of, dtype=jnp.int32)[seq_rank]
    pool_size = block_pool.shape[0]

    global_ids = seq_rank * local_blocks + jnp.arange(local_blocks, dtype=jnp.int32)
    matches = block_pool[None, :] == global_ids[:, None]
    slot_of = jnp.sum(
        jnp.where(matches, jnp.arange(pool_size, dtype=jnp.int32)[None, :], 0), axis=1
    )
    starts = jnp.cumsum(cached_blocks) - cached_blocks
    owner = jnp.sum((starts[None, :] <= slot_of[:, None]).astype(jnp.int32), axis=1) - 1
    ordinal = slot_of - starts[owner]
    owns = owner[None, :] == jnp.arange(request_count, dtype=jnp.int32)[:, None]

    self_scores = (
        jnp.einsum("nkhc,thc->hnkt", queries, new_keys, preferred_element_type=jnp.float32)
        * scale_q
    )
    causal = token_ids[None, :] <= token_ids[:, None]
    self_scores = jnp.where(causal[None, :, None, :], self_scores, NEG_FILL)
    self_best = jnp.max(self_scores, axis=-1)
    self_weights = jnp.exp(self_scores - self_best[..., None])
    self_total = jnp.sum(self_weights, axis=-1)
    self_accum = jnp.einsum(
        "hnkt,thc->hnkc",
        self_weights.astype(jnp.bfloat16),
        new_values,
        preferred_element_type=jnp.float32,
    )
    ring_queries, self_best, self_total, self_accum = lax.optimization_barrier(
        (ring_queries, self_best, self_total, self_accum)
    )
    owner_offset = (jnp.asarray(position_of, dtype=jnp.int32)[owner] - position) % ring_size
    valid = jnp.clip(cached_len[owner] - ordinal * block_size, 0, block_size).astype(jnp.int32)
    query_rows = new_count * 2
    request_best, totals, accum = block_attention(
        ring_queries,
        kv_cache[0],
        jnp.swapaxes(kv_cache[1], 1, 2),
        owner_offset,
        owner,
        valid,
        request_count,
    )
    request_best = request_best[:, :, 0]
    best_hi, best_lo = split_bf16(request_best)
    request_ref = best_hi + best_lo
    present = request_best > 0.5 * NEG_FILL
    adjust = jnp.exp(jnp.where(present, request_best - request_ref, 0.0))
    totals = totals[:, :, 0] * adjust
    accum = accum * adjust[:, :, None, :]
    totals_hi, totals_lo = split_bf16(totals)
    stats = jnp.stack([best_hi, best_lo, totals_hi, totals_lo], axis=1).astype(jnp.bfloat16)
    payload = jnp.concatenate(
        [
            accum.astype(jnp.bfloat16).reshape(request_count, -1, query_rows),
            stats.reshape(request_count, -1, query_rows),
        ],
        axis=1,
    )
    received = lax.all_to_all(payload, "seq", 0, 0, tiled=True)
    acc_rows = local_heads * HD
    sources = received.shape[0]
    part_accum = received[:, :acc_rows].astype(jnp.float32).reshape(
        sources, local_heads, HD, query_rows
    )
    part_stats = received[:, acc_rows:].astype(jnp.float32).reshape(
        sources, 4, local_heads, query_rows
    )
    part_best = part_stats[:, 0] + part_stats[:, 1]
    part_totals = part_stats[:, 2] + part_stats[:, 3]
    cache_best = jnp.max(part_best, axis=0)
    share = jnp.exp(part_best - cache_best[None])
    cache_total = jnp.sum(part_totals * share, axis=0).reshape(local_heads, new_count, 2)
    cache_accum = jnp.transpose(
        jnp.sum(part_accum * share[:, :, None, :], axis=0), (0, 2, 1)
    ).reshape(local_heads, new_count, 2, HD)
    cache_best = cache_best.reshape(local_heads, new_count, 2)

    peak = jnp.maximum(cache_best, self_best)
    cache_share = jnp.exp(cache_best - peak)
    self_share = jnp.exp(self_best - peak)
    numerator = cache_accum * cache_share[..., None] + self_accum * self_share[..., None]
    denominator = cache_total * cache_share + self_total * self_share
    attended = (
        jnp.transpose((numerator / denominator[..., None]).astype(jnp.bfloat16), (1, 2, 0, 3))
        .reshape(new_count, 2, local_heads * HD)
    )
    output_blocks = []
    for block in range(head_count):
        rows = slice(block * rows_each, (block + 1) * rows_each)
        block_out = jnp.zeros((rows_each, o_weight.shape[2]), jnp.float32)
        for expert in range(o_weight.shape[0]):
            weight_expert = jnp.sum(onehot[rows, :, expert] * gates[rows], axis=1)
            picked = jnp.where(
                chosen[rows, 0:1] == expert,
                attended[rows, 0],
                jnp.where(
                    chosen[rows, 1:2] == expert, attended[rows, 1], jnp.zeros_like(attended[rows, 0])
                ),
            )
            block_out = block_out + weight_expert[:, None] * jnp.dot(
                picked, o_weight[expert], preferred_element_type=jnp.float32
            )
        output_blocks.append(block_out.astype(jnp.bfloat16))
    summed = shift_reduce_scatter(output_blocks, "heads")
    return summed[None].astype(jnp.bfloat16)


def solution(mesh):
    return jax.shard_map(
        functools.partial(per_device, tuple(seq_cycle(mesh))),
        mesh=mesh,
        in_specs=(
            P("seq", "heads", None),
            P(),
            P(),
            P("seq", None, None),
            P(None, None, "heads"),
            P(None, None, "heads"),
            P(None, "heads", None),
            P(None, "seq", None, "heads"),
            P(),
            P(),
            P(),
        ),
        out_specs=P("seq", "heads", None),
        check_vma=False,
    )
```

```python
import functools

import numpy as np
import jax
import jax.numpy as jnp
from jax import lax
from jax.experimental import pallas as pl
from jax.experimental.pallas import tpu as pltpu
from jax.sharding import PartitionSpec as P

HD = 128


NEG_FILL = -1e30


def rotate(values, positions):
    half_dim = values.shape[-1] // 2
    inverse = 10000.0 ** (-2.0 * jnp.arange(half_dim, dtype=jnp.float32) / values.shape[-1])
    angles = positions.astype(jnp.float32)[:, None] * inverse[None, :]
    target = (values.shape[0],) + (1,) * (values.ndim - 2) + (half_dim,)
    cosine = jnp.cos(angles).reshape(target)
    sine_part = jnp.sin(angles).reshape(target)
    leading_part = values[..., :half_dim]
    trailing_part = values[..., half_dim:]
    return jnp.concatenate(
        [
            leading_part * cosine - trailing_part * sine_part,
            trailing_part * cosine + leading_part * sine_part,
        ],
        axis=-1,
    )


def normalize(rows, norm_gain):
    wide_rows = rows.astype(jnp.float32)
    scaled = wide_rows * lax.rsqrt(jnp.mean(wide_rows * wide_rows, axis=-1, keepdims=True) + 1e-05)
    return (scaled * norm_gain.astype(jnp.float32)).astype(jnp.bfloat16)


def route(normed, router_weight, chosen):
    logits = jnp.dot(normed, router_weight, preferred_element_type=jnp.float32)
    experts_all = router_weight.shape[1]
    onehot = (chosen[:, :, None] == jnp.arange(experts_all, dtype=jnp.int32)[None, None, :]).astype(
        jnp.float32
    )
    picked = jnp.sum(onehot * logits[:, None, :], axis=-1)
    return (onehot, jax.nn.softmax(picked, axis=-1))


def split_bf16(x):
    hi = lax.reduce_precision(x, exponent_bits=8, mantissa_bits=7)
    lo = lax.reduce_precision(x - hi, exponent_bits=8, mantissa_bits=7)
    return hi, lo


def seq_cycle(mesh):
    size = mesh.shape["seq"]
    plain = list(range(size))
    try:
        devices = np.moveaxis(np.asarray(mesh.devices), mesh.axis_names.index("seq"), -1)
        line = devices.reshape(-1, size)[0]
        coords = np.array([list(d.coords) for d in line])
    except Exception:
        return plain
    varying = [k for k in range(coords.shape[1]) if len(set(coords[:, k])) > 1]
    if len(varying) == 1:
        order = sorted(plain, key=lambda j: coords[j, varying[0]])
        return order[0::2] + order[1::2][::-1]
    if len(varying) != 2:
        return plain
    dim_a, dim_b = varying
    values_a = sorted(set(coords[:, dim_a]))
    values_b = sorted(set(coords[:, dim_b]))
    if len(values_a) % 2:
        dim_a, dim_b, values_a, values_b = dim_b, dim_a, values_b, values_a
    if len(values_a) % 2 or len(values_a) * len(values_b) != size:
        return plain
    at = {(coords[j, dim_a], coords[j, dim_b]): j for j in plain}
    cycle = [at[(a, values_b[0])] for a in values_a]
    for row, a in enumerate(reversed(values_a)):
        columns = values_b[1:] if row % 2 == 0 else values_b[1:][::-1]
        cycle += [at[(a, b)] for b in columns]
    if sorted(cycle) != plain:
        return plain
    return cycle


def shift_all_gather(piece, axis_name):
    size = lax.axis_size(axis_name)
    rank = lax.axis_index(axis_name)
    by_offset = [piece] + [
        lax.ppermute(piece, axis_name, [(i, (i + s) % size) for i in range(size)])
        for s in range(1, size)
    ]
    return jnp.stack(by_offset[:1] + by_offset[1:][::-1], axis=0)


def shift_reduce_scatter(blocks, axis_name):
    size = lax.axis_size(axis_name)
    total = blocks[0].astype(jnp.float32)
    for s in range(1, size):
        moved = lax.ppermute(blocks[s], axis_name, [(i, (i + s) % size) for i in range(size)])
        total = total + moved.astype(jnp.float32)
    return total


def ring_all_gather(piece, axis_name, cycle):
    size = len(cycle)
    forward = [(cycle[i], cycle[(i + 1) % size]) for i in range(size)]
    backward = [(cycle[(i + 1) % size], cycle[i]) for i in range(size)]
    ahead = size // 2
    behind = size - 1 - ahead
    from_behind, from_ahead = [], []
    moving = piece
    for _ in range(ahead):
        moving = lax.ppermute(moving, axis_name, forward)
        from_behind.append(moving)
    moving = piece
    for _ in range(behind):
        moving = lax.ppermute(moving, axis_name, backward)
        from_ahead.append(moving)
    return jnp.stack([piece] + from_ahead + from_behind[::-1], axis=0)


def block_attention(ring_queries, keys, values_t, owner_offset, owner, valid, requests):
    blocks, block_size, width = keys.shape
    query_rows = ring_queries.shape[1]
    heads = width // HD
    scale = HD ** (-0.5)

    def kernel(offset_ref, owner_ref, valid_ref, q_ref, k_ref, v_ref, best_ref, total_ref, accum_ref):
        b = pl.program_id(0)

        @pl.when(b == 0)
        def _():
            best_ref[...] = jnp.full(best_ref.shape, NEG_FILL, jnp.float32)
            total_ref[...] = jnp.zeros(total_ref.shape, jnp.float32)
            accum_ref[...] = jnp.zeros(accum_ref.shape, jnp.float32)

        request = owner_ref[b]
        limit = valid_ref[b]
        row = lax.broadcasted_iota(jnp.int32, (block_size, query_rows), 0)
        for h in range(heads):
            q = q_ref[0, :, h * HD:(h + 1) * HD]
            k = k_ref[0, :, h * HD:(h + 1) * HD]
            scores = lax.dot_general(
                k, q, (((1,), (1,)), ((), ())), preferred_element_type=jnp.float32
            ) * scale
            scores = jnp.where(row < limit, scores, NEG_FILL)
            old_best = best_ref[request, h]
            new_best = jnp.maximum(old_best, jnp.max(scores, axis=0, keepdims=True))
            rescale = jnp.exp(old_best - new_best)
            weights = jnp.exp(scores - new_best)
            best_ref[request, h] = new_best
            total_ref[request, h] = total_ref[request, h] * rescale + jnp.sum(
                weights, axis=0, keepdims=True
            )
            v_t = v_ref[0, h * HD:(h + 1) * HD, :]
            accum_ref[request, h] = accum_ref[request, h] * rescale + jnp.dot(
                v_t, weights.astype(jnp.bfloat16), preferred_element_type=jnp.float32
            )

    grid_spec = pltpu.PrefetchScalarGridSpec(
        num_scalar_prefetch=3,
        grid=(blocks,),
        in_specs=[
            pl.BlockSpec((1, query_rows, width), lambda b, off, own, val: (off[b], 0, 0)),
            pl.BlockSpec((1, block_size, width), lambda b, off, own, val: (b, 0, 0)),
            pl.BlockSpec((1, width, block_size), lambda b, off, own, val: (b, 0, 0)),
        ],
        out_specs=[
            pl.BlockSpec((requests, heads, 1, query_rows), lambda b, off, own, val: (0, 0, 0, 0)),
            pl.BlockSpec((requests, heads, 1, query_rows), lambda b, off, own, val: (0, 0, 0, 0)),
            pl.BlockSpec((requests, heads, HD, query_rows), lambda b, off, own, val: (0, 0, 0, 0)),
        ],
    )
    resident = 2 * requests * heads * (HD + 16) * query_rows * 4
    return pl.pallas_call(
        kernel,
        grid_spec=grid_spec,
        out_shape=[
            jax.ShapeDtypeStruct((requests, heads, 1, query_rows), jnp.float32),
            jax.ShapeDtypeStruct((requests, heads, 1, query_rows), jnp.float32),
            jax.ShapeDtypeStruct((requests, heads, HD, query_rows), jnp.float32),
        ],
        compiler_params=pltpu.CompilerParams(
            dimension_semantics=("arbitrary",),
            vmem_limit_bytes=resident + 24 * 1024 * 1024,
        ),
    )(owner_offset, owner, valid, ring_queries, keys, values_t)


def per_device(
    cycle,
    hidden,
    norm_gain,
    router_weight,
    att_experts,
    q_weight,
    kv_weight,
    o_weight,
    kv_cache,
    cached_blocks,
    tail_trim,
    block_pool,
):
    head_count = lax.axis_size("heads")
    seq_rank = lax.axis_index("seq")
    block_size = kv_cache.shape[2]
    local_blocks = kv_cache.shape[1]
    local_heads = q_weight.shape[2] // HD
    scale_q = HD ** (-0.5)
    normed = normalize(hidden[0], norm_gain)
    gathered = shift_all_gather(normed, "heads").reshape(-1, normed.shape[1])
    new_count = gathered.shape[0]
    rows_each = new_count // head_count
    head_rank = lax.axis_index("heads")
    token_ids = (
        ((head_rank + jnp.arange(head_count, dtype=jnp.int32)[:, None]) % head_count) * rows_each
        + jnp.arange(rows_each, dtype=jnp.int32)[None, :]
    ).reshape(new_count)
    chosen = jnp.take(att_experts[0], token_ids, axis=0)
    cached_len = cached_blocks * block_size - tail_trim
    positions = cached_len[seq_rank] + token_ids
    onehot, gates = route(gathered, router_weight, chosen)
    expert_ids = jnp.arange(q_weight.shape[0], dtype=jnp.int32)
    slot_queries = []
    for slot in range(chosen.shape[1]):
        picks = chosen[:, slot][None, :, None] == expert_ids[:, None, None]
        masked = jnp.where(picks, gathered[None], jnp.zeros_like(gathered[None]))
        slot_queries.append(
            jnp.einsum("end,edc->nc", masked, q_weight, preferred_element_type=jnp.float32)
        )
    chosen_q = jnp.stack(slot_queries, axis=1).reshape(new_count, 2, local_heads, HD)
    queries = rotate(chosen_q, positions).astype(jnp.bfloat16)
    fresh = jnp.einsum("nd,sdc->snc", gathered, kv_weight, preferred_element_type=jnp.float32)
    new_keys = rotate(fresh[0].reshape(new_count, local_heads, HD), positions).astype(jnp.bfloat16)
    new_values = fresh[1].reshape(new_count, local_heads, HD).astype(jnp.bfloat16)
    ring_queries = ring_all_gather(
        queries.reshape(new_count * 2, local_heads * HD), "seq", cycle
    )
    request_count = ring_queries.shape[0]
    ring_size = len(cycle)
    position_of = np.argsort(np.asarray(cycle))
    position = jnp.asarray(position_of, dtype=jnp.int32)[seq_rank]
    pool_size = block_pool.shape[0]

    global_ids = seq_rank * local_blocks + jnp.arange(local_blocks, dtype=jnp.int32)
    matches = block_pool[None, :] == global_ids[:, None]
    slot_of = jnp.sum(
        jnp.where(matches, jnp.arange(pool_size, dtype=jnp.int32)[None, :], 0), axis=1
    )
    starts = jnp.cumsum(cached_blocks) - cached_blocks
    owner = jnp.sum((starts[None, :] <= slot_of[:, None]).astype(jnp.int32), axis=1) - 1
    ordinal = slot_of - starts[owner]
    owns = owner[None, :] == jnp.arange(request_count, dtype=jnp.int32)[:, None]

    self_scores = (
        jnp.einsum("nkhc,thc->hnkt", queries, new_keys, preferred_element_type=jnp.float32)
        * scale_q
    )
    causal = token_ids[None, :] <= token_ids[:, None]
    self_scores = jnp.where(causal[None, :, None, :], self_scores, NEG_FILL)
    self_best = jnp.max(self_scores, axis=-1)
    self_weights = jnp.exp(self_scores - self_best[..., None])
    self_total = jnp.sum(self_weights, axis=-1)
    self_accum = jnp.einsum(
        "hnkt,thc->hnkc",
        self_weights.astype(jnp.bfloat16),
        new_values,
        preferred_element_type=jnp.float32,
    )
    ring_queries, self_best, self_total, self_accum = lax.optimization_barrier(
        (ring_queries, self_best, self_total, self_accum)
    )
    owner_offset = (jnp.asarray(position_of, dtype=jnp.int32)[owner] - position) % ring_size
    valid = jnp.clip(cached_len[owner] - ordinal * block_size, 0, block_size).astype(jnp.int32)
    query_rows = new_count * 2
    request_best, totals, accum = block_attention(
        ring_queries,
        kv_cache[0],
        jnp.swapaxes(kv_cache[1], 1, 2),
        owner_offset,
        owner,
        valid,
        request_count,
    )
    request_best = request_best[:, :, 0]
    best_hi, best_lo = split_bf16(request_best)
    request_ref = best_hi + best_lo
    present = request_best > 0.5 * NEG_FILL
    adjust = jnp.exp(jnp.where(present, request_best - request_ref, 0.0))
    totals = totals[:, :, 0] * adjust
    accum = accum * adjust[:, :, None, :]
    totals_hi, totals_lo = split_bf16(totals)
    stats = jnp.stack([best_hi, best_lo, totals_hi, totals_lo], axis=1).astype(jnp.bfloat16)
    payload = jnp.concatenate(
        [
            accum.astype(jnp.bfloat16).reshape(request_count, -1, query_rows),
            stats.reshape(request_count, -1, query_rows),
        ],
        axis=1,
    )
    received = lax.all_to_all(payload, "seq", 0, 0, tiled=True)
    acc_rows = local_heads * HD
    sources = received.shape[0]
    part_accum = received[:, :acc_rows].astype(jnp.float32).reshape(
        sources, local_heads, HD, query_rows
    )
    part_stats = received[:, acc_rows:].astype(jnp.float32).reshape(
        sources, 4, local_heads, query_rows
    )
    part_best = part_stats[:, 0] + part_stats[:, 1]
    part_totals = part_stats[:, 2] + part_stats[:, 3]
    cache_best = jnp.max(part_best, axis=0)
    share = jnp.exp(part_best - cache_best[None])
    cache_total = jnp.sum(part_totals * share, axis=0).reshape(local_heads, new_count, 2)
    cache_accum = jnp.transpose(
        jnp.sum(part_accum * share[:, :, None, :], axis=0), (0, 2, 1)
    ).reshape(local_heads, new_count, 2, HD)
    cache_best = cache_best.reshape(local_heads, new_count, 2)

    peak = jnp.maximum(cache_best, self_best)
    cache_share = jnp.exp(cache_best - peak)
    self_share = jnp.exp(self_best - peak)
    numerator = cache_accum * cache_share[..., None] + self_accum * self_share[..., None]
    denominator = cache_total * cache_share + self_total * self_share
    attended = (
        jnp.transpose((numerator / denominator[..., None]).astype(jnp.bfloat16), (1, 2, 0, 3))
        .reshape(new_count, 2, local_heads * HD)
    )
    output_blocks = []
    for block in range(head_count):
        rows = slice(block * rows_each, (block + 1) * rows_each)
        block_out = jnp.zeros((rows_each, o_weight.shape[2]), jnp.float32)
        for expert in range(o_weight.shape[0]):
            weight_expert = jnp.sum(onehot[rows, :, expert] * gates[rows], axis=1)
            picked = jnp.where(
                chosen[rows, 0:1] == expert,
                attended[rows, 0],
                jnp.where(
                    chosen[rows, 1:2] == expert, attended[rows, 1], jnp.zeros_like(attended[rows, 0])
                ),
            )
            block_out = block_out + weight_expert[:, None] * jnp.dot(
                picked, o_weight[expert], preferred_element_type=jnp.float32
            )
        output_blocks.append(block_out.astype(jnp.bfloat16))
    summed = shift_reduce_scatter(output_blocks, "heads")
    return summed[None].astype(jnp.bfloat16)


def solution(mesh):
    return jax.shard_map(
        functools.partial(per_device, tuple(seq_cycle(mesh))),
        mesh=mesh,
        in_specs=(
            P("seq", "heads", None),
            P(),
            P(),
            P("seq", None, None),
            P(None, None, "heads"),
            P(None, None, "heads"),
            P(None, "heads", None),
            P(None, "seq", None, "heads"),
            P(),
            P(),
            P(),
        ),
        out_specs=P("seq", "heads", None),
        check_vma=False,
    )
```

```python
import functools

import numpy as np
import jax
import jax.numpy as jnp
from jax import lax
from jax.experimental import pallas as pl
from jax.experimental.pallas import tpu as pltpu
from jax.sharding import PartitionSpec as P

HD = 128


NEG_FILL = -1e30


def rotate(values, positions):
    half_dim = values.shape[-1] // 2
    inverse = 10000.0 ** (-2.0 * jnp.arange(half_dim, dtype=jnp.float32) / values.shape[-1])
    angles = positions.astype(jnp.float32)[:, None] * inverse[None, :]
    target = (values.shape[0],) + (1,) * (values.ndim - 2) + (half_dim,)
    cosine = jnp.cos(angles).reshape(target)
    sine_part = jnp.sin(angles).reshape(target)
    leading_part = values[..., :half_dim]
    trailing_part = values[..., half_dim:]
    return jnp.concatenate(
        [
            leading_part * cosine - trailing_part * sine_part,
            trailing_part * cosine + leading_part * sine_part,
        ],
        axis=-1,
    )


def normalize(rows, norm_gain):
    wide_rows = rows.astype(jnp.float32)
    scaled = wide_rows * lax.rsqrt(jnp.mean(wide_rows * wide_rows, axis=-1, keepdims=True) + 1e-05)
    return (scaled * norm_gain.astype(jnp.float32)).astype(jnp.bfloat16)


def route(normed, router_weight, chosen):
    logits = jnp.dot(normed, router_weight, preferred_element_type=jnp.float32)
    experts_all = router_weight.shape[1]
    onehot = (chosen[:, :, None] == jnp.arange(experts_all, dtype=jnp.int32)[None, None, :]).astype(
        jnp.float32
    )
    picked = jnp.sum(onehot * logits[:, None, :], axis=-1)
    return (onehot, jax.nn.softmax(picked, axis=-1))


def split_bf16(x):
    hi = lax.reduce_precision(x, exponent_bits=8, mantissa_bits=7)
    lo = lax.reduce_precision(x - hi, exponent_bits=8, mantissa_bits=7)
    return hi, lo


def seq_cycle(mesh):
    size = mesh.shape["seq"]
    plain = list(range(size))
    try:
        devices = np.moveaxis(np.asarray(mesh.devices), mesh.axis_names.index("seq"), -1)
        line = devices.reshape(-1, size)[0]
        coords = np.array([list(d.coords) for d in line])
    except Exception:
        return plain
    varying = [k for k in range(coords.shape[1]) if len(set(coords[:, k])) > 1]
    if len(varying) == 1:
        order = sorted(plain, key=lambda j: coords[j, varying[0]])
        return order[0::2] + order[1::2][::-1]
    if len(varying) != 2:
        return plain
    dim_a, dim_b = varying
    values_a = sorted(set(coords[:, dim_a]))
    values_b = sorted(set(coords[:, dim_b]))
    if len(values_a) % 2:
        dim_a, dim_b, values_a, values_b = dim_b, dim_a, values_b, values_a
    if len(values_a) % 2 or len(values_a) * len(values_b) != size:
        return plain
    at = {(coords[j, dim_a], coords[j, dim_b]): j for j in plain}
    cycle = [at[(a, values_b[0])] for a in values_a]
    for row, a in enumerate(reversed(values_a)):
        columns = values_b[1:] if row % 2 == 0 else values_b[1:][::-1]
        cycle += [at[(a, b)] for b in columns]
    if sorted(cycle) != plain:
        return plain
    return cycle


def shift_all_gather(piece, axis_name):
    size = lax.axis_size(axis_name)
    rank = lax.axis_index(axis_name)
    by_offset = [piece] + [
        lax.ppermute(piece, axis_name, [(i, (i + s) % size) for i in range(size)])
        for s in range(1, size)
    ]
    return jnp.stack(by_offset[:1] + by_offset[1:][::-1], axis=0)


def shift_reduce_scatter(blocks, axis_name):
    size = lax.axis_size(axis_name)
    total = blocks[0].astype(jnp.float32)
    for s in range(1, size):
        moved = lax.ppermute(blocks[s], axis_name, [(i, (i + s) % size) for i in range(size)])
        total = total + moved.astype(jnp.float32)
    return total


def ring_all_gather(piece, axis_name, cycle):
    size = len(cycle)
    forward = [(cycle[i], cycle[(i + 1) % size]) for i in range(size)]
    backward = [(cycle[(i + 1) % size], cycle[i]) for i in range(size)]
    ahead = size // 2
    behind = size - 1 - ahead
    from_behind, from_ahead = [], []
    moving = piece
    for _ in range(ahead):
        moving = lax.ppermute(moving, axis_name, forward)
        from_behind.append(moving)
    moving = piece
    for _ in range(behind):
        moving = lax.ppermute(moving, axis_name, backward)
        from_ahead.append(moving)
    return jnp.stack([piece] + from_ahead + from_behind[::-1], axis=0)


def block_attention(ring_queries, keys, values_t, owner_offset, owner, valid, requests):
    blocks, block_size, width = keys.shape
    query_rows = ring_queries.shape[1]
    heads = width // HD
    scale = HD ** (-0.5)

    def kernel(offset_ref, owner_ref, valid_ref, q_ref, k_ref, v_ref, best_ref, total_ref, accum_ref):
        b = pl.program_id(0)

        @pl.when(b == 0)
        def _():
            best_ref[...] = jnp.full(best_ref.shape, NEG_FILL, jnp.float32)
            total_ref[...] = jnp.zeros(total_ref.shape, jnp.float32)
            accum_ref[...] = jnp.zeros(accum_ref.shape, jnp.float32)

        request = owner_ref[b]
        limit = valid_ref[b]
        row = lax.broadcasted_iota(jnp.int32, (block_size, query_rows), 0)
        for h in range(heads):
            q = q_ref[0, :, h * HD:(h + 1) * HD]
            k = k_ref[0, :, h * HD:(h + 1) * HD]
            scores = lax.dot_general(
                k, q, (((1,), (1,)), ((), ())), preferred_element_type=jnp.float32
            ) * scale
            scores = jnp.where(row < limit, scores, NEG_FILL)
            old_best = best_ref[request, h]
            new_best = jnp.maximum(old_best, jnp.max(scores, axis=0, keepdims=True))
            rescale = jnp.exp(old_best - new_best)
            weights = jnp.exp(scores - new_best)
            best_ref[request, h] = new_best
            total_ref[request, h] = total_ref[request, h] * rescale + jnp.sum(
                weights, axis=0, keepdims=True
            )
            v_t = v_ref[0, h * HD:(h + 1) * HD, :]
            accum_ref[request, h] = accum_ref[request, h] * rescale + jnp.dot(
                v_t, weights.astype(jnp.bfloat16), preferred_element_type=jnp.float32
            )

    grid_spec = pltpu.PrefetchScalarGridSpec(
        num_scalar_prefetch=3,
        grid=(blocks,),
        in_specs=[
            pl.BlockSpec((1, query_rows, width), lambda b, off, own, val: (off[b], 0, 0)),
            pl.BlockSpec((1, block_size, width), lambda b, off, own, val: (b, 0, 0)),
            pl.BlockSpec((1, width, block_size), lambda b, off, own, val: (b, 0, 0)),
        ],
        out_specs=[
            pl.BlockSpec((requests, heads, 1, query_rows), lambda b, off, own, val: (0, 0, 0, 0)),
            pl.BlockSpec((requests, heads, 1, query_rows), lambda b, off, own, val: (0, 0, 0, 0)),
            pl.BlockSpec((requests, heads, HD, query_rows), lambda b, off, own, val: (0, 0, 0, 0)),
        ],
    )
    resident = 2 * requests * heads * (HD + 16) * query_rows * 4
    return pl.pallas_call(
        kernel,
        grid_spec=grid_spec,
        out_shape=[
            jax.ShapeDtypeStruct((requests, heads, 1, query_rows), jnp.float32),
            jax.ShapeDtypeStruct((requests, heads, 1, query_rows), jnp.float32),
            jax.ShapeDtypeStruct((requests, heads, HD, query_rows), jnp.float32),
        ],
        compiler_params=pltpu.CompilerParams(
            dimension_semantics=("arbitrary",),
            vmem_limit_bytes=resident + 24 * 1024 * 1024,
        ),
    )(owner_offset, owner, valid, ring_queries, keys, values_t)


def per_device(
    cycle,
    hidden,
    norm_gain,
    router_weight,
    att_experts,
    q_weight,
    kv_weight,
    o_weight,
    kv_cache,
    cached_blocks,
    tail_trim,
    block_pool,
):
    head_count = lax.axis_size("heads")
    seq_rank = lax.axis_index("seq")
    block_size = kv_cache.shape[2]
    local_blocks = kv_cache.shape[1]
    local_heads = q_weight.shape[2] // HD
    scale_q = HD ** (-0.5)
    normed = normalize(hidden[0], norm_gain)
    gathered = shift_all_gather(normed, "heads").reshape(-1, normed.shape[1])
    new_count = gathered.shape[0]
    rows_each = new_count // head_count
    head_rank = lax.axis_index("heads")
    token_ids = (
        ((head_rank + jnp.arange(head_count, dtype=jnp.int32)[:, None]) % head_count) * rows_each
        + jnp.arange(rows_each, dtype=jnp.int32)[None, :]
    ).reshape(new_count)
    chosen = jnp.take(att_experts[0], token_ids, axis=0)
    cached_len = cached_blocks * block_size - tail_trim
    positions = cached_len[seq_rank] + token_ids
    onehot, gates = route(gathered, router_weight, chosen)
    every_q = jnp.einsum("nd,edc->nec", gathered, q_weight, preferred_element_type=jnp.float32)
    chosen_q = jnp.sum(onehot[:, :, :, None] * every_q[:, None, :, :], axis=2).reshape(
        new_count, 2, local_heads, HD
    )
    queries = rotate(chosen_q, positions).astype(jnp.bfloat16)
    fresh = jnp.einsum("nd,sdc->snc", gathered, kv_weight, preferred_element_type=jnp.float32)
    new_keys = rotate(fresh[0].reshape(new_count, local_heads, HD), positions).astype(jnp.bfloat16)
    new_values = fresh[1].reshape(new_count, local_heads, HD).astype(jnp.bfloat16)
    ring_queries = ring_all_gather(
        queries.reshape(new_count * 2, local_heads * HD), "seq", cycle
    )
    request_count = ring_queries.shape[0]
    ring_size = len(cycle)
    position_of = np.argsort(np.asarray(cycle))
    position = jnp.asarray(position_of, dtype=jnp.int32)[seq_rank]
    pool_size = block_pool.shape[0]

    global_ids = seq_rank * local_blocks + jnp.arange(local_blocks, dtype=jnp.int32)
    matches = block_pool[None, :] == global_ids[:, None]
    slot_of = jnp.sum(
        jnp.where(matches, jnp.arange(pool_size, dtype=jnp.int32)[None, :], 0), axis=1
    )
    starts = jnp.cumsum(cached_blocks) - cached_blocks
    owner = jnp.sum((starts[None, :] <= slot_of[:, None]).astype(jnp.int32), axis=1) - 1
    ordinal = slot_of - starts[owner]
    owns = owner[None, :] == jnp.arange(request_count, dtype=jnp.int32)[:, None]

    self_scores = (
        jnp.einsum("nkhc,thc->hnkt", queries, new_keys, preferred_element_type=jnp.float32)
        * scale_q
    )
    causal = token_ids[None, :] <= token_ids[:, None]
    self_scores = jnp.where(causal[None, :, None, :], self_scores, NEG_FILL)
    self_best = jnp.max(self_scores, axis=-1)
    self_weights = jnp.exp(self_scores - self_best[..., None])
    self_total = jnp.sum(self_weights, axis=-1)
    self_accum = jnp.einsum(
        "hnkt,thc->hnkc",
        self_weights.astype(jnp.bfloat16),
        new_values,
        preferred_element_type=jnp.float32,
    )
    ring_queries, self_best, self_total, self_accum = lax.optimization_barrier(
        (ring_queries, self_best, self_total, self_accum)
    )
    owner_offset = (jnp.asarray(position_of, dtype=jnp.int32)[owner] - position) % ring_size
    valid = jnp.clip(cached_len[owner] - ordinal * block_size, 0, block_size).astype(jnp.int32)
    query_rows = new_count * 2
    request_best, totals, accum = block_attention(
        ring_queries,
        kv_cache[0],
        jnp.swapaxes(kv_cache[1], 1, 2),
        owner_offset,
        owner,
        valid,
        request_count,
    )
    request_best = request_best[:, :, 0]
    best_hi, best_lo = split_bf16(request_best)
    request_ref = best_hi + best_lo
    present = request_best > 0.5 * NEG_FILL
    adjust = jnp.exp(jnp.where(present, request_best - request_ref, 0.0))
    totals = totals[:, :, 0] * adjust
    accum = accum * adjust[:, :, None, :]
    totals_hi, totals_lo = split_bf16(totals)
    stats = jnp.stack([best_hi, best_lo, totals_hi, totals_lo], axis=1).astype(jnp.bfloat16)
    payload = jnp.concatenate(
        [
            accum.astype(jnp.bfloat16).reshape(request_count, -1, query_rows),
            stats.reshape(request_count, -1, query_rows),
        ],
        axis=1,
    )
    cycle_arr = jnp.asarray(cycle, dtype=jnp.int32)
    arrivals = [lax.dynamic_index_in_dim(payload, seq_rank, 0, keepdims=False)]
    for s in range(1, ring_size):
        target = cycle_arr[(position + s) % ring_size]
        pairs = [(cycle[i], cycle[(i + s) % ring_size]) for i in range(ring_size)]
        arrivals.append(
            lax.ppermute(lax.dynamic_index_in_dim(payload, target, 0, keepdims=False), "seq", pairs)
        )
    received = jnp.stack(arrivals, axis=0)
    acc_rows = local_heads * HD
    sources = received.shape[0]
    part_accum = received[:, :acc_rows].astype(jnp.float32).reshape(
        sources, local_heads, HD, query_rows
    )
    part_stats = received[:, acc_rows:].astype(jnp.float32).reshape(
        sources, 4, local_heads, query_rows
    )
    part_best = part_stats[:, 0] + part_stats[:, 1]
    part_totals = part_stats[:, 2] + part_stats[:, 3]
    cache_best = jnp.max(part_best, axis=0)
    share = jnp.exp(part_best - cache_best[None])
    cache_total = jnp.sum(part_totals * share, axis=0).reshape(local_heads, new_count, 2)
    cache_accum = jnp.transpose(
        jnp.sum(part_accum * share[:, :, None, :], axis=0), (0, 2, 1)
    ).reshape(local_heads, new_count, 2, HD)
    cache_best = cache_best.reshape(local_heads, new_count, 2)

    peak = jnp.maximum(cache_best, self_best)
    cache_share = jnp.exp(cache_best - peak)
    self_share = jnp.exp(self_best - peak)
    numerator = cache_accum * cache_share[..., None] + self_accum * self_share[..., None]
    denominator = cache_total * cache_share + self_total * self_share
    attended = (
        jnp.transpose((numerator / denominator[..., None]).astype(jnp.bfloat16), (1, 2, 0, 3))
        .reshape(new_count, 2, local_heads * HD)
    )
    output_blocks = []
    for block in range(head_count):
        rows = slice(block * rows_each, (block + 1) * rows_each)
        block_out = jnp.zeros((rows_each, o_weight.shape[2]), jnp.float32)
        for expert in range(o_weight.shape[0]):
            weight_expert = jnp.sum(onehot[rows, :, expert] * gates[rows], axis=1)
            picked = jnp.where(
                chosen[rows, 0:1] == expert,
                attended[rows, 0],
                jnp.where(
                    chosen[rows, 1:2] == expert, attended[rows, 1], jnp.zeros_like(attended[rows, 0])
                ),
            )
            block_out = block_out + weight_expert[:, None] * jnp.dot(
                picked, o_weight[expert], preferred_element_type=jnp.float32
            )
        output_blocks.append(block_out.astype(jnp.bfloat16))
    summed = shift_reduce_scatter(output_blocks, "heads")
    return summed[None].astype(jnp.bfloat16)


def solution(mesh):
    return jax.shard_map(
        functools.partial(per_device, tuple(seq_cycle(mesh))),
        mesh=mesh,
        in_specs=(
            P("seq", "heads", None),
            P(),
            P(),
            P("seq", None, None),
            P(None, None, "heads"),
            P(None, None, "heads"),
            P(None, "heads", None),
            P(None, "seq", None, "heads"),
            P(),
            P(),
            P(),
        ),
        out_specs=P("seq", "heads", None),
        check_vma=False,
    )
```

```python
import functools

import numpy as np
import jax
import jax.numpy as jnp
from jax import lax
from jax.experimental import pallas as pl
from jax.experimental.pallas import tpu as pltpu
from jax.sharding import PartitionSpec as P

HD = 128


NEG_FILL = -1e30


def rotate(values, positions):
    half_dim = values.shape[-1] // 2
    inverse = 10000.0 ** (-2.0 * jnp.arange(half_dim, dtype=jnp.float32) / values.shape[-1])
    angles = positions.astype(jnp.float32)[:, None] * inverse[None, :]
    target = (values.shape[0],) + (1,) * (values.ndim - 2) + (half_dim,)
    cosine = jnp.cos(angles).reshape(target)
    sine_part = jnp.sin(angles).reshape(target)
    leading_part = values[..., :half_dim]
    trailing_part = values[..., half_dim:]
    return jnp.concatenate(
        [
            leading_part * cosine - trailing_part * sine_part,
            trailing_part * cosine + leading_part * sine_part,
        ],
        axis=-1,
    )


def normalize(rows, norm_gain):
    wide_rows = rows.astype(jnp.float32)
    scaled = wide_rows * lax.rsqrt(jnp.mean(wide_rows * wide_rows, axis=-1, keepdims=True) + 1e-05)
    return (scaled * norm_gain.astype(jnp.float32)).astype(jnp.bfloat16)


def route(normed, router_weight, chosen):
    logits = jnp.dot(normed, router_weight, preferred_element_type=jnp.float32)
    experts_all = router_weight.shape[1]
    onehot = (chosen[:, :, None] == jnp.arange(experts_all, dtype=jnp.int32)[None, None, :]).astype(
        jnp.float32
    )
    picked = jnp.sum(onehot * logits[:, None, :], axis=-1)
    return (onehot, jax.nn.softmax(picked, axis=-1))


def split_bf16(x):
    hi = lax.reduce_precision(x, exponent_bits=8, mantissa_bits=7)
    lo = lax.reduce_precision(x - hi, exponent_bits=8, mantissa_bits=7)
    return hi, lo


def seq_cycle(mesh):
    size = mesh.shape["seq"]
    plain = list(range(size))
    try:
        devices = np.moveaxis(np.asarray(mesh.devices), mesh.axis_names.index("seq"), -1)
        line = devices.reshape(-1, size)[0]
        coords = np.array([list(d.coords) for d in line])
    except Exception:
        return plain
    varying = [k for k in range(coords.shape[1]) if len(set(coords[:, k])) > 1]
    if len(varying) == 1:
        order = sorted(plain, key=lambda j: coords[j, varying[0]])
        return order[0::2] + order[1::2][::-1]
    if len(varying) != 2:
        return plain
    dim_a, dim_b = varying
    values_a = sorted(set(coords[:, dim_a]))
    values_b = sorted(set(coords[:, dim_b]))
    if len(values_a) % 2:
        dim_a, dim_b, values_a, values_b = dim_b, dim_a, values_b, values_a
    if len(values_a) % 2 or len(values_a) * len(values_b) != size:
        return plain
    at = {(coords[j, dim_a], coords[j, dim_b]): j for j in plain}
    cycle = [at[(a, values_b[0])] for a in values_a]
    for row, a in enumerate(reversed(values_a)):
        columns = values_b[1:] if row % 2 == 0 else values_b[1:][::-1]
        cycle += [at[(a, b)] for b in columns]
    if sorted(cycle) != plain:
        return plain
    return cycle


def shift_all_gather(piece, axis_name):
    size = lax.axis_size(axis_name)
    rank = lax.axis_index(axis_name)
    by_offset = [piece] + [
        lax.ppermute(piece, axis_name, [(i, (i + s) % size) for i in range(size)])
        for s in range(1, size)
    ]
    return jnp.stack(by_offset[:1] + by_offset[1:][::-1], axis=0)


def shift_reduce_scatter(blocks, axis_name):
    size = lax.axis_size(axis_name)
    total = blocks[0].astype(jnp.float32)
    for s in range(1, size):
        moved = lax.ppermute(blocks[s], axis_name, [(i, (i + s) % size) for i in range(size)])
        total = total + moved.astype(jnp.float32)
    return total


def ring_all_gather(piece, axis_name, cycle):
    size = len(cycle)
    forward = [(cycle[i], cycle[(i + 1) % size]) for i in range(size)]
    backward = [(cycle[(i + 1) % size], cycle[i]) for i in range(size)]
    ahead = size // 2
    behind = size - 1 - ahead
    from_behind, from_ahead = [], []
    moving = piece
    for _ in range(ahead):
        moving = lax.ppermute(moving, axis_name, forward)
        from_behind.append(moving)
    moving = piece
    for _ in range(behind):
        moving = lax.ppermute(moving, axis_name, backward)
        from_ahead.append(moving)
    return jnp.stack([piece] + from_ahead + from_behind[::-1], axis=0)


def block_attention(ring_queries, keys, values_t, owner_offset, owner, valid, requests):
    blocks, block_size, width = keys.shape
    query_rows = ring_queries.shape[1]
    heads = width // HD
    scale = HD ** (-0.5)

    def kernel(offset_ref, owner_ref, valid_ref, q_ref, k_ref, v_ref, best_ref, total_ref, accum_ref):
        b = pl.program_id(0)

        @pl.when(b == 0)
        def _():
            best_ref[...] = jnp.full(best_ref.shape, NEG_FILL, jnp.float32)
            total_ref[...] = jnp.zeros(total_ref.shape, jnp.float32)
            accum_ref[...] = jnp.zeros(accum_ref.shape, jnp.float32)

        request = owner_ref[b]
        limit = valid_ref[b]
        row = lax.broadcasted_iota(jnp.int32, (block_size, query_rows), 0)
        for h in range(heads):
            q = q_ref[0, :, h * HD:(h + 1) * HD]
            k = k_ref[0, :, h * HD:(h + 1) * HD]
            scores = lax.dot_general(
                k, q, (((1,), (1,)), ((), ())), preferred_element_type=jnp.float32
            ) * scale
            scores = jnp.where(row < limit, scores, NEG_FILL)
            old_best = best_ref[request, h]
            new_best = jnp.maximum(old_best, jnp.max(scores, axis=0, keepdims=True))
            rescale = jnp.exp(old_best - new_best)
            weights = jnp.exp(scores - new_best)
            best_ref[request, h] = new_best
            total_ref[request, h] = total_ref[request, h] * rescale + jnp.sum(
                weights, axis=0, keepdims=True
            )
            v_t = v_ref[0, h * HD:(h + 1) * HD, :]
            accum_ref[request, h] = accum_ref[request, h] * rescale + jnp.dot(
                v_t, weights.astype(jnp.bfloat16), preferred_element_type=jnp.float32
            )

    grid_spec = pltpu.PrefetchScalarGridSpec(
        num_scalar_prefetch=3,
        grid=(blocks,),
        in_specs=[
            pl.BlockSpec((1, query_rows, width), lambda b, off, own, val: (off[b], 0, 0)),
            pl.BlockSpec((1, block_size, width), lambda b, off, own, val: (b, 0, 0)),
            pl.BlockSpec((1, width, block_size), lambda b, off, own, val: (b, 0, 0)),
        ],
        out_specs=[
            pl.BlockSpec((requests, heads, 1, query_rows), lambda b, off, own, val: (0, 0, 0, 0)),
            pl.BlockSpec((requests, heads, 1, query_rows), lambda b, off, own, val: (0, 0, 0, 0)),
            pl.BlockSpec((requests, heads, HD, query_rows), lambda b, off, own, val: (0, 0, 0, 0)),
        ],
    )
    resident = 2 * requests * heads * (HD + 16) * query_rows * 4
    return pl.pallas_call(
        kernel,
        grid_spec=grid_spec,
        out_shape=[
            jax.ShapeDtypeStruct((requests, heads, 1, query_rows), jnp.float32),
            jax.ShapeDtypeStruct((requests, heads, 1, query_rows), jnp.float32),
            jax.ShapeDtypeStruct((requests, heads, HD, query_rows), jnp.float32),
        ],
        compiler_params=pltpu.CompilerParams(
            dimension_semantics=("arbitrary",),
            vmem_limit_bytes=resident + 24 * 1024 * 1024,
        ),
    )(owner_offset, owner, valid, ring_queries, keys, values_t)


def per_device(
    cycle,
    hidden,
    norm_gain,
    router_weight,
    att_experts,
    q_weight,
    kv_weight,
    o_weight,
    kv_cache,
    cached_blocks,
    tail_trim,
    block_pool,
):
    head_count = lax.axis_size("heads")
    seq_rank = lax.axis_index("seq")
    block_size = kv_cache.shape[2]
    local_blocks = kv_cache.shape[1]
    local_heads = q_weight.shape[2] // HD
    scale_q = HD ** (-0.5)
    normed = normalize(hidden[0], norm_gain)
    gathered = shift_all_gather(normed, "heads").reshape(-1, normed.shape[1])
    new_count = gathered.shape[0]
    rows_each = new_count // head_count
    head_rank = lax.axis_index("heads")
    token_ids = (
        ((head_rank + jnp.arange(head_count, dtype=jnp.int32)[:, None]) % head_count) * rows_each
        + jnp.arange(rows_each, dtype=jnp.int32)[None, :]
    ).reshape(new_count)
    chosen = jnp.take(att_experts[0], token_ids, axis=0)
    cached_len = cached_blocks * block_size - tail_trim
    positions = cached_len[seq_rank] + token_ids
    onehot, gates = route(gathered, router_weight, chosen)
    every_q = jnp.einsum("nd,edc->nec", gathered, q_weight, preferred_element_type=jnp.float32)
    chosen_q = jnp.sum(onehot[:, :, :, None] * every_q[:, None, :, :], axis=2).reshape(
        new_count, 2, local_heads, HD
    )
    queries = rotate(chosen_q, positions).astype(jnp.bfloat16)
    fresh = jnp.einsum("nd,sdc->snc", gathered, kv_weight, preferred_element_type=jnp.float32)
    new_keys = rotate(fresh[0].reshape(new_count, local_heads, HD), positions).astype(jnp.bfloat16)
    new_values = fresh[1].reshape(new_count, local_heads, HD).astype(jnp.bfloat16)
    ring_queries = ring_all_gather(
        queries.reshape(new_count * 2, local_heads * HD), "seq", cycle
    )
    request_count = ring_queries.shape[0]
    ring_size = len(cycle)
    position_of = np.argsort(np.asarray(cycle))
    position = jnp.asarray(position_of, dtype=jnp.int32)[seq_rank]
    pool_size = block_pool.shape[0]

    global_ids = seq_rank * local_blocks + jnp.arange(local_blocks, dtype=jnp.int32)
    matches = block_pool[None, :] == global_ids[:, None]
    slot_of = jnp.sum(
        jnp.where(matches, jnp.arange(pool_size, dtype=jnp.int32)[None, :], 0), axis=1
    )
    starts = jnp.cumsum(cached_blocks) - cached_blocks
    owner = jnp.sum((starts[None, :] <= slot_of[:, None]).astype(jnp.int32), axis=1) - 1
    ordinal = slot_of - starts[owner]
    owns = owner[None, :] == jnp.arange(request_count, dtype=jnp.int32)[:, None]

    self_scores = (
        jnp.einsum("nkhc,thc->hnkt", queries, new_keys, preferred_element_type=jnp.float32)
        * scale_q
    )
    causal = token_ids[None, :] <= token_ids[:, None]
    self_scores = jnp.where(causal[None, :, None, :], self_scores, NEG_FILL)
    self_best = jnp.max(self_scores, axis=-1)
    self_weights = jnp.exp(self_scores - self_best[..., None])
    self_total = jnp.sum(self_weights, axis=-1)
    self_accum = jnp.einsum(
        "hnkt,thc->hnkc",
        self_weights.astype(jnp.bfloat16),
        new_values,
        preferred_element_type=jnp.float32,
    )
    ring_queries, self_best, self_total, self_accum = lax.optimization_barrier(
        (ring_queries, self_best, self_total, self_accum)
    )
    owner_offset = (jnp.asarray(position_of, dtype=jnp.int32)[owner] - position) % ring_size
    valid = jnp.clip(cached_len[owner] - ordinal * block_size, 0, block_size).astype(jnp.int32)
    query_rows = new_count * 2
    request_best, totals, accum = block_attention(
        ring_queries,
        kv_cache[0],
        jnp.swapaxes(kv_cache[1], 1, 2),
        owner_offset,
        owner,
        valid,
        request_count,
    )
    request_best = request_best[:, :, 0]
    best_hi, best_lo = split_bf16(request_best)
    request_ref = best_hi + best_lo
    present = request_best > 0.5 * NEG_FILL
    adjust = jnp.exp(jnp.where(present, request_best - request_ref, 0.0))
    totals = totals[:, :, 0] * adjust
    accum = accum * adjust[:, :, None, :]
    totals_hi, totals_lo = split_bf16(totals)
    stats = jnp.stack([best_hi, best_lo, totals_hi, totals_lo], axis=1).astype(jnp.bfloat16)
    payload = jnp.concatenate(
        [
            accum.astype(jnp.bfloat16).reshape(request_count, -1, query_rows),
            stats.reshape(request_count, -1, query_rows),
        ],
        axis=1,
    )
    received = lax.all_to_all(payload, "seq", 0, 0, tiled=True)
    acc_rows = local_heads * HD
    sources = received.shape[0]
    part_accum = received[:, :acc_rows].astype(jnp.float32).reshape(
        sources, local_heads, HD, query_rows
    )
    part_stats = received[:, acc_rows:].astype(jnp.float32).reshape(
        sources, 4, local_heads, query_rows
    )
    part_best = part_stats[:, 0] + part_stats[:, 1]
    part_totals = part_stats[:, 2] + part_stats[:, 3]
    cache_best = jnp.max(part_best, axis=0)
    share = jnp.exp(part_best - cache_best[None])
    cache_total = jnp.sum(part_totals * share, axis=0).reshape(local_heads, new_count, 2)
    cache_accum = jnp.transpose(
        jnp.sum(part_accum * share[:, :, None, :], axis=0), (0, 2, 1)
    ).reshape(local_heads, new_count, 2, HD)
    cache_best = cache_best.reshape(local_heads, new_count, 2)

    peak = jnp.maximum(cache_best, self_best)
    cache_share = jnp.exp(cache_best - peak)
    self_share = jnp.exp(self_best - peak)
    numerator = cache_accum * cache_share[..., None] + self_accum * self_share[..., None]
    denominator = cache_total * cache_share + self_total * self_share
    attended = (
        jnp.transpose((numerator / denominator[..., None]).astype(jnp.bfloat16), (1, 2, 0, 3))
        .reshape(new_count, 2, local_heads * HD)
    )
    output_blocks = []
    for block in list(range(1, head_count)) + [0]:
        rows = slice(block * rows_each, (block + 1) * rows_each)
        block_out = jnp.zeros((rows_each, o_weight.shape[2]), jnp.float32)
        for expert in range(o_weight.shape[0]):
            weight_expert = jnp.sum(onehot[rows, :, expert] * gates[rows], axis=1)
            picked = jnp.where(
                chosen[rows, 0:1] == expert,
                attended[rows, 0],
                jnp.where(
                    chosen[rows, 1:2] == expert, attended[rows, 1], jnp.zeros_like(attended[rows, 0])
                ),
            )
            block_out = block_out + weight_expert[:, None] * jnp.dot(
                picked, o_weight[expert], preferred_element_type=jnp.float32
            )
        block_out = block_out.astype(jnp.bfloat16)
        block_out, attended = lax.optimization_barrier((block_out, attended))
        output_blocks.append(block_out)
    summed = shift_reduce_scatter(output_blocks[-1:] + output_blocks[:-1], "heads")
    return summed[None].astype(jnp.bfloat16)


def solution(mesh):
    return jax.shard_map(
        functools.partial(per_device, tuple(seq_cycle(mesh))),
        mesh=mesh,
        in_specs=(
            P("seq", "heads", None),
            P(),
            P(),
            P("seq", None, None),
            P(None, None, "heads"),
            P(None, None, "heads"),
            P(None, "heads", None),
            P(None, "seq", None, "heads"),
            P(),
            P(),
            P(),
        ),
        out_specs=P("seq", "heads", None),
        check_vma=False,
    )
```

```python
import functools

import numpy as np
import jax
import jax.numpy as jnp
from jax import lax
from jax.experimental import pallas as pl
from jax.experimental.pallas import tpu as pltpu
from jax.sharding import PartitionSpec as P

HD = 128


NEG_FILL = -1e30


def rotate(values, positions):
    half_dim = values.shape[-1] // 2
    inverse = 10000.0 ** (-2.0 * jnp.arange(half_dim, dtype=jnp.float32) / values.shape[-1])
    angles = positions.astype(jnp.float32)[:, None] * inverse[None, :]
    target = (values.shape[0],) + (1,) * (values.ndim - 2) + (half_dim,)
    cosine = jnp.cos(angles).reshape(target)
    sine_part = jnp.sin(angles).reshape(target)
    leading_part = values[..., :half_dim]
    trailing_part = values[..., half_dim:]
    return jnp.concatenate(
        [
            leading_part * cosine - trailing_part * sine_part,
            trailing_part * cosine + leading_part * sine_part,
        ],
        axis=-1,
    )


def normalize(rows, norm_gain):
    wide_rows = rows.astype(jnp.float32)
    scaled = wide_rows * lax.rsqrt(jnp.mean(wide_rows * wide_rows, axis=-1, keepdims=True) + 1e-05)
    return (scaled * norm_gain.astype(jnp.float32)).astype(jnp.bfloat16)


def route(normed, router_weight, chosen):
    logits = jnp.dot(normed, router_weight, preferred_element_type=jnp.float32)
    experts_all = router_weight.shape[1]
    onehot = (chosen[:, :, None] == jnp.arange(experts_all, dtype=jnp.int32)[None, None, :]).astype(
        jnp.float32
    )
    picked = jnp.sum(onehot * logits[:, None, :], axis=-1)
    return (onehot, jax.nn.softmax(picked, axis=-1))


def split_bf16(x):
    hi = lax.reduce_precision(x, exponent_bits=8, mantissa_bits=7)
    lo = lax.reduce_precision(x - hi, exponent_bits=8, mantissa_bits=7)
    return hi, lo


def seq_cycle(mesh):
    size = mesh.shape["seq"]
    plain = list(range(size))
    try:
        devices = np.moveaxis(np.asarray(mesh.devices), mesh.axis_names.index("seq"), -1)
        line = devices.reshape(-1, size)[0]
        coords = np.array([list(d.coords) for d in line])
    except Exception:
        return plain
    varying = [k for k in range(coords.shape[1]) if len(set(coords[:, k])) > 1]
    if len(varying) == 1:
        order = sorted(plain, key=lambda j: coords[j, varying[0]])
        return order[0::2] + order[1::2][::-1]
    if len(varying) != 2:
        return plain
    dim_a, dim_b = varying
    values_a = sorted(set(coords[:, dim_a]))
    values_b = sorted(set(coords[:, dim_b]))
    if len(values_a) % 2:
        dim_a, dim_b, values_a, values_b = dim_b, dim_a, values_b, values_a
    if len(values_a) % 2 or len(values_a) * len(values_b) != size:
        return plain
    at = {(coords[j, dim_a], coords[j, dim_b]): j for j in plain}
    cycle = [at[(a, values_b[0])] for a in values_a]
    for row, a in enumerate(reversed(values_a)):
        columns = values_b[1:] if row % 2 == 0 else values_b[1:][::-1]
        cycle += [at[(a, b)] for b in columns]
    if sorted(cycle) != plain:
        return plain
    return cycle


def shift_all_gather(piece, axis_name):
    size = lax.axis_size(axis_name)
    rank = lax.axis_index(axis_name)
    by_offset = [piece] + [
        lax.ppermute(piece, axis_name, [(i, (i + s) % size) for i in range(size)])
        for s in range(1, size)
    ]
    return jnp.stack(by_offset[:1] + by_offset[1:][::-1], axis=0)


def shift_reduce_scatter(blocks, axis_name):
    size = lax.axis_size(axis_name)
    total = blocks[0].astype(jnp.float32)
    for s in range(1, size):
        moved = lax.ppermute(blocks[s], axis_name, [(i, (i + s) % size) for i in range(size)])
        total = total + moved.astype(jnp.float32)
    return total


def ring_all_gather(piece, axis_name, cycle):
    size = len(cycle)
    forward = [(cycle[i], cycle[(i + 1) % size]) for i in range(size)]
    backward = [(cycle[(i + 1) % size], cycle[i]) for i in range(size)]
    ahead = size // 2
    behind = size - 1 - ahead
    from_behind, from_ahead = [], []
    moving = piece
    for _ in range(ahead):
        moving = lax.ppermute(moving, axis_name, forward)
        from_behind.append(moving)
    moving = piece
    for _ in range(behind):
        moving = lax.ppermute(moving, axis_name, backward)
        from_ahead.append(moving)
    return jnp.stack([piece] + from_ahead + from_behind[::-1], axis=0)


def block_attention(ring_queries, keys, values_t, owner_offset, owner, valid, requests):
    blocks, block_size, width = keys.shape
    query_rows = ring_queries.shape[1]
    heads = width // HD
    scale = HD ** (-0.5)

    def kernel(offset_ref, owner_ref, valid_ref, q_ref, k_ref, v_ref, best_ref, total_ref, accum_ref):
        b = pl.program_id(0)

        @pl.when(b == 0)
        def _():
            best_ref[...] = jnp.full(best_ref.shape, NEG_FILL, jnp.float32)
            total_ref[...] = jnp.zeros(total_ref.shape, jnp.float32)
            accum_ref[...] = jnp.zeros(accum_ref.shape, jnp.float32)

        request = owner_ref[b]
        limit = valid_ref[b]
        row = lax.broadcasted_iota(jnp.int32, (block_size, query_rows), 0)
        for h in range(heads):
            q = q_ref[0, :, h * HD:(h + 1) * HD]
            k = k_ref[0, :, h * HD:(h + 1) * HD]
            scores = lax.dot_general(
                k, q, (((1,), (1,)), ((), ())), preferred_element_type=jnp.float32
            ) * scale
            scores = jnp.where(row < limit, scores, NEG_FILL)
            old_best = best_ref[request, h]
            new_best = jnp.maximum(old_best, jnp.max(scores, axis=0, keepdims=True))
            rescale = jnp.exp(old_best - new_best)
            weights = jnp.exp(scores - new_best)
            best_ref[request, h] = new_best
            total_ref[request, h] = total_ref[request, h] * rescale + jnp.sum(
                weights, axis=0, keepdims=True
            )
            v_t = v_ref[0, h * HD:(h + 1) * HD, :]
            accum_ref[request, h] = accum_ref[request, h] * rescale + jnp.dot(
                v_t, weights.astype(jnp.bfloat16), preferred_element_type=jnp.float32
            )

    grid_spec = pltpu.PrefetchScalarGridSpec(
        num_scalar_prefetch=3,
        grid=(blocks,),
        in_specs=[
            pl.BlockSpec((1, query_rows, width), lambda b, off, own, val: (off[b], 0, 0)),
            pl.BlockSpec((1, block_size, width), lambda b, off, own, val: (b, 0, 0)),
            pl.BlockSpec((1, width, block_size), lambda b, off, own, val: (b, 0, 0)),
        ],
        out_specs=[
            pl.BlockSpec((requests, heads, 1, query_rows), lambda b, off, own, val: (0, 0, 0, 0)),
            pl.BlockSpec((requests, heads, 1, query_rows), lambda b, off, own, val: (0, 0, 0, 0)),
            pl.BlockSpec((requests, heads, HD, query_rows), lambda b, off, own, val: (0, 0, 0, 0)),
        ],
    )
    resident = 2 * requests * heads * (HD + 16) * query_rows * 4
    return pl.pallas_call(
        kernel,
        grid_spec=grid_spec,
        out_shape=[
            jax.ShapeDtypeStruct((requests, heads, 1, query_rows), jnp.float32),
            jax.ShapeDtypeStruct((requests, heads, 1, query_rows), jnp.float32),
            jax.ShapeDtypeStruct((requests, heads, HD, query_rows), jnp.float32),
        ],
        compiler_params=pltpu.CompilerParams(
            dimension_semantics=("arbitrary",),
            vmem_limit_bytes=resident + 24 * 1024 * 1024,
        ),
    )(owner_offset, owner, valid, ring_queries, keys, values_t)


def per_device(
    cycle,
    hidden,
    norm_gain,
    router_weight,
    att_experts,
    q_weight,
    kv_weight,
    o_weight,
    kv_cache,
    cached_blocks,
    tail_trim,
    block_pool,
):
    head_count = lax.axis_size("heads")
    seq_rank = lax.axis_index("seq")
    block_size = kv_cache.shape[2]
    local_blocks = kv_cache.shape[1]
    local_heads = q_weight.shape[2] // HD
    scale_q = HD ** (-0.5)
    normed = normalize(hidden[0], norm_gain)
    gathered = shift_all_gather(normed, "heads").reshape(-1, normed.shape[1])
    new_count = gathered.shape[0]
    rows_each = new_count // head_count
    head_rank = lax.axis_index("heads")
    token_ids = (
        ((head_rank + jnp.arange(head_count, dtype=jnp.int32)[:, None]) % head_count) * rows_each
        + jnp.arange(rows_each, dtype=jnp.int32)[None, :]
    ).reshape(new_count)
    chosen = jnp.take(att_experts[0], token_ids, axis=0)
    cached_len = cached_blocks * block_size - tail_trim
    positions = cached_len[seq_rank] + token_ids
    onehot, gates = route(gathered, router_weight, chosen)
    every_q = jnp.einsum("nd,edc->nec", gathered, q_weight, preferred_element_type=jnp.float32)
    chosen_q = jnp.sum(onehot[:, :, :, None] * every_q[:, None, :, :], axis=2).reshape(
        new_count, 2, local_heads, HD
    )
    queries = rotate(chosen_q, positions).astype(jnp.bfloat16)
    fresh = jnp.einsum("nd,sdc->snc", gathered, kv_weight, preferred_element_type=jnp.float32)
    new_keys = rotate(fresh[0].reshape(new_count, local_heads, HD), positions).astype(jnp.bfloat16)
    new_values = fresh[1].reshape(new_count, local_heads, HD).astype(jnp.bfloat16)
    query_table = queries.reshape(new_count * 2, local_heads * HD)
    ring_by_head = [
        ring_all_gather(query_table[:, h * HD:(h + 1) * HD], "seq", cycle)
        for h in range(local_heads)
    ]
    request_count = ring_by_head[0].shape[0]
    ring_size = len(cycle)
    position_of = np.argsort(np.asarray(cycle))
    position = jnp.asarray(position_of, dtype=jnp.int32)[seq_rank]
    pool_size = block_pool.shape[0]

    global_ids = seq_rank * local_blocks + jnp.arange(local_blocks, dtype=jnp.int32)
    matches = block_pool[None, :] == global_ids[:, None]
    slot_of = jnp.sum(
        jnp.where(matches, jnp.arange(pool_size, dtype=jnp.int32)[None, :], 0), axis=1
    )
    starts = jnp.cumsum(cached_blocks) - cached_blocks
    owner = jnp.sum((starts[None, :] <= slot_of[:, None]).astype(jnp.int32), axis=1) - 1
    ordinal = slot_of - starts[owner]
    owns = owner[None, :] == jnp.arange(request_count, dtype=jnp.int32)[:, None]

    self_scores = (
        jnp.einsum("nkhc,thc->hnkt", queries, new_keys, preferred_element_type=jnp.float32)
        * scale_q
    )
    causal = token_ids[None, :] <= token_ids[:, None]
    self_scores = jnp.where(causal[None, :, None, :], self_scores, NEG_FILL)
    self_best = jnp.max(self_scores, axis=-1)
    self_weights = jnp.exp(self_scores - self_best[..., None])
    self_total = jnp.sum(self_weights, axis=-1)
    self_accum = jnp.einsum(
        "hnkt,thc->hnkc",
        self_weights.astype(jnp.bfloat16),
        new_values,
        preferred_element_type=jnp.float32,
    )
    first_ring, self_best, self_total, self_accum = lax.optimization_barrier(
        (ring_by_head[0], self_best, self_total, self_accum)
    )
    ring_by_head = [first_ring] + ring_by_head[1:]
    owner_offset = (jnp.asarray(position_of, dtype=jnp.int32)[owner] - position) % ring_size
    valid = jnp.clip(cached_len[owner] - ordinal * block_size, 0, block_size).astype(jnp.int32)
    query_rows = new_count * 2
    values_t = jnp.swapaxes(kv_cache[1], 1, 2)

    def head_payload(head, head_queries):
        request_best, totals, accum = block_attention(
            head_queries,
            kv_cache[0][:, :, head * HD:(head + 1) * HD],
            values_t[:, head * HD:(head + 1) * HD],
            owner_offset,
            owner,
            valid,
            request_count,
        )
        request_best = request_best[:, :, 0]
        best_hi, best_lo = split_bf16(request_best)
        request_ref = best_hi + best_lo
        present = request_best > 0.5 * NEG_FILL
        adjust = jnp.exp(jnp.where(present, request_best - request_ref, 0.0))
        totals = totals[:, :, 0] * adjust
        accum = accum * adjust[:, :, None, :]
        totals_hi, totals_lo = split_bf16(totals)
        stats = jnp.stack([best_hi, best_lo, totals_hi, totals_lo], axis=1).astype(jnp.bfloat16)
        return jnp.concatenate(
            [
                accum.astype(jnp.bfloat16).reshape(request_count, -1, query_rows),
                stats.reshape(request_count, -1, query_rows),
            ],
            axis=1,
        )

    def head_parts(received):
        sources = received.shape[0]
        part_accum = received[:, :HD].astype(jnp.float32)
        part_stats = received[:, HD:].astype(jnp.float32).reshape(sources, 4, query_rows)
        part_best = part_stats[:, 0] + part_stats[:, 1]
        part_totals = part_stats[:, 2] + part_stats[:, 3]
        best = jnp.max(part_best, axis=0)
        share = jnp.exp(part_best - best[None])
        total = jnp.sum(part_totals * share, axis=0)
        accum = jnp.sum(part_accum * share[:, None, :], axis=0)
        return best, total, accum

    head_results = []
    pending = ring_by_head
    for head in range(local_heads):
        payload = head_payload(head, pending[head])
        if head + 1 < local_heads:
            payload, next_queries = lax.optimization_barrier((payload, pending[head + 1]))
            pending = pending[: head + 1] + [next_queries] + pending[head + 2:]
        received = lax.all_to_all(payload, "seq", 0, 0, tiled=True)
        head_results.append(head_parts(received))
    cache_best = jnp.stack([r[0] for r in head_results]).reshape(local_heads, new_count, 2)
    cache_total = jnp.stack([r[1] for r in head_results]).reshape(local_heads, new_count, 2)
    cache_accum = jnp.transpose(jnp.stack([r[2] for r in head_results]), (0, 2, 1)).reshape(
        local_heads, new_count, 2, HD
    )

    peak = jnp.maximum(cache_best, self_best)
    cache_share = jnp.exp(cache_best - peak)
    self_share = jnp.exp(self_best - peak)
    numerator = cache_accum * cache_share[..., None] + self_accum * self_share[..., None]
    denominator = cache_total * cache_share + self_total * self_share
    attended = (
        jnp.transpose((numerator / denominator[..., None]).astype(jnp.bfloat16), (1, 2, 0, 3))
        .reshape(new_count, 2, local_heads * HD)
    )
    output_blocks = []
    for block in list(range(1, head_count)) + [0]:
        rows = slice(block * rows_each, (block + 1) * rows_each)
        block_out = jnp.zeros((rows_each, o_weight.shape[2]), jnp.float32)
        for expert in range(o_weight.shape[0]):
            weight_expert = jnp.sum(onehot[rows, :, expert] * gates[rows], axis=1)
            picked = jnp.where(
                chosen[rows, 0:1] == expert,
                attended[rows, 0],
                jnp.where(
                    chosen[rows, 1:2] == expert, attended[rows, 1], jnp.zeros_like(attended[rows, 0])
                ),
            )
            block_out = block_out + weight_expert[:, None] * jnp.dot(
                picked, o_weight[expert], preferred_element_type=jnp.float32
            )
        block_out = block_out.astype(jnp.bfloat16)
        block_out, attended = lax.optimization_barrier((block_out, attended))
        output_blocks.append(block_out)
    summed = shift_reduce_scatter(output_blocks[-1:] + output_blocks[:-1], "heads")
    return summed[None].astype(jnp.bfloat16)


def solution(mesh):
    return jax.shard_map(
        functools.partial(per_device, tuple(seq_cycle(mesh))),
        mesh=mesh,
        in_specs=(
            P("seq", "heads", None),
            P(),
            P(),
            P("seq", None, None),
            P(None, None, "heads"),
            P(None, None, "heads"),
            P(None, "heads", None),
            P(None, "seq", None, "heads"),
            P(),
            P(),
            P(),
        ),
        out_specs=P("seq", "heads", None),
        check_vma=False,
    )
```

```python
import functools

import numpy as np
import jax
import jax.numpy as jnp
from jax import lax
from jax.experimental import pallas as pl
from jax.experimental.pallas import tpu as pltpu
from jax.sharding import PartitionSpec as P

HD = 128


NEG_FILL = -1e30


def rotate(values, positions):
    half_dim = values.shape[-1] // 2
    inverse = 10000.0 ** (-2.0 * jnp.arange(half_dim, dtype=jnp.float32) / values.shape[-1])
    angles = positions.astype(jnp.float32)[:, None] * inverse[None, :]
    target = (values.shape[0],) + (1,) * (values.ndim - 2) + (half_dim,)
    cosine = jnp.cos(angles).reshape(target)
    sine_part = jnp.sin(angles).reshape(target)
    leading_part = values[..., :half_dim]
    trailing_part = values[..., half_dim:]
    return jnp.concatenate(
        [
            leading_part * cosine - trailing_part * sine_part,
            trailing_part * cosine + leading_part * sine_part,
        ],
        axis=-1,
    )


def normalize(rows, norm_gain):
    wide_rows = rows.astype(jnp.float32)
    scaled = wide_rows * lax.rsqrt(jnp.mean(wide_rows * wide_rows, axis=-1, keepdims=True) + 1e-05)
    return (scaled * norm_gain.astype(jnp.float32)).astype(jnp.bfloat16)


def route(normed, router_weight, chosen):
    logits = jnp.dot(normed, router_weight, preferred_element_type=jnp.float32)
    experts_all = router_weight.shape[1]
    onehot = (chosen[:, :, None] == jnp.arange(experts_all, dtype=jnp.int32)[None, None, :]).astype(
        jnp.float32
    )
    picked = jnp.sum(onehot * logits[:, None, :], axis=-1)
    return (onehot, jax.nn.softmax(picked, axis=-1))


def split_bf16(x):
    hi = lax.reduce_precision(x, exponent_bits=8, mantissa_bits=7)
    lo = lax.reduce_precision(x - hi, exponent_bits=8, mantissa_bits=7)
    return hi, lo


def seq_cycle(mesh):
    size = mesh.shape["seq"]
    plain = list(range(size))
    try:
        devices = np.moveaxis(np.asarray(mesh.devices), mesh.axis_names.index("seq"), -1)
        line = devices.reshape(-1, size)[0]
        coords = np.array([list(d.coords) for d in line])
    except Exception:
        return plain
    varying = [k for k in range(coords.shape[1]) if len(set(coords[:, k])) > 1]
    if len(varying) == 1:
        order = sorted(plain, key=lambda j: coords[j, varying[0]])
        return order[0::2] + order[1::2][::-1]
    if len(varying) != 2:
        return plain
    dim_a, dim_b = varying
    values_a = sorted(set(coords[:, dim_a]))
    values_b = sorted(set(coords[:, dim_b]))
    if len(values_a) % 2:
        dim_a, dim_b, values_a, values_b = dim_b, dim_a, values_b, values_a
    if len(values_a) % 2 or len(values_a) * len(values_b) != size:
        return plain
    at = {(coords[j, dim_a], coords[j, dim_b]): j for j in plain}
    cycle = [at[(a, values_b[0])] for a in values_a]
    for row, a in enumerate(reversed(values_a)):
        columns = values_b[1:] if row % 2 == 0 else values_b[1:][::-1]
        cycle += [at[(a, b)] for b in columns]
    if sorted(cycle) != plain:
        return plain
    return cycle


def shift_all_gather(piece, axis_name):
    size = lax.axis_size(axis_name)
    rank = lax.axis_index(axis_name)
    copies = jnp.broadcast_to(piece[None], (size,) + piece.shape)
    everyone = lax.all_to_all(copies, axis_name, 0, 0, tiled=True)
    return jnp.take(everyone, (rank + jnp.arange(size, dtype=jnp.int32)) % size, axis=0)


def shift_reduce_scatter(blocks, axis_name):
    size = lax.axis_size(axis_name)
    total = blocks[0].astype(jnp.float32)
    for s in range(1, size):
        moved = lax.ppermute(blocks[s], axis_name, [(i, (i + s) % size) for i in range(size)])
        total = total + moved.astype(jnp.float32)
    return total


def ring_all_gather(piece, axis_name, cycle):
    size = len(cycle)
    forward = [(cycle[i], cycle[(i + 1) % size]) for i in range(size)]
    backward = [(cycle[(i + 1) % size], cycle[i]) for i in range(size)]
    ahead = size // 2
    behind = size - 1 - ahead
    from_behind, from_ahead = [], []
    moving = piece
    for _ in range(ahead):
        moving = lax.ppermute(moving, axis_name, forward)
        from_behind.append(moving)
    moving = piece
    for _ in range(behind):
        moving = lax.ppermute(moving, axis_name, backward)
        from_ahead.append(moving)
    return jnp.stack([piece] + from_ahead + from_behind[::-1], axis=0)


def block_attention(ring_queries, keys, values_t, owner_offset, owner, valid, requests):
    blocks, block_size, width = keys.shape
    query_rows = ring_queries.shape[1]
    heads = width // HD
    scale = HD ** (-0.5)

    def kernel(offset_ref, owner_ref, valid_ref, q_ref, k_ref, v_ref, best_ref, total_ref, accum_ref):
        b = pl.program_id(0)

        @pl.when(b == 0)
        def _():
            best_ref[...] = jnp.full(best_ref.shape, NEG_FILL, jnp.float32)
            total_ref[...] = jnp.zeros(total_ref.shape, jnp.float32)
            accum_ref[...] = jnp.zeros(accum_ref.shape, jnp.float32)

        request = owner_ref[b]
        limit = valid_ref[b]
        row = lax.broadcasted_iota(jnp.int32, (block_size, query_rows), 0)
        for h in range(heads):
            q = q_ref[0, :, h * HD:(h + 1) * HD]
            k = k_ref[0, :, h * HD:(h + 1) * HD]
            scores = lax.dot_general(
                k, q, (((1,), (1,)), ((), ())), preferred_element_type=jnp.float32
            ) * scale
            scores = jnp.where(row < limit, scores, NEG_FILL)
            old_best = best_ref[request, h]
            new_best = jnp.maximum(old_best, jnp.max(scores, axis=0, keepdims=True))
            rescale = jnp.exp(old_best - new_best)
            weights = jnp.exp(scores - new_best)
            best_ref[request, h] = new_best
            total_ref[request, h] = total_ref[request, h] * rescale + jnp.sum(
                weights, axis=0, keepdims=True
            )
            v_t = v_ref[0, h * HD:(h + 1) * HD, :]
            accum_ref[request, h] = accum_ref[request, h] * rescale + jnp.dot(
                v_t, weights.astype(jnp.bfloat16), preferred_element_type=jnp.float32
            )

    grid_spec = pltpu.PrefetchScalarGridSpec(
        num_scalar_prefetch=3,
        grid=(blocks,),
        in_specs=[
            pl.BlockSpec((1, query_rows, width), lambda b, off, own, val: (off[b], 0, 0)),
            pl.BlockSpec((1, block_size, width), lambda b, off, own, val: (b, 0, 0)),
            pl.BlockSpec((1, width, block_size), lambda b, off, own, val: (b, 0, 0)),
        ],
        out_specs=[
            pl.BlockSpec((requests, heads, 1, query_rows), lambda b, off, own, val: (0, 0, 0, 0)),
            pl.BlockSpec((requests, heads, 1, query_rows), lambda b, off, own, val: (0, 0, 0, 0)),
            pl.BlockSpec((requests, heads, HD, query_rows), lambda b, off, own, val: (0, 0, 0, 0)),
        ],
    )
    resident = 2 * requests * heads * (HD + 16) * query_rows * 4
    return pl.pallas_call(
        kernel,
        grid_spec=grid_spec,
        out_shape=[
            jax.ShapeDtypeStruct((requests, heads, 1, query_rows), jnp.float32),
            jax.ShapeDtypeStruct((requests, heads, 1, query_rows), jnp.float32),
            jax.ShapeDtypeStruct((requests, heads, HD, query_rows), jnp.float32),
        ],
        compiler_params=pltpu.CompilerParams(
            dimension_semantics=("arbitrary",),
            vmem_limit_bytes=resident + 24 * 1024 * 1024,
        ),
    )(owner_offset, owner, valid, ring_queries, keys, values_t)


def per_device(
    cycle,
    hidden,
    norm_gain,
    router_weight,
    att_experts,
    q_weight,
    kv_weight,
    o_weight,
    kv_cache,
    cached_blocks,
    tail_trim,
    block_pool,
):
    head_count = lax.axis_size("heads")
    seq_rank = lax.axis_index("seq")
    block_size = kv_cache.shape[2]
    local_blocks = kv_cache.shape[1]
    local_heads = q_weight.shape[2] // HD
    scale_q = HD ** (-0.5)
    normed = normalize(hidden[0], norm_gain)
    gathered = shift_all_gather(normed, "heads").reshape(-1, normed.shape[1])
    new_count = gathered.shape[0]
    rows_each = new_count // head_count
    head_rank = lax.axis_index("heads")
    token_ids = (
        ((head_rank + jnp.arange(head_count, dtype=jnp.int32)[:, None]) % head_count) * rows_each
        + jnp.arange(rows_each, dtype=jnp.int32)[None, :]
    ).reshape(new_count)
    chosen = jnp.take(att_experts[0], token_ids, axis=0)
    cached_len = cached_blocks * block_size - tail_trim
    positions = cached_len[seq_rank] + token_ids
    onehot, gates = route(gathered, router_weight, chosen)
    every_q = jnp.einsum("nd,edc->nec", gathered, q_weight, preferred_element_type=jnp.float32)
    chosen_q = jnp.sum(onehot[:, :, :, None] * every_q[:, None, :, :], axis=2).reshape(
        new_count, 2, local_heads, HD
    )
    queries = rotate(chosen_q, positions).astype(jnp.bfloat16)
    fresh = jnp.einsum("nd,sdc->snc", gathered, kv_weight, preferred_element_type=jnp.float32)
    new_keys = rotate(fresh[0].reshape(new_count, local_heads, HD), positions).astype(jnp.bfloat16)
    new_values = fresh[1].reshape(new_count, local_heads, HD).astype(jnp.bfloat16)
    ring_queries = ring_all_gather(
        queries.reshape(new_count * 2, local_heads * HD), "seq", cycle
    )
    request_count = ring_queries.shape[0]
    ring_size = len(cycle)
    position_of = np.argsort(np.asarray(cycle))
    position = jnp.asarray(position_of, dtype=jnp.int32)[seq_rank]
    pool_size = block_pool.shape[0]

    global_ids = seq_rank * local_blocks + jnp.arange(local_blocks, dtype=jnp.int32)
    matches = block_pool[None, :] == global_ids[:, None]
    slot_of = jnp.sum(
        jnp.where(matches, jnp.arange(pool_size, dtype=jnp.int32)[None, :], 0), axis=1
    )
    starts = jnp.cumsum(cached_blocks) - cached_blocks
    owner = jnp.sum((starts[None, :] <= slot_of[:, None]).astype(jnp.int32), axis=1) - 1
    ordinal = slot_of - starts[owner]
    owns = owner[None, :] == jnp.arange(request_count, dtype=jnp.int32)[:, None]

    self_scores = (
        jnp.einsum("nkhc,thc->hnkt", queries, new_keys, preferred_element_type=jnp.float32)
        * scale_q
    )
    causal = token_ids[None, :] <= token_ids[:, None]
    self_scores = jnp.where(causal[None, :, None, :], self_scores, NEG_FILL)
    self_best = jnp.max(self_scores, axis=-1)
    self_weights = jnp.exp(self_scores - self_best[..., None])
    self_total = jnp.sum(self_weights, axis=-1)
    self_accum = jnp.einsum(
        "hnkt,thc->hnkc",
        self_weights.astype(jnp.bfloat16),
        new_values,
        preferred_element_type=jnp.float32,
    )
    ring_queries, self_best, self_total, self_accum = lax.optimization_barrier(
        (ring_queries, self_best, self_total, self_accum)
    )
    owner_offset = (jnp.asarray(position_of, dtype=jnp.int32)[owner] - position) % ring_size
    valid = jnp.clip(cached_len[owner] - ordinal * block_size, 0, block_size).astype(jnp.int32)
    query_rows = new_count * 2
    request_best, totals, accum = block_attention(
        ring_queries,
        kv_cache[0],
        jnp.swapaxes(kv_cache[1], 1, 2),
        owner_offset,
        owner,
        valid,
        request_count,
    )
    request_best = request_best[:, :, 0]
    best_hi, best_lo = split_bf16(request_best)
    request_ref = best_hi + best_lo
    present = request_best > 0.5 * NEG_FILL
    adjust = jnp.exp(jnp.where(present, request_best - request_ref, 0.0))
    totals = totals[:, :, 0] * adjust
    accum = accum * adjust[:, :, None, :]
    totals_hi, totals_lo = split_bf16(totals)
    stats = jnp.stack([best_hi, best_lo, totals_hi, totals_lo], axis=1).astype(jnp.bfloat16)
    payload = jnp.concatenate(
        [
            accum.astype(jnp.bfloat16).reshape(request_count, -1, query_rows),
            stats.reshape(request_count, -1, query_rows),
        ],
        axis=1,
    )
    received = lax.all_to_all(payload, "seq", 0, 0, tiled=True)
    acc_rows = local_heads * HD
    sources = received.shape[0]
    part_accum = received[:, :acc_rows].astype(jnp.float32).reshape(
        sources, local_heads, HD, query_rows
    )
    part_stats = received[:, acc_rows:].astype(jnp.float32).reshape(
        sources, 4, local_heads, query_rows
    )
    part_best = part_stats[:, 0] + part_stats[:, 1]
    part_totals = part_stats[:, 2] + part_stats[:, 3]
    cache_best = jnp.max(part_best, axis=0)
    share = jnp.exp(part_best - cache_best[None])
    cache_total = jnp.sum(part_totals * share, axis=0).reshape(local_heads, new_count, 2)
    cache_accum = jnp.transpose(
        jnp.sum(part_accum * share[:, :, None, :], axis=0), (0, 2, 1)
    ).reshape(local_heads, new_count, 2, HD)
    cache_best = cache_best.reshape(local_heads, new_count, 2)

    peak = jnp.maximum(cache_best, self_best)
    cache_share = jnp.exp(cache_best - peak)
    self_share = jnp.exp(self_best - peak)
    numerator = cache_accum * cache_share[..., None] + self_accum * self_share[..., None]
    denominator = cache_total * cache_share + self_total * self_share
    attended = (
        jnp.transpose((numerator / denominator[..., None]).astype(jnp.bfloat16), (1, 2, 0, 3))
        .reshape(new_count, 2, local_heads * HD)
    )
    output_blocks = []
    for block in list(range(1, head_count)) + [0]:
        rows = slice(block * rows_each, (block + 1) * rows_each)
        block_out = jnp.zeros((rows_each, o_weight.shape[2]), jnp.float32)
        for expert in range(o_weight.shape[0]):
            weight_expert = jnp.sum(onehot[rows, :, expert] * gates[rows], axis=1)
            picked = jnp.where(
                chosen[rows, 0:1] == expert,
                attended[rows, 0],
                jnp.where(
                    chosen[rows, 1:2] == expert, attended[rows, 1], jnp.zeros_like(attended[rows, 0])
                ),
            )
            block_out = block_out + weight_expert[:, None] * jnp.dot(
                picked, o_weight[expert], preferred_element_type=jnp.float32
            )
        block_out = block_out.astype(jnp.bfloat16)
        block_out, attended = lax.optimization_barrier((block_out, attended))
        output_blocks.append(block_out)
    summed = shift_reduce_scatter(output_blocks[-1:] + output_blocks[:-1], "heads")
    return summed[None].astype(jnp.bfloat16)


def solution(mesh):
    return jax.shard_map(
        functools.partial(per_device, tuple(seq_cycle(mesh))),
        mesh=mesh,
        in_specs=(
            P("seq", "heads", None),
            P(),
            P(),
            P("seq", None, None),
            P(None, None, "heads"),
            P(None, None, "heads"),
            P(None, "heads", None),
            P(None, "seq", None, "heads"),
            P(),
            P(),
            P(),
        ),
        out_specs=P("seq", "heads", None),
        check_vma=False,
    )
```

```python
import functools

import numpy as np
import jax
import jax.numpy as jnp
from jax import lax
from jax.experimental import pallas as pl
from jax.experimental.pallas import tpu as pltpu
from jax.sharding import PartitionSpec as P

HD = 128


NEG_FILL = -1e30


def rotate(values, positions):
    half_dim = values.shape[-1] // 2
    inverse = 10000.0 ** (-2.0 * jnp.arange(half_dim, dtype=jnp.float32) / values.shape[-1])
    angles = positions.astype(jnp.float32)[:, None] * inverse[None, :]
    target = (values.shape[0],) + (1,) * (values.ndim - 2) + (half_dim,)
    cosine = jnp.cos(angles).reshape(target)
    sine_part = jnp.sin(angles).reshape(target)
    leading_part = values[..., :half_dim]
    trailing_part = values[..., half_dim:]
    return jnp.concatenate(
        [
            leading_part * cosine - trailing_part * sine_part,
            trailing_part * cosine + leading_part * sine_part,
        ],
        axis=-1,
    )


def normalize(rows, norm_gain):
    wide_rows = rows.astype(jnp.float32)
    scaled = wide_rows * lax.rsqrt(jnp.mean(wide_rows * wide_rows, axis=-1, keepdims=True) + 1e-05)
    return (scaled * norm_gain.astype(jnp.float32)).astype(jnp.bfloat16)


def route(normed, router_weight, chosen):
    logits = jnp.dot(normed, router_weight, preferred_element_type=jnp.float32)
    experts_all = router_weight.shape[1]
    onehot = (chosen[:, :, None] == jnp.arange(experts_all, dtype=jnp.int32)[None, None, :]).astype(
        jnp.float32
    )
    picked = jnp.sum(onehot * logits[:, None, :], axis=-1)
    return (onehot, jax.nn.softmax(picked, axis=-1))


def split_bf16(x):
    hi = lax.reduce_precision(x, exponent_bits=8, mantissa_bits=7)
    lo = lax.reduce_precision(x - hi, exponent_bits=8, mantissa_bits=7)
    return hi, lo


def seq_cycle(mesh):
    size = mesh.shape["seq"]
    plain = list(range(size))
    try:
        devices = np.moveaxis(np.asarray(mesh.devices), mesh.axis_names.index("seq"), -1)
        line = devices.reshape(-1, size)[0]
        coords = np.array([list(d.coords) for d in line])
    except Exception:
        return plain
    varying = [k for k in range(coords.shape[1]) if len(set(coords[:, k])) > 1]
    if len(varying) == 1:
        order = sorted(plain, key=lambda j: coords[j, varying[0]])
        return order[0::2] + order[1::2][::-1]
    if len(varying) != 2:
        return plain
    dim_a, dim_b = varying
    values_a = sorted(set(coords[:, dim_a]))
    values_b = sorted(set(coords[:, dim_b]))
    if len(values_a) % 2:
        dim_a, dim_b, values_a, values_b = dim_b, dim_a, values_b, values_a
    if len(values_a) % 2 or len(values_a) * len(values_b) != size:
        return plain
    at = {(coords[j, dim_a], coords[j, dim_b]): j for j in plain}
    cycle = [at[(a, values_b[0])] for a in values_a]
    for row, a in enumerate(reversed(values_a)):
        columns = values_b[1:] if row % 2 == 0 else values_b[1:][::-1]
        cycle += [at[(a, b)] for b in columns]
    if sorted(cycle) != plain:
        return plain
    return cycle


def shift_all_gather(piece, axis_name):
    size = lax.axis_size(axis_name)
    rank = lax.axis_index(axis_name)
    by_offset = [piece] + [
        lax.ppermute(piece, axis_name, [(i, (i + s) % size) for i in range(size)])
        for s in range(1, size)
    ]
    return jnp.stack(by_offset[:1] + by_offset[1:][::-1], axis=0)


def shift_reduce_scatter(blocks, axis_name):
    size = lax.axis_size(axis_name)
    total = blocks[0].astype(jnp.float32)
    for s in range(1, size):
        moved = lax.ppermute(blocks[s], axis_name, [(i, (i + s) % size) for i in range(size)])
        total = total + moved.astype(jnp.float32)
    return total


def ring_all_gather(piece, axis_name, cycle):
    size = len(cycle)
    forward = [(cycle[i], cycle[(i + 1) % size]) for i in range(size)]
    backward = [(cycle[(i + 1) % size], cycle[i]) for i in range(size)]
    ahead = size // 2
    behind = size - 1 - ahead
    from_behind, from_ahead = [], []
    moving = piece
    for _ in range(ahead):
        moving = lax.ppermute(moving, axis_name, forward)
        from_behind.append(moving)
    moving = piece
    for _ in range(behind):
        moving = lax.ppermute(moving, axis_name, backward)
        from_ahead.append(moving)
    return jnp.stack([piece] + from_ahead + from_behind[::-1], axis=0)


def block_attention(ring_queries, keys, values_t, owner_offset, owner, valid, requests):
    blocks, block_size, width = keys.shape
    query_rows = ring_queries.shape[1]
    heads = width // HD
    scale = HD ** (-0.5)

    def kernel(offset_ref, owner_ref, valid_ref, q_ref, k_ref, v_ref, best_ref, total_ref, accum_ref):
        b = pl.program_id(0)

        @pl.when(b == 0)
        def _():
            best_ref[...] = jnp.full(best_ref.shape, NEG_FILL, jnp.float32)
            total_ref[...] = jnp.zeros(total_ref.shape, jnp.float32)
            accum_ref[...] = jnp.zeros(accum_ref.shape, jnp.float32)

        request = owner_ref[b]
        limit = valid_ref[b]
        row = lax.broadcasted_iota(jnp.int32, (block_size, query_rows), 0)
        for h in range(heads):
            q = q_ref[0, :, h * HD:(h + 1) * HD]
            k = k_ref[0, :, h * HD:(h + 1) * HD]
            scores = lax.dot_general(
                k, q, (((1,), (1,)), ((), ())), preferred_element_type=jnp.float32
            ) * scale
            scores = jnp.where(row < limit, scores, NEG_FILL)
            old_best = best_ref[request, h]
            new_best = jnp.maximum(old_best, jnp.max(scores, axis=0, keepdims=True))
            rescale = jnp.exp(old_best - new_best)
            weights = jnp.exp(scores - new_best)
            best_ref[request, h] = new_best
            total_ref[request, h] = total_ref[request, h] * rescale + jnp.sum(
                weights, axis=0, keepdims=True
            )
            v_t = v_ref[0, h * HD:(h + 1) * HD, :]
            accum_ref[request, h] = accum_ref[request, h] * rescale + jnp.dot(
                v_t, weights.astype(jnp.bfloat16), preferred_element_type=jnp.float32
            )

    grid_spec = pltpu.PrefetchScalarGridSpec(
        num_scalar_prefetch=3,
        grid=(blocks,),
        in_specs=[
            pl.BlockSpec((1, query_rows, width), lambda b, off, own, val: (off[b], 0, 0)),
            pl.BlockSpec((1, block_size, width), lambda b, off, own, val: (b, 0, 0)),
            pl.BlockSpec((1, width, block_size), lambda b, off, own, val: (b, 0, 0)),
        ],
        out_specs=[
            pl.BlockSpec((requests, heads, 1, query_rows), lambda b, off, own, val: (0, 0, 0, 0)),
            pl.BlockSpec((requests, heads, 1, query_rows), lambda b, off, own, val: (0, 0, 0, 0)),
            pl.BlockSpec((requests, heads, HD, query_rows), lambda b, off, own, val: (0, 0, 0, 0)),
        ],
    )
    resident = 2 * requests * heads * (HD + 16) * query_rows * 4
    return pl.pallas_call(
        kernel,
        grid_spec=grid_spec,
        out_shape=[
            jax.ShapeDtypeStruct((requests, heads, 1, query_rows), jnp.float32),
            jax.ShapeDtypeStruct((requests, heads, 1, query_rows), jnp.float32),
            jax.ShapeDtypeStruct((requests, heads, HD, query_rows), jnp.float32),
        ],
        compiler_params=pltpu.CompilerParams(
            dimension_semantics=("arbitrary",),
            vmem_limit_bytes=resident + 24 * 1024 * 1024,
        ),
    )(owner_offset, owner, valid, ring_queries, keys, values_t)


def per_device(
    cycle,
    hidden,
    norm_gain,
    router_weight,
    att_experts,
    q_weight,
    kv_weight,
    o_weight,
    kv_cache,
    cached_blocks,
    tail_trim,
    block_pool,
):
    head_count = lax.axis_size("heads")
    seq_rank = lax.axis_index("seq")
    block_size = kv_cache.shape[2]
    local_blocks = kv_cache.shape[1]
    local_heads = q_weight.shape[2] // HD
    scale_q = HD ** (-0.5)
    normed = normalize(hidden[0], norm_gain)
    gathered = shift_all_gather(normed, "heads").reshape(-1, normed.shape[1])
    new_count = gathered.shape[0]
    rows_each = new_count // head_count
    head_rank = lax.axis_index("heads")
    token_ids = (
        ((head_rank + jnp.arange(head_count, dtype=jnp.int32)[:, None]) % head_count) * rows_each
        + jnp.arange(rows_each, dtype=jnp.int32)[None, :]
    ).reshape(new_count)
    chosen = jnp.take(att_experts[0], token_ids, axis=0)
    cached_len = cached_blocks * block_size - tail_trim
    positions = cached_len[seq_rank] + token_ids
    onehot, gates = route(gathered, router_weight, chosen)
    every_q = jnp.einsum("nd,edc->nec", gathered, q_weight, preferred_element_type=jnp.float32)
    chosen_q = jnp.sum(onehot[:, :, :, None] * every_q[:, None, :, :], axis=2).reshape(
        new_count, 2, local_heads, HD
    )
    queries = rotate(chosen_q, positions).astype(jnp.bfloat16)
    fresh = jnp.einsum("nd,sdc->snc", gathered, kv_weight, preferred_element_type=jnp.float32)
    new_keys = rotate(fresh[0].reshape(new_count, local_heads, HD), positions).astype(jnp.bfloat16)
    new_values = fresh[1].reshape(new_count, local_heads, HD).astype(jnp.bfloat16)
    ring_queries = ring_all_gather(
        queries.reshape(new_count * 2, local_heads * HD), "seq", cycle
    )
    request_count = ring_queries.shape[0]
    ring_size = len(cycle)
    position_of = np.argsort(np.asarray(cycle))
    position = jnp.asarray(position_of, dtype=jnp.int32)[seq_rank]
    pool_size = block_pool.shape[0]

    global_ids = seq_rank * local_blocks + jnp.arange(local_blocks, dtype=jnp.int32)
    matches = block_pool[None, :] == global_ids[:, None]
    slot_of = jnp.sum(
        jnp.where(matches, jnp.arange(pool_size, dtype=jnp.int32)[None, :], 0), axis=1
    )
    starts = jnp.cumsum(cached_blocks) - cached_blocks
    owner = jnp.sum((starts[None, :] <= slot_of[:, None]).astype(jnp.int32), axis=1) - 1
    ordinal = slot_of - starts[owner]
    owns = owner[None, :] == jnp.arange(request_count, dtype=jnp.int32)[:, None]

    self_scores = (
        jnp.einsum("nkhc,thc->hnkt", queries, new_keys, preferred_element_type=jnp.float32)
        * scale_q
    )
    causal = token_ids[None, :] <= token_ids[:, None]
    self_scores = jnp.where(causal[None, :, None, :], self_scores, NEG_FILL)
    self_best = jnp.max(self_scores, axis=-1)
    self_weights = jnp.exp(self_scores - self_best[..., None])
    self_total = jnp.sum(self_weights, axis=-1)
    self_accum = jnp.einsum(
        "hnkt,thc->hnkc",
        self_weights.astype(jnp.bfloat16),
        new_values,
        preferred_element_type=jnp.float32,
    )
    ring_queries, self_best, self_total, self_accum = lax.optimization_barrier(
        (ring_queries, self_best, self_total, self_accum)
    )
    owner_offset = (jnp.asarray(position_of, dtype=jnp.int32)[owner] - position) % ring_size
    valid = jnp.clip(cached_len[owner] - ordinal * block_size, 0, block_size).astype(jnp.int32)
    query_rows = new_count * 2
    request_best, totals, accum = block_attention(
        ring_queries,
        kv_cache[0],
        jnp.swapaxes(kv_cache[1], 1, 2),
        owner_offset,
        owner,
        valid,
        request_count,
    )
    request_best = request_best[:, :, 0]
    best_hi, best_lo = split_bf16(request_best)
    request_ref = best_hi + best_lo
    present = request_best > 0.5 * NEG_FILL
    adjust = jnp.exp(jnp.where(present, request_best - request_ref, 0.0))
    totals = totals[:, :, 0] * adjust
    accum = accum * adjust[:, :, None, :]
    totals_hi, totals_lo = split_bf16(totals)
    stats = jnp.stack([best_hi, best_lo, totals_hi, totals_lo], axis=1).astype(jnp.bfloat16)
    payload = jnp.concatenate(
        [
            accum.astype(jnp.bfloat16).reshape(request_count, -1, query_rows),
            stats.reshape(request_count, -1, query_rows),
        ],
        axis=1,
    )
    cycle_arr = jnp.asarray(cycle, dtype=jnp.int32)
    arrivals = [lax.dynamic_index_in_dim(payload, seq_rank, 0, keepdims=False)]
    for s in range(1, ring_size):
        target = cycle_arr[(position + s) % ring_size]
        pairs = [(cycle[i], cycle[(i + s) % ring_size]) for i in range(ring_size)]
        arrivals.append(
            lax.ppermute(lax.dynamic_index_in_dim(payload, target, 0, keepdims=False), "seq", pairs)
        )
    received = jnp.stack(arrivals, axis=0)
    acc_rows = local_heads * HD
    sources = received.shape[0]
    part_accum = received[:, :acc_rows].astype(jnp.float32).reshape(
        sources, local_heads, HD, query_rows
    )
    part_stats = received[:, acc_rows:].astype(jnp.float32).reshape(
        sources, 4, local_heads, query_rows
    )
    part_best = part_stats[:, 0] + part_stats[:, 1]
    part_totals = part_stats[:, 2] + part_stats[:, 3]
    cache_best = jnp.max(part_best, axis=0)
    share = jnp.exp(part_best - cache_best[None])
    cache_total = jnp.sum(part_totals * share, axis=0).reshape(local_heads, new_count, 2)
    cache_accum = jnp.transpose(
        jnp.sum(part_accum * share[:, :, None, :], axis=0), (0, 2, 1)
    ).reshape(local_heads, new_count, 2, HD)
    cache_best = cache_best.reshape(local_heads, new_count, 2)

    peak = jnp.maximum(cache_best, self_best)
    cache_share = jnp.exp(cache_best - peak)
    self_share = jnp.exp(self_best - peak)
    numerator = cache_accum * cache_share[..., None] + self_accum * self_share[..., None]
    denominator = cache_total * cache_share + self_total * self_share
    attended = (
        jnp.transpose((numerator / denominator[..., None]).astype(jnp.bfloat16), (1, 2, 0, 3))
        .reshape(new_count, 2, local_heads * HD)
    )
    output_blocks = []
    for block in list(range(1, head_count)) + [0]:
        rows = slice(block * rows_each, (block + 1) * rows_each)
        block_out = jnp.zeros((rows_each, o_weight.shape[2]), jnp.float32)
        for expert in range(o_weight.shape[0]):
            weight_expert = jnp.sum(onehot[rows, :, expert] * gates[rows], axis=1)
            picked = jnp.where(
                chosen[rows, 0:1] == expert,
                attended[rows, 0],
                jnp.where(
                    chosen[rows, 1:2] == expert, attended[rows, 1], jnp.zeros_like(attended[rows, 0])
                ),
            )
            block_out = block_out + weight_expert[:, None] * jnp.dot(
                picked, o_weight[expert], preferred_element_type=jnp.float32
            )
        block_out = block_out.astype(jnp.bfloat16)
        block_out, attended = lax.optimization_barrier((block_out, attended))
        output_blocks.append(block_out)
    summed = shift_reduce_scatter(output_blocks[-1:] + output_blocks[:-1], "heads")
    return summed[None].astype(jnp.bfloat16)


def solution(mesh):
    return jax.shard_map(
        functools.partial(per_device, tuple(seq_cycle(mesh))),
        mesh=mesh,
        in_specs=(
            P("seq", "heads", None),
            P(),
            P(),
            P("seq", None, None),
            P(None, None, "heads"),
            P(None, None, "heads"),
            P(None, "heads", None),
            P(None, "seq", None, "heads"),
            P(),
            P(),
            P(),
        ),
        out_specs=P("seq", "heads", None),
        check_vma=False,
    )
```

```python
import functools

import numpy as np
import jax
import jax.numpy as jnp
from jax import lax
from jax.experimental import pallas as pl
from jax.experimental.pallas import tpu as pltpu
from jax.sharding import PartitionSpec as P

HD = 128


NEG_FILL = -1e30


def rotate(values, positions):
    half_dim = values.shape[-1] // 2
    inverse = 10000.0 ** (-2.0 * jnp.arange(half_dim, dtype=jnp.float32) / values.shape[-1])
    angles = positions.astype(jnp.float32)[:, None] * inverse[None, :]
    target = (values.shape[0],) + (1,) * (values.ndim - 2) + (half_dim,)
    cosine = jnp.cos(angles).reshape(target)
    sine_part = jnp.sin(angles).reshape(target)
    leading_part = values[..., :half_dim]
    trailing_part = values[..., half_dim:]
    return jnp.concatenate(
        [
            leading_part * cosine - trailing_part * sine_part,
            trailing_part * cosine + leading_part * sine_part,
        ],
        axis=-1,
    )


def normalize(rows, norm_gain):
    wide_rows = rows.astype(jnp.float32)
    scaled = wide_rows * lax.rsqrt(jnp.mean(wide_rows * wide_rows, axis=-1, keepdims=True) + 1e-05)
    return (scaled * norm_gain.astype(jnp.float32)).astype(jnp.bfloat16)


def route(normed, router_weight, chosen):
    logits = jnp.dot(normed, router_weight, preferred_element_type=jnp.float32)
    experts_all = router_weight.shape[1]
    onehot = (chosen[:, :, None] == jnp.arange(experts_all, dtype=jnp.int32)[None, None, :]).astype(
        jnp.float32
    )
    picked = jnp.sum(onehot * logits[:, None, :], axis=-1)
    return (onehot, jax.nn.softmax(picked, axis=-1))


def split_bf16(x):
    hi = lax.reduce_precision(x, exponent_bits=8, mantissa_bits=7)
    lo = lax.reduce_precision(x - hi, exponent_bits=8, mantissa_bits=7)
    return hi, lo


def seq_cycle(mesh):
    size = mesh.shape["seq"]
    plain = list(range(size))
    try:
        devices = np.moveaxis(np.asarray(mesh.devices), mesh.axis_names.index("seq"), -1)
        line = devices.reshape(-1, size)[0]
        coords = np.array([list(d.coords) for d in line])
    except Exception:
        return plain
    varying = [k for k in range(coords.shape[1]) if len(set(coords[:, k])) > 1]
    if len(varying) == 1:
        order = sorted(plain, key=lambda j: coords[j, varying[0]])
        return order[0::2] + order[1::2][::-1]
    if len(varying) != 2:
        return plain
    dim_a, dim_b = varying
    values_a = sorted(set(coords[:, dim_a]))
    values_b = sorted(set(coords[:, dim_b]))
    if len(values_a) % 2:
        dim_a, dim_b, values_a, values_b = dim_b, dim_a, values_b, values_a
    if len(values_a) % 2 or len(values_a) * len(values_b) != size:
        return plain
    at = {(coords[j, dim_a], coords[j, dim_b]): j for j in plain}
    cycle = [at[(a, values_b[0])] for a in values_a]
    for row, a in enumerate(reversed(values_a)):
        columns = values_b[1:] if row % 2 == 0 else values_b[1:][::-1]
        cycle += [at[(a, b)] for b in columns]
    if sorted(cycle) != plain:
        return plain
    return cycle


def shift_all_gather(piece, axis_name):
    size = lax.axis_size(axis_name)
    rank = lax.axis_index(axis_name)
    by_offset = [piece] + [
        lax.ppermute(piece, axis_name, [(i, (i + s) % size) for i in range(size)])
        for s in range(1, size)
    ]
    return jnp.stack(by_offset[:1] + by_offset[1:][::-1], axis=0)


def shift_reduce_scatter(blocks, axis_name):
    size = lax.axis_size(axis_name)
    total = blocks[0].astype(jnp.float32)
    for s in range(1, size):
        moved = lax.ppermute(blocks[s], axis_name, [(i, (i + s) % size) for i in range(size)])
        total = total + moved.astype(jnp.float32)
    return total


def ring_all_gather(piece, axis_name, cycle):
    size = len(cycle)
    forward = [(cycle[i], cycle[(i + 1) % size]) for i in range(size)]
    backward = [(cycle[(i + 1) % size], cycle[i]) for i in range(size)]
    ahead = size // 2
    behind = size - 1 - ahead
    from_behind, from_ahead = [], []
    moving = piece
    for _ in range(ahead):
        moving = lax.ppermute(moving, axis_name, forward)
        from_behind.append(moving)
    moving = piece
    for _ in range(behind):
        moving = lax.ppermute(moving, axis_name, backward)
        from_ahead.append(moving)
    return jnp.stack([piece] + from_ahead + from_behind[::-1], axis=0)


def block_attention(ring_queries, keys, values_t, owner_offset, owner, valid, requests):
    blocks, block_size, width = keys.shape
    query_rows = ring_queries.shape[1]
    heads = width // HD
    scale = HD ** (-0.5)

    def kernel(offset_ref, owner_ref, valid_ref, q_ref, k_ref, v_ref, best_ref, total_ref, accum_ref):
        b = pl.program_id(0)

        @pl.when(b == 0)
        def _():
            best_ref[...] = jnp.full(best_ref.shape, NEG_FILL, jnp.float32)
            total_ref[...] = jnp.zeros(total_ref.shape, jnp.float32)
            accum_ref[...] = jnp.zeros(accum_ref.shape, jnp.float32)

        request = owner_ref[b]
        limit = valid_ref[b]
        row = lax.broadcasted_iota(jnp.int32, (block_size, query_rows), 0)
        for h in range(heads):
            q = q_ref[0, :, h * HD:(h + 1) * HD]
            k = k_ref[0, :, h * HD:(h + 1) * HD]
            scores = lax.dot_general(
                k, q, (((1,), (1,)), ((), ())), preferred_element_type=jnp.float32
            ) * scale
            scores = jnp.where(row < limit, scores, NEG_FILL)
            old_best = best_ref[request, h]
            new_best = jnp.maximum(old_best, jnp.max(scores, axis=0, keepdims=True))
            rescale = jnp.exp(old_best - new_best)
            weights = jnp.exp(scores - new_best)
            best_ref[request, h] = new_best
            total_ref[request, h] = total_ref[request, h] * rescale + jnp.sum(
                weights, axis=0, keepdims=True
            )
            v_t = v_ref[0, h * HD:(h + 1) * HD, :]
            accum_ref[request, h] = accum_ref[request, h] * rescale + jnp.dot(
                v_t, weights.astype(jnp.bfloat16), preferred_element_type=jnp.float32
            )

    grid_spec = pltpu.PrefetchScalarGridSpec(
        num_scalar_prefetch=3,
        grid=(blocks,),
        in_specs=[
            pl.BlockSpec((1, query_rows, width), lambda b, off, own, val: (off[b], 0, 0)),
            pl.BlockSpec((1, block_size, width), lambda b, off, own, val: (b, 0, 0)),
            pl.BlockSpec((1, width, block_size), lambda b, off, own, val: (b, 0, 0)),
        ],
        out_specs=[
            pl.BlockSpec((requests, heads, 1, query_rows), lambda b, off, own, val: (0, 0, 0, 0)),
            pl.BlockSpec((requests, heads, 1, query_rows), lambda b, off, own, val: (0, 0, 0, 0)),
            pl.BlockSpec((requests, heads, HD, query_rows), lambda b, off, own, val: (0, 0, 0, 0)),
        ],
    )
    resident = 2 * requests * heads * (HD + 16) * query_rows * 4
    return pl.pallas_call(
        kernel,
        grid_spec=grid_spec,
        out_shape=[
            jax.ShapeDtypeStruct((requests, heads, 1, query_rows), jnp.float32),
            jax.ShapeDtypeStruct((requests, heads, 1, query_rows), jnp.float32),
            jax.ShapeDtypeStruct((requests, heads, HD, query_rows), jnp.float32),
        ],
        compiler_params=pltpu.CompilerParams(
            dimension_semantics=("arbitrary",),
            vmem_limit_bytes=resident + 24 * 1024 * 1024,
        ),
    )(owner_offset, owner, valid, ring_queries, keys, values_t)


def per_device(
    cycle,
    hidden,
    norm_gain,
    router_weight,
    att_experts,
    q_weight,
    kv_weight,
    o_weight,
    kv_cache,
    cached_blocks,
    tail_trim,
    block_pool,
):
    head_count = lax.axis_size("heads")
    seq_rank = lax.axis_index("seq")
    block_size = kv_cache.shape[2]
    local_blocks = kv_cache.shape[1]
    local_heads = q_weight.shape[2] // HD
    scale_q = HD ** (-0.5)
    normed = normalize(hidden[0], norm_gain)
    gathered = shift_all_gather(normed, "heads").reshape(-1, normed.shape[1])
    new_count = gathered.shape[0]
    rows_each = new_count // head_count
    head_rank = lax.axis_index("heads")
    token_ids = (
        ((head_rank + jnp.arange(head_count, dtype=jnp.int32)[:, None]) % head_count) * rows_each
        + jnp.arange(rows_each, dtype=jnp.int32)[None, :]
    ).reshape(new_count)
    chosen = jnp.take(att_experts[0], token_ids, axis=0)
    cached_len = cached_blocks * block_size - tail_trim
    positions = cached_len[seq_rank] + token_ids
    onehot, gates = route(gathered, router_weight, chosen)
    every_q = jnp.einsum("nd,edc->enc", gathered, q_weight, preferred_element_type=jnp.float32)
    half_dim = HD // 2
    inverse = 10000.0 ** (-2.0 * jnp.arange(half_dim, dtype=jnp.float32) / HD)
    angles = positions.astype(jnp.float32)[:, None] * inverse[None, :]
    cosine = jnp.tile(jnp.cos(angles), (1, 2 * local_heads))
    signed_sine = jnp.tile(
        jnp.concatenate([-jnp.sin(angles), jnp.sin(angles)], axis=-1), (1, local_heads)
    )
    slot_tables = []
    for slot in range(chosen.shape[1]):
        slot_q = jnp.sum(onehot[:, slot, :].T[:, :, None] * every_q, axis=0)
        swapped = jnp.concatenate(
            [
                part
                for h in range(local_heads)
                for part in (
                    slot_q[:, h * HD + half_dim:(h + 1) * HD],
                    slot_q[:, h * HD:h * HD + half_dim],
                )
            ],
            axis=-1,
        )
        slot_tables.append((slot_q * cosine + swapped * signed_sine).astype(jnp.bfloat16))
    queries = jnp.stack(slot_tables, axis=1).reshape(new_count, 2, local_heads, HD)
    fresh = jnp.einsum("nd,sdc->snc", gathered, kv_weight, preferred_element_type=jnp.float32)
    new_keys = rotate(fresh[0].reshape(new_count, local_heads, HD), positions).astype(jnp.bfloat16)
    new_values = fresh[1].reshape(new_count, local_heads, HD).astype(jnp.bfloat16)
    ring_queries = ring_all_gather(jnp.concatenate(slot_tables, axis=0), "seq", cycle)
    request_count = ring_queries.shape[0]
    ring_size = len(cycle)
    position_of = np.argsort(np.asarray(cycle))
    position = jnp.asarray(position_of, dtype=jnp.int32)[seq_rank]
    pool_size = block_pool.shape[0]

    global_ids = seq_rank * local_blocks + jnp.arange(local_blocks, dtype=jnp.int32)
    matches = block_pool[None, :] == global_ids[:, None]
    slot_of = jnp.sum(
        jnp.where(matches, jnp.arange(pool_size, dtype=jnp.int32)[None, :], 0), axis=1
    )
    starts = jnp.cumsum(cached_blocks) - cached_blocks
    owner = jnp.sum((starts[None, :] <= slot_of[:, None]).astype(jnp.int32), axis=1) - 1
    ordinal = slot_of - starts[owner]
    owns = owner[None, :] == jnp.arange(request_count, dtype=jnp.int32)[:, None]

    self_scores = (
        jnp.einsum("nkhc,thc->hnkt", queries, new_keys, preferred_element_type=jnp.float32)
        * scale_q
    )
    causal = token_ids[None, :] <= token_ids[:, None]
    self_scores = jnp.where(causal[None, :, None, :], self_scores, NEG_FILL)
    self_best = jnp.max(self_scores, axis=-1)
    self_weights = jnp.exp(self_scores - self_best[..., None])
    self_total = jnp.sum(self_weights, axis=-1)
    self_accum = jnp.einsum(
        "hnkt,thc->hnkc",
        self_weights.astype(jnp.bfloat16),
        new_values,
        preferred_element_type=jnp.float32,
    )
    ring_queries, self_best, self_total, self_accum = lax.optimization_barrier(
        (ring_queries, self_best, self_total, self_accum)
    )
    owner_offset = (jnp.asarray(position_of, dtype=jnp.int32)[owner] - position) % ring_size
    valid = jnp.clip(cached_len[owner] - ordinal * block_size, 0, block_size).astype(jnp.int32)
    query_rows = new_count * 2
    request_best, totals, accum = block_attention(
        ring_queries,
        kv_cache[0],
        jnp.swapaxes(kv_cache[1], 1, 2),
        owner_offset,
        owner,
        valid,
        request_count,
    )
    request_best = request_best[:, :, 0]
    best_hi, best_lo = split_bf16(request_best)
    request_ref = best_hi + best_lo
    present = request_best > 0.5 * NEG_FILL
    adjust = jnp.exp(jnp.where(present, request_best - request_ref, 0.0))
    totals = totals[:, :, 0] * adjust
    accum = accum * adjust[:, :, None, :]
    totals_hi, totals_lo = split_bf16(totals)
    stats = jnp.stack([best_hi, best_lo, totals_hi, totals_lo], axis=1).astype(jnp.bfloat16)
    payload = jnp.concatenate(
        [
            accum.astype(jnp.bfloat16).reshape(request_count, -1, query_rows),
            stats.reshape(request_count, -1, query_rows),
        ],
        axis=1,
    )
    received = lax.all_to_all(payload, "seq", 0, 0, tiled=True)
    acc_rows = local_heads * HD
    sources = received.shape[0]
    part_accum = received[:, :acc_rows].astype(jnp.float32).reshape(
        sources, local_heads, HD, query_rows
    )
    part_stats = received[:, acc_rows:].astype(jnp.float32).reshape(
        sources, 4, local_heads, query_rows
    )
    part_best = part_stats[:, 0] + part_stats[:, 1]
    part_totals = part_stats[:, 2] + part_stats[:, 3]
    cache_best = jnp.max(part_best, axis=0)
    share = jnp.exp(part_best - cache_best[None])
    cache_total = jnp.swapaxes(
        jnp.sum(part_totals * share, axis=0).reshape(local_heads, 2, new_count), 1, 2
    )
    cache_accum = jnp.transpose(
        jnp.sum(part_accum * share[:, :, None, :], axis=0).reshape(local_heads, HD, 2, new_count),
        (0, 3, 2, 1),
    )
    cache_best = jnp.swapaxes(cache_best.reshape(local_heads, 2, new_count), 1, 2)

    peak = jnp.maximum(cache_best, self_best)
    cache_share = jnp.exp(cache_best - peak)
    self_share = jnp.exp(self_best - peak)
    numerator = cache_accum * cache_share[..., None] + self_accum * self_share[..., None]
    denominator = cache_total * cache_share + self_total * self_share
    attended = (
        jnp.transpose((numerator / denominator[..., None]).astype(jnp.bfloat16), (1, 2, 0, 3))
        .reshape(new_count, 2, local_heads * HD)
    )
    output_blocks = []
    for block in list(range(1, head_count)) + [0]:
        rows = slice(block * rows_each, (block + 1) * rows_each)
        block_out = jnp.zeros((rows_each, o_weight.shape[2]), jnp.float32)
        for expert in range(o_weight.shape[0]):
            weight_expert = jnp.sum(onehot[rows, :, expert] * gates[rows], axis=1)
            picked = jnp.where(
                chosen[rows, 0:1] == expert,
                attended[rows, 0],
                jnp.where(
                    chosen[rows, 1:2] == expert, attended[rows, 1], jnp.zeros_like(attended[rows, 0])
                ),
            )
            block_out = block_out + weight_expert[:, None] * jnp.dot(
                picked, o_weight[expert], preferred_element_type=jnp.float32
            )
        block_out = block_out.astype(jnp.bfloat16)
        block_out, attended = lax.optimization_barrier((block_out, attended))
        output_blocks.append(block_out)
    summed = shift_reduce_scatter(output_blocks[-1:] + output_blocks[:-1], "heads")
    return summed[None].astype(jnp.bfloat16)


def solution(mesh):
    return jax.shard_map(
        functools.partial(per_device, tuple(seq_cycle(mesh))),
        mesh=mesh,
        in_specs=(
            P("seq", "heads", None),
            P(),
            P(),
            P("seq", None, None),
            P(None, None, "heads"),
            P(None, None, "heads"),
            P(None, "heads", None),
            P(None, "seq", None, "heads"),
            P(),
            P(),
            P(),
        ),
        out_specs=P("seq", "heads", None),
        check_vma=False,
    )
```

```python
import functools

import numpy as np
import jax
import jax.numpy as jnp
from jax import lax
from jax.experimental import pallas as pl
from jax.experimental.pallas import tpu as pltpu
from jax.sharding import PartitionSpec as P

HD = 128


NEG_FILL = -1e30


def rotate(values, positions):
    half_dim = values.shape[-1] // 2
    inverse = 10000.0 ** (-2.0 * jnp.arange(half_dim, dtype=jnp.float32) / values.shape[-1])
    angles = positions.astype(jnp.float32)[:, None] * inverse[None, :]
    target = (values.shape[0],) + (1,) * (values.ndim - 2) + (half_dim,)
    cosine = jnp.cos(angles).reshape(target)
    sine_part = jnp.sin(angles).reshape(target)
    leading_part = values[..., :half_dim]
    trailing_part = values[..., half_dim:]
    return jnp.concatenate(
        [
            leading_part * cosine - trailing_part * sine_part,
            trailing_part * cosine + leading_part * sine_part,
        ],
        axis=-1,
    )


def normalize(rows, norm_gain):
    wide_rows = rows.astype(jnp.float32)
    scaled = wide_rows * lax.rsqrt(jnp.mean(wide_rows * wide_rows, axis=-1, keepdims=True) + 1e-05)
    return (scaled * norm_gain.astype(jnp.float32)).astype(jnp.bfloat16)


def route(normed, router_weight, chosen):
    logits = jnp.dot(normed, router_weight, preferred_element_type=jnp.float32)
    experts_all = router_weight.shape[1]
    onehot = (chosen[:, :, None] == jnp.arange(experts_all, dtype=jnp.int32)[None, None, :]).astype(
        jnp.float32
    )
    picked = jnp.sum(onehot * logits[:, None, :], axis=-1)
    return (onehot, jax.nn.softmax(picked, axis=-1))


def split_bf16(x):
    hi = lax.reduce_precision(x, exponent_bits=8, mantissa_bits=7)
    lo = lax.reduce_precision(x - hi, exponent_bits=8, mantissa_bits=7)
    return hi, lo


def seq_cycle(mesh):
    size = mesh.shape["seq"]
    plain = list(range(size))
    try:
        devices = np.moveaxis(np.asarray(mesh.devices), mesh.axis_names.index("seq"), -1)
        line = devices.reshape(-1, size)[0]
        coords = np.array([list(d.coords) for d in line])
    except Exception:
        return plain
    varying = [k for k in range(coords.shape[1]) if len(set(coords[:, k])) > 1]
    if len(varying) == 1:
        order = sorted(plain, key=lambda j: coords[j, varying[0]])
        return order[0::2] + order[1::2][::-1]
    if len(varying) != 2:
        return plain
    dim_a, dim_b = varying
    values_a = sorted(set(coords[:, dim_a]))
    values_b = sorted(set(coords[:, dim_b]))
    if len(values_a) % 2:
        dim_a, dim_b, values_a, values_b = dim_b, dim_a, values_b, values_a
    if len(values_a) % 2 or len(values_a) * len(values_b) != size:
        return plain
    at = {(coords[j, dim_a], coords[j, dim_b]): j for j in plain}
    cycle = [at[(a, values_b[0])] for a in values_a]
    for row, a in enumerate(reversed(values_a)):
        columns = values_b[1:] if row % 2 == 0 else values_b[1:][::-1]
        cycle += [at[(a, b)] for b in columns]
    if sorted(cycle) != plain:
        return plain
    return cycle


def shift_all_gather(piece, axis_name):
    size = lax.axis_size(axis_name)
    rank = lax.axis_index(axis_name)
    by_offset = [piece] + [
        lax.ppermute(piece, axis_name, [(i, (i + s) % size) for i in range(size)])
        for s in range(1, size)
    ]
    return jnp.stack(by_offset[:1] + by_offset[1:][::-1], axis=0)


def shift_reduce_scatter(blocks, axis_name):
    size = lax.axis_size(axis_name)
    total = blocks[0].astype(jnp.float32)
    for s in range(1, size):
        moved = lax.ppermute(blocks[s], axis_name, [(i, (i + s) % size) for i in range(size)])
        total = total + moved.astype(jnp.float32)
    return total


def ring_all_gather(piece, axis_name, cycle):
    size = len(cycle)
    forward = [(cycle[i], cycle[(i + 1) % size]) for i in range(size)]
    backward = [(cycle[(i + 1) % size], cycle[i]) for i in range(size)]
    ahead = size // 2
    behind = size - 1 - ahead
    from_behind, from_ahead = [], []
    moving = piece
    for _ in range(ahead):
        moving = lax.ppermute(moving, axis_name, forward)
        from_behind.append(moving)
    moving = piece
    for _ in range(behind):
        moving = lax.ppermute(moving, axis_name, backward)
        from_ahead.append(moving)
    return jnp.stack([piece] + from_ahead + from_behind[::-1], axis=0)


def block_attention(ring_queries, keys, values_t, owner_offset, owner, valid, requests):
    blocks, block_size, width = keys.shape
    query_rows = ring_queries.shape[1]
    heads = width // HD
    scale = HD ** (-0.5)

    def kernel(offset_ref, owner_ref, valid_ref, q_ref, k_ref, v_ref, best_ref, total_ref, accum_ref):
        b = pl.program_id(0)

        @pl.when(b == 0)
        def _():
            best_ref[...] = jnp.full(best_ref.shape, NEG_FILL, jnp.float32)
            total_ref[...] = jnp.zeros(total_ref.shape, jnp.float32)
            accum_ref[...] = jnp.zeros(accum_ref.shape, jnp.float32)

        request = owner_ref[b]
        limit = valid_ref[b]
        row = lax.broadcasted_iota(jnp.int32, (block_size, query_rows), 0)
        for h in range(heads):
            q = q_ref[0, :, h * HD:(h + 1) * HD]
            k = k_ref[0, :, h * HD:(h + 1) * HD]
            scores = lax.dot_general(
                k, q, (((1,), (1,)), ((), ())), preferred_element_type=jnp.float32
            ) * scale
            scores = jnp.where(row < limit, scores, NEG_FILL)
            old_best = best_ref[request, h]
            new_best = jnp.maximum(old_best, jnp.max(scores, axis=0, keepdims=True))
            rescale = jnp.exp(old_best - new_best)
            weights = jnp.exp(scores - new_best)
            best_ref[request, h] = new_best
            total_ref[request, h] = total_ref[request, h] * rescale + jnp.sum(
                weights, axis=0, keepdims=True
            )
            v_t = v_ref[0, h * HD:(h + 1) * HD, :]
            accum_ref[request, h] = accum_ref[request, h] * rescale + jnp.dot(
                v_t, weights.astype(jnp.bfloat16), preferred_element_type=jnp.float32
            )

    grid_spec = pltpu.PrefetchScalarGridSpec(
        num_scalar_prefetch=3,
        grid=(blocks,),
        in_specs=[
            pl.BlockSpec((1, query_rows, width), lambda b, off, own, val: (off[b], 0, 0)),
            pl.BlockSpec((1, block_size, width), lambda b, off, own, val: (b, 0, 0)),
            pl.BlockSpec((1, width, block_size), lambda b, off, own, val: (b, 0, 0)),
        ],
        out_specs=[
            pl.BlockSpec((requests, heads, 1, query_rows), lambda b, off, own, val: (0, 0, 0, 0)),
            pl.BlockSpec((requests, heads, 1, query_rows), lambda b, off, own, val: (0, 0, 0, 0)),
            pl.BlockSpec((requests, heads, HD, query_rows), lambda b, off, own, val: (0, 0, 0, 0)),
        ],
    )
    resident = 2 * requests * heads * (HD + 16) * query_rows * 4
    return pl.pallas_call(
        kernel,
        grid_spec=grid_spec,
        out_shape=[
            jax.ShapeDtypeStruct((requests, heads, 1, query_rows), jnp.float32),
            jax.ShapeDtypeStruct((requests, heads, 1, query_rows), jnp.float32),
            jax.ShapeDtypeStruct((requests, heads, HD, query_rows), jnp.float32),
        ],
        compiler_params=pltpu.CompilerParams(
            dimension_semantics=("arbitrary",),
            vmem_limit_bytes=resident + 24 * 1024 * 1024,
        ),
    )(owner_offset, owner, valid, ring_queries, keys, values_t)


def per_device(
    cycle,
    hidden,
    norm_gain,
    router_weight,
    att_experts,
    q_weight,
    kv_weight,
    o_weight,
    kv_cache,
    cached_blocks,
    tail_trim,
    block_pool,
):
    head_count = lax.axis_size("heads")
    seq_rank = lax.axis_index("seq")
    block_size = kv_cache.shape[2]
    local_blocks = kv_cache.shape[1]
    local_heads = q_weight.shape[2] // HD
    scale_q = HD ** (-0.5)
    normed = normalize(hidden[0], norm_gain)
    gathered = shift_all_gather(normed, "heads").reshape(-1, normed.shape[1])
    new_count = gathered.shape[0]
    rows_each = new_count // head_count
    head_rank = lax.axis_index("heads")
    token_ids = (
        ((head_rank + jnp.arange(head_count, dtype=jnp.int32)[:, None]) % head_count) * rows_each
        + jnp.arange(rows_each, dtype=jnp.int32)[None, :]
    ).reshape(new_count)
    chosen = jnp.take(att_experts[0], token_ids, axis=0)
    cached_len = cached_blocks * block_size - tail_trim
    positions = cached_len[seq_rank] + token_ids
    onehot, gates = route(gathered, router_weight, chosen)
    every_q = jnp.einsum("nd,edc->enc", gathered, q_weight, preferred_element_type=jnp.float32)
    half_dim = HD // 2
    inverse = 10000.0 ** (-2.0 * jnp.arange(half_dim, dtype=jnp.float32) / HD)
    angles = positions.astype(jnp.float32)[:, None] * inverse[None, :]
    cosine = jnp.tile(jnp.cos(angles), (1, 2 * local_heads))
    signed_sine = jnp.tile(
        jnp.concatenate([-jnp.sin(angles), jnp.sin(angles)], axis=-1), (1, local_heads)
    )
    slot_tables = []
    for slot in range(chosen.shape[1]):
        slot_q = every_q[0]
        for expert in range(1, every_q.shape[0]):
            slot_q = jnp.where(chosen[:, slot, None] == expert, every_q[expert], slot_q)
        swapped = jnp.concatenate(
            [
                part
                for h in range(local_heads)
                for part in (
                    slot_q[:, h * HD + half_dim:(h + 1) * HD],
                    slot_q[:, h * HD:h * HD + half_dim],
                )
            ],
            axis=-1,
        )
        slot_tables.append((slot_q * cosine + swapped * signed_sine).astype(jnp.bfloat16))
    queries = jnp.stack(slot_tables, axis=1).reshape(new_count, 2, local_heads, HD)
    fresh = jnp.einsum("nd,sdc->snc", gathered, kv_weight, preferred_element_type=jnp.float32)
    new_keys = rotate(fresh[0].reshape(new_count, local_heads, HD), positions).astype(jnp.bfloat16)
    new_values = fresh[1].reshape(new_count, local_heads, HD).astype(jnp.bfloat16)
    ring_queries = ring_all_gather(jnp.concatenate(slot_tables, axis=0), "seq", cycle)
    request_count = ring_queries.shape[0]
    ring_size = len(cycle)
    position_of = np.argsort(np.asarray(cycle))
    position = jnp.asarray(position_of, dtype=jnp.int32)[seq_rank]
    pool_size = block_pool.shape[0]

    global_ids = seq_rank * local_blocks + jnp.arange(local_blocks, dtype=jnp.int32)
    matches = block_pool[None, :] == global_ids[:, None]
    slot_of = jnp.sum(
        jnp.where(matches, jnp.arange(pool_size, dtype=jnp.int32)[None, :], 0), axis=1
    )
    starts = jnp.cumsum(cached_blocks) - cached_blocks
    owner = jnp.sum((starts[None, :] <= slot_of[:, None]).astype(jnp.int32), axis=1) - 1
    ordinal = slot_of - starts[owner]
    owns = owner[None, :] == jnp.arange(request_count, dtype=jnp.int32)[:, None]

    self_scores = (
        jnp.einsum("nkhc,thc->hnkt", queries, new_keys, preferred_element_type=jnp.float32)
        * scale_q
    )
    causal = token_ids[None, :] <= token_ids[:, None]
    self_scores = jnp.where(causal[None, :, None, :], self_scores, NEG_FILL)
    self_best = jnp.max(self_scores, axis=-1)
    self_weights = jnp.exp(self_scores - self_best[..., None])
    self_total = jnp.sum(self_weights, axis=-1)
    self_accum = jnp.einsum(
        "hnkt,thc->hnkc",
        self_weights.astype(jnp.bfloat16),
        new_values,
        preferred_element_type=jnp.float32,
    )
    ring_queries, self_best, self_total, self_accum = lax.optimization_barrier(
        (ring_queries, self_best, self_total, self_accum)
    )
    owner_offset = (jnp.asarray(position_of, dtype=jnp.int32)[owner] - position) % ring_size
    valid = jnp.clip(cached_len[owner] - ordinal * block_size, 0, block_size).astype(jnp.int32)
    query_rows = new_count * 2
    request_best, totals, accum = block_attention(
        ring_queries,
        kv_cache[0],
        jnp.swapaxes(kv_cache[1], 1, 2),
        owner_offset,
        owner,
        valid,
        request_count,
    )
    request_best = request_best[:, :, 0]
    best_hi, best_lo = split_bf16(request_best)
    request_ref = best_hi + best_lo
    present = request_best > 0.5 * NEG_FILL
    adjust = jnp.exp(jnp.where(present, request_best - request_ref, 0.0))
    totals = totals[:, :, 0] * adjust
    accum = accum * adjust[:, :, None, :]
    totals_hi, totals_lo = split_bf16(totals)
    stats = jnp.stack([best_hi, best_lo, totals_hi, totals_lo], axis=1).astype(jnp.bfloat16)
    payload = jnp.concatenate(
        [
            accum.astype(jnp.bfloat16).reshape(request_count, -1, query_rows),
            stats.reshape(request_count, -1, query_rows),
        ],
        axis=1,
    )
    received = lax.all_to_all(payload, "seq", 0, 0, tiled=True)
    acc_rows = local_heads * HD
    sources = received.shape[0]
    part_accum = received[:, :acc_rows].astype(jnp.float32).reshape(
        sources, local_heads, HD, query_rows
    )
    part_stats = received[:, acc_rows:].astype(jnp.float32).reshape(
        sources, 4, local_heads, query_rows
    )
    part_best = part_stats[:, 0] + part_stats[:, 1]
    part_totals = part_stats[:, 2] + part_stats[:, 3]
    cache_best = jnp.max(part_best, axis=0)
    share = jnp.exp(part_best - cache_best[None])
    cache_total = jnp.swapaxes(
        jnp.sum(part_totals * share, axis=0).reshape(local_heads, 2, new_count), 1, 2
    )
    cache_accum = jnp.transpose(
        jnp.sum(part_accum * share[:, :, None, :], axis=0).reshape(local_heads, HD, 2, new_count),
        (0, 3, 2, 1),
    )
    cache_best = jnp.swapaxes(cache_best.reshape(local_heads, 2, new_count), 1, 2)

    peak = jnp.maximum(cache_best, self_best)
    cache_share = jnp.exp(cache_best - peak)
    self_share = jnp.exp(self_best - peak)
    numerator = cache_accum * cache_share[..., None] + self_accum * self_share[..., None]
    denominator = cache_total * cache_share + self_total * self_share
    attended = (
        jnp.transpose((numerator / denominator[..., None]).astype(jnp.bfloat16), (1, 2, 0, 3))
        .reshape(new_count, 2, local_heads * HD)
    )
    output_blocks = []
    for block in list(range(1, head_count)) + [0]:
        rows = slice(block * rows_each, (block + 1) * rows_each)
        block_out = jnp.zeros((rows_each, o_weight.shape[2]), jnp.float32)
        for expert in range(o_weight.shape[0]):
            weight_expert = jnp.sum(onehot[rows, :, expert] * gates[rows], axis=1)
            picked = jnp.where(
                chosen[rows, 0:1] == expert,
                attended[rows, 0],
                jnp.where(
                    chosen[rows, 1:2] == expert, attended[rows, 1], jnp.zeros_like(attended[rows, 0])
                ),
            )
            block_out = block_out + weight_expert[:, None] * jnp.dot(
                picked, o_weight[expert], preferred_element_type=jnp.float32
            )
        block_out = block_out.astype(jnp.bfloat16)
        block_out, attended = lax.optimization_barrier((block_out, attended))
        output_blocks.append(block_out)
    summed = shift_reduce_scatter(output_blocks[-1:] + output_blocks[:-1], "heads")
    return summed[None].astype(jnp.bfloat16)


def solution(mesh):
    return jax.shard_map(
        functools.partial(per_device, tuple(seq_cycle(mesh))),
        mesh=mesh,
        in_specs=(
            P("seq", "heads", None),
            P(),
            P(),
            P("seq", None, None),
            P(None, None, "heads"),
            P(None, None, "heads"),
            P(None, "heads", None),
            P(None, "seq", None, "heads"),
            P(),
            P(),
            P(),
        ),
        out_specs=P("seq", "heads", None),
        check_vma=False,
    )
```

```python
import functools

import numpy as np
import jax
import jax.numpy as jnp
from jax import lax
from jax.experimental import pallas as pl
from jax.experimental.pallas import tpu as pltpu
from jax.sharding import PartitionSpec as P

HD = 128


NEG_FILL = -1e30


def rotate(values, positions):
    half_dim = values.shape[-1] // 2
    inverse = 10000.0 ** (-2.0 * jnp.arange(half_dim, dtype=jnp.float32) / values.shape[-1])
    angles = positions.astype(jnp.float32)[:, None] * inverse[None, :]
    target = (values.shape[0],) + (1,) * (values.ndim - 2) + (half_dim,)
    cosine = jnp.cos(angles).reshape(target)
    sine_part = jnp.sin(angles).reshape(target)
    leading_part = values[..., :half_dim]
    trailing_part = values[..., half_dim:]
    return jnp.concatenate(
        [
            leading_part * cosine - trailing_part * sine_part,
            trailing_part * cosine + leading_part * sine_part,
        ],
        axis=-1,
    )


def normalize(rows, norm_gain):
    wide_rows = rows.astype(jnp.float32)
    scaled = wide_rows * lax.rsqrt(jnp.mean(wide_rows * wide_rows, axis=-1, keepdims=True) + 1e-05)
    return (scaled * norm_gain.astype(jnp.float32)).astype(jnp.bfloat16)


def route(normed, router_weight, chosen):
    logits = jnp.dot(normed, router_weight, preferred_element_type=jnp.float32)
    experts_all = router_weight.shape[1]
    onehot = (chosen[:, :, None] == jnp.arange(experts_all, dtype=jnp.int32)[None, None, :]).astype(
        jnp.float32
    )
    picked = jnp.sum(onehot * logits[:, None, :], axis=-1)
    return (onehot, jax.nn.softmax(picked, axis=-1))


def split_bf16(x):
    hi = lax.reduce_precision(x, exponent_bits=8, mantissa_bits=7)
    lo = lax.reduce_precision(x - hi, exponent_bits=8, mantissa_bits=7)
    return hi, lo


def seq_cycle(mesh):
    size = mesh.shape["seq"]
    plain = list(range(size))
    try:
        devices = np.moveaxis(np.asarray(mesh.devices), mesh.axis_names.index("seq"), -1)
        line = devices.reshape(-1, size)[0]
        coords = np.array([list(d.coords) for d in line])
    except Exception:
        return plain
    varying = [k for k in range(coords.shape[1]) if len(set(coords[:, k])) > 1]
    if len(varying) == 1:
        order = sorted(plain, key=lambda j: coords[j, varying[0]])
        return order[0::2] + order[1::2][::-1]
    if len(varying) != 2:
        return plain
    dim_a, dim_b = varying
    values_a = sorted(set(coords[:, dim_a]))
    values_b = sorted(set(coords[:, dim_b]))
    if len(values_a) % 2:
        dim_a, dim_b, values_a, values_b = dim_b, dim_a, values_b, values_a
    if len(values_a) % 2 or len(values_a) * len(values_b) != size:
        return plain
    at = {(coords[j, dim_a], coords[j, dim_b]): j for j in plain}
    cycle = [at[(a, values_b[0])] for a in values_a]
    for row, a in enumerate(reversed(values_a)):
        columns = values_b[1:] if row % 2 == 0 else values_b[1:][::-1]
        cycle += [at[(a, b)] for b in columns]
    if sorted(cycle) != plain:
        return plain
    return cycle


def shift_all_gather(piece, axis_name):
    size = lax.axis_size(axis_name)
    rank = lax.axis_index(axis_name)
    by_offset = [piece] + [
        lax.ppermute(piece, axis_name, [(i, (i + s) % size) for i in range(size)])
        for s in range(1, size)
    ]
    return jnp.stack(by_offset[:1] + by_offset[1:][::-1], axis=0)


def shift_reduce_scatter(blocks, axis_name):
    size = lax.axis_size(axis_name)
    total = blocks[0].astype(jnp.float32)
    for s in range(1, size):
        moved = lax.ppermute(blocks[s], axis_name, [(i, (i + s) % size) for i in range(size)])
        total = total + moved.astype(jnp.float32)
    return total


def ring_all_gather(piece, axis_name, cycle):
    size = len(cycle)
    forward = [(cycle[i], cycle[(i + 1) % size]) for i in range(size)]
    backward = [(cycle[(i + 1) % size], cycle[i]) for i in range(size)]
    ahead = size // 2
    behind = size - 1 - ahead
    from_behind, from_ahead = [], []
    moving = piece
    for _ in range(ahead):
        moving = lax.ppermute(moving, axis_name, forward)
        from_behind.append(moving)
    moving = piece
    for _ in range(behind):
        moving = lax.ppermute(moving, axis_name, backward)
        from_ahead.append(moving)
    return jnp.stack([piece] + from_ahead + from_behind[::-1], axis=0)


def block_attention(ring_queries, keys, values_t, owner_offset, owner, valid, requests):
    blocks, block_size, width = keys.shape
    query_rows = ring_queries.shape[1]
    heads = width // HD
    scale = HD ** (-0.5)

    def kernel(offset_ref, owner_ref, valid_ref, q_ref, k_ref, v_ref, best_ref, total_ref, accum_ref):
        b = pl.program_id(0)

        @pl.when(b == 0)
        def _():
            best_ref[...] = jnp.full(best_ref.shape, NEG_FILL, jnp.float32)
            total_ref[...] = jnp.zeros(total_ref.shape, jnp.float32)
            accum_ref[...] = jnp.zeros(accum_ref.shape, jnp.float32)

        request = owner_ref[b]
        limit = valid_ref[b]
        row = lax.broadcasted_iota(jnp.int32, (block_size, query_rows), 0)
        for h in range(heads):
            q = q_ref[0, :, h * HD:(h + 1) * HD]
            k = k_ref[0, :, h * HD:(h + 1) * HD]
            scores = lax.dot_general(
                k, q, (((1,), (1,)), ((), ())), preferred_element_type=jnp.float32
            ) * scale
            scores = jnp.where(row < limit, scores, NEG_FILL)
            old_best = best_ref[request, h]
            new_best = jnp.maximum(old_best, jnp.max(scores, axis=0, keepdims=True))
            rescale = jnp.exp(old_best - new_best)
            weights = jnp.exp(scores - new_best)
            best_ref[request, h] = new_best
            total_ref[request, h] = total_ref[request, h] * rescale + jnp.sum(
                weights, axis=0, keepdims=True
            )
            v_t = v_ref[0, h * HD:(h + 1) * HD, :]
            accum_ref[request, h] = accum_ref[request, h] * rescale + jnp.dot(
                v_t, weights.astype(jnp.bfloat16), preferred_element_type=jnp.float32
            )

    grid_spec = pltpu.PrefetchScalarGridSpec(
        num_scalar_prefetch=3,
        grid=(blocks,),
        in_specs=[
            pl.BlockSpec((1, query_rows, width), lambda b, off, own, val: (off[b], 0, 0)),
            pl.BlockSpec((1, block_size, width), lambda b, off, own, val: (b, 0, 0)),
            pl.BlockSpec((1, width, block_size), lambda b, off, own, val: (b, 0, 0)),
        ],
        out_specs=[
            pl.BlockSpec((requests, heads, 1, query_rows), lambda b, off, own, val: (0, 0, 0, 0)),
            pl.BlockSpec((requests, heads, 1, query_rows), lambda b, off, own, val: (0, 0, 0, 0)),
            pl.BlockSpec((requests, heads, HD, query_rows), lambda b, off, own, val: (0, 0, 0, 0)),
        ],
    )
    resident = 2 * requests * heads * (HD + 16) * query_rows * 4
    return pl.pallas_call(
        kernel,
        grid_spec=grid_spec,
        out_shape=[
            jax.ShapeDtypeStruct((requests, heads, 1, query_rows), jnp.float32),
            jax.ShapeDtypeStruct((requests, heads, 1, query_rows), jnp.float32),
            jax.ShapeDtypeStruct((requests, heads, HD, query_rows), jnp.float32),
        ],
        compiler_params=pltpu.CompilerParams(
            dimension_semantics=("arbitrary",),
            vmem_limit_bytes=resident + 24 * 1024 * 1024,
        ),
    )(owner_offset, owner, valid, ring_queries, keys, values_t)


def per_device(
    cycle,
    hidden,
    norm_gain,
    router_weight,
    att_experts,
    q_weight,
    kv_weight,
    o_weight,
    kv_cache,
    cached_blocks,
    tail_trim,
    block_pool,
):
    head_count = lax.axis_size("heads")
    seq_rank = lax.axis_index("seq")
    block_size = kv_cache.shape[2]
    local_blocks = kv_cache.shape[1]
    local_heads = q_weight.shape[2] // HD
    scale_q = HD ** (-0.5)
    normed = normalize(hidden[0], norm_gain)
    gathered = shift_all_gather(normed, "heads").reshape(-1, normed.shape[1])
    new_count = gathered.shape[0]
    rows_each = new_count // head_count
    head_rank = lax.axis_index("heads")
    token_ids = (
        ((head_rank + jnp.arange(head_count, dtype=jnp.int32)[:, None]) % head_count) * rows_each
        + jnp.arange(rows_each, dtype=jnp.int32)[None, :]
    ).reshape(new_count)
    chosen = jnp.take(att_experts[0], token_ids, axis=0)
    cached_len = cached_blocks * block_size - tail_trim
    positions = cached_len[seq_rank] + token_ids
    onehot, gates = route(gathered, router_weight, chosen)
    every_q = jnp.einsum("nd,edc->enc", gathered, q_weight, preferred_element_type=jnp.float32)
    half_dim = HD // 2
    inverse = 10000.0 ** (-2.0 * jnp.arange(half_dim, dtype=jnp.float32) / HD)
    angles = positions.astype(jnp.float32)[:, None] * inverse[None, :]
    cosine = jnp.tile(jnp.cos(angles), (1, 2 * local_heads))
    signed_sine = jnp.tile(
        jnp.concatenate([-jnp.sin(angles), jnp.sin(angles)], axis=-1), (1, local_heads)
    )
    slot_tables = []
    for slot in range(chosen.shape[1]):
        slot_q = jnp.sum(onehot[:, slot, :].T[:, :, None] * every_q, axis=0)
        swapped = jnp.concatenate(
            [
                part
                for h in range(local_heads)
                for part in (
                    slot_q[:, h * HD + half_dim:(h + 1) * HD],
                    slot_q[:, h * HD:h * HD + half_dim],
                )
            ],
            axis=-1,
        )
        slot_tables.append((slot_q * cosine + swapped * signed_sine).astype(jnp.bfloat16))
    queries = jnp.stack(slot_tables, axis=1).reshape(new_count, 2, local_heads, HD)
    fresh = jnp.einsum("nd,sdc->snc", gathered, kv_weight, preferred_element_type=jnp.float32)
    new_keys = rotate(fresh[0].reshape(new_count, local_heads, HD), positions).astype(jnp.bfloat16)
    new_values = fresh[1].reshape(new_count, local_heads, HD).astype(jnp.bfloat16)
    ring_queries = ring_all_gather(jnp.concatenate(slot_tables, axis=0), "seq", cycle)
    request_count = ring_queries.shape[0]
    ring_size = len(cycle)
    position_of = np.argsort(np.asarray(cycle))
    position = jnp.asarray(position_of, dtype=jnp.int32)[seq_rank]
    pool_size = block_pool.shape[0]

    global_ids = seq_rank * local_blocks + jnp.arange(local_blocks, dtype=jnp.int32)
    matches = block_pool[None, :] == global_ids[:, None]
    slot_of = jnp.sum(
        jnp.where(matches, jnp.arange(pool_size, dtype=jnp.int32)[None, :], 0), axis=1
    )
    starts = jnp.cumsum(cached_blocks) - cached_blocks
    owner = jnp.sum((starts[None, :] <= slot_of[:, None]).astype(jnp.int32), axis=1) - 1
    ordinal = slot_of - starts[owner]
    owns = owner[None, :] == jnp.arange(request_count, dtype=jnp.int32)[:, None]

    self_scores = (
        jnp.einsum("nkhc,thc->hnkt", queries, new_keys, preferred_element_type=jnp.float32)
        * scale_q
    )
    causal = token_ids[None, :] <= token_ids[:, None]
    self_scores = jnp.where(causal[None, :, None, :], self_scores, NEG_FILL)
    self_best = jnp.max(self_scores, axis=-1)
    self_weights = jnp.exp(self_scores - self_best[..., None])
    self_total = jnp.sum(self_weights, axis=-1)
    self_accum = jnp.einsum(
        "hnkt,thc->hnkc",
        self_weights.astype(jnp.bfloat16),
        new_values,
        preferred_element_type=jnp.float32,
    )
    self_best = jnp.transpose(self_best, (0, 2, 1))
    self_total = jnp.transpose(self_total, (0, 2, 1))
    self_accum = jnp.transpose(self_accum, (0, 3, 2, 1))
    ring_queries, self_best, self_total, self_accum = lax.optimization_barrier(
        (ring_queries, self_best, self_total, self_accum)
    )
    owner_offset = (jnp.asarray(position_of, dtype=jnp.int32)[owner] - position) % ring_size
    valid = jnp.clip(cached_len[owner] - ordinal * block_size, 0, block_size).astype(jnp.int32)
    query_rows = new_count * 2
    request_best, totals, accum = block_attention(
        ring_queries,
        kv_cache[0],
        jnp.swapaxes(kv_cache[1], 1, 2),
        owner_offset,
        owner,
        valid,
        request_count,
    )
    request_best = request_best[:, :, 0]
    best_hi, best_lo = split_bf16(request_best)
    request_ref = best_hi + best_lo
    present = request_best > 0.5 * NEG_FILL
    adjust = jnp.exp(jnp.where(present, request_best - request_ref, 0.0))
    totals = totals[:, :, 0] * adjust
    accum = accum * adjust[:, :, None, :]
    totals_hi, totals_lo = split_bf16(totals)
    stats = jnp.stack([best_hi, best_lo, totals_hi, totals_lo], axis=1).astype(jnp.bfloat16)
    payload = jnp.concatenate(
        [
            accum.astype(jnp.bfloat16).reshape(request_count, -1, query_rows),
            stats.reshape(request_count, -1, query_rows),
        ],
        axis=1,
    )
    received = lax.all_to_all(payload, "seq", 0, 0, tiled=True)
    acc_rows = local_heads * HD
    sources = received.shape[0]
    part_accum = received[:, :acc_rows].astype(jnp.float32).reshape(
        sources, local_heads, HD, query_rows
    )
    part_stats = received[:, acc_rows:].astype(jnp.float32).reshape(
        sources, 4, local_heads, query_rows
    )
    part_best = part_stats[:, 0] + part_stats[:, 1]
    part_totals = part_stats[:, 2] + part_stats[:, 3]
    cache_best = jnp.max(part_best, axis=0)
    share = jnp.exp(part_best - cache_best[None])
    cache_total = jnp.sum(part_totals * share, axis=0).reshape(local_heads, 2, new_count)
    cache_accum = jnp.sum(part_accum * share[:, :, None, :], axis=0).reshape(
        local_heads, HD, 2, new_count
    )
    cache_best = cache_best.reshape(local_heads, 2, new_count)

    peak = jnp.maximum(cache_best, self_best)
    cache_share = jnp.exp(cache_best - peak)
    self_share = jnp.exp(self_best - peak)
    numerator = cache_accum * cache_share[:, None] + self_accum * self_share[:, None]
    denominator = cache_total * cache_share + self_total * self_share
    attended = jnp.transpose(
        (numerator / denominator[:, None]).astype(jnp.bfloat16), (3, 2, 0, 1)
    ).reshape(new_count, 2, local_heads * HD)
    output_blocks = []
    for block in list(range(1, head_count)) + [0]:
        rows = slice(block * rows_each, (block + 1) * rows_each)
        block_out = jnp.zeros((rows_each, o_weight.shape[2]), jnp.float32)
        for expert in range(o_weight.shape[0]):
            weight_expert = jnp.sum(onehot[rows, :, expert] * gates[rows], axis=1)
            picked = jnp.where(
                chosen[rows, 0:1] == expert,
                attended[rows, 0],
                jnp.where(
                    chosen[rows, 1:2] == expert, attended[rows, 1], jnp.zeros_like(attended[rows, 0])
                ),
            )
            block_out = block_out + weight_expert[:, None] * jnp.dot(
                picked, o_weight[expert], preferred_element_type=jnp.float32
            )
        block_out = block_out.astype(jnp.bfloat16)
        block_out, attended = lax.optimization_barrier((block_out, attended))
        output_blocks.append(block_out)
    summed = shift_reduce_scatter(output_blocks[-1:] + output_blocks[:-1], "heads")
    return summed[None].astype(jnp.bfloat16)


def solution(mesh):
    return jax.shard_map(
        functools.partial(per_device, tuple(seq_cycle(mesh))),
        mesh=mesh,
        in_specs=(
            P("seq", "heads", None),
            P(),
            P(),
            P("seq", None, None),
            P(None, None, "heads"),
            P(None, None, "heads"),
            P(None, "heads", None),
            P(None, "seq", None, "heads"),
            P(),
            P(),
            P(),
        ),
        out_specs=P("seq", "heads", None),
        check_vma=False,
    )
```

```python
import functools

import numpy as np
import jax
import jax.numpy as jnp
from jax import lax
from jax.experimental import pallas as pl
from jax.experimental.pallas import tpu as pltpu
from jax.sharding import PartitionSpec as P

HD = 128


NEG_FILL = -1e30


def rotate(values, positions):
    half_dim = values.shape[-1] // 2
    inverse = 10000.0 ** (-2.0 * jnp.arange(half_dim, dtype=jnp.float32) / values.shape[-1])
    angles = positions.astype(jnp.float32)[:, None] * inverse[None, :]
    target = (values.shape[0],) + (1,) * (values.ndim - 2) + (half_dim,)
    cosine = jnp.cos(angles).reshape(target)
    sine_part = jnp.sin(angles).reshape(target)
    leading_part = values[..., :half_dim]
    trailing_part = values[..., half_dim:]
    return jnp.concatenate(
        [
            leading_part * cosine - trailing_part * sine_part,
            trailing_part * cosine + leading_part * sine_part,
        ],
        axis=-1,
    )


def normalize(rows, norm_gain):
    wide_rows = rows.astype(jnp.float32)
    scaled = wide_rows * lax.rsqrt(jnp.mean(wide_rows * wide_rows, axis=-1, keepdims=True) + 1e-05)
    return (scaled * norm_gain.astype(jnp.float32)).astype(jnp.bfloat16)


def route(normed, router_weight, chosen):
    logits = jnp.dot(normed, router_weight, preferred_element_type=jnp.float32)
    experts_all = router_weight.shape[1]
    onehot = (chosen[:, :, None] == jnp.arange(experts_all, dtype=jnp.int32)[None, None, :]).astype(
        jnp.float32
    )
    picked = jnp.sum(onehot * logits[:, None, :], axis=-1)
    return (onehot, jax.nn.softmax(picked, axis=-1))


def split_bf16(x):
    hi = lax.reduce_precision(x, exponent_bits=8, mantissa_bits=7)
    lo = lax.reduce_precision(x - hi, exponent_bits=8, mantissa_bits=7)
    return hi, lo


def seq_cycle(mesh):
    size = mesh.shape["seq"]
    plain = list(range(size))
    try:
        devices = np.moveaxis(np.asarray(mesh.devices), mesh.axis_names.index("seq"), -1)
        line = devices.reshape(-1, size)[0]
        coords = np.array([list(d.coords) for d in line])
    except Exception:
        return plain
    varying = [k for k in range(coords.shape[1]) if len(set(coords[:, k])) > 1]
    if len(varying) == 1:
        order = sorted(plain, key=lambda j: coords[j, varying[0]])
        return order[0::2] + order[1::2][::-1]
    if len(varying) != 2:
        return plain
    dim_a, dim_b = varying
    values_a = sorted(set(coords[:, dim_a]))
    values_b = sorted(set(coords[:, dim_b]))
    if len(values_a) % 2:
        dim_a, dim_b, values_a, values_b = dim_b, dim_a, values_b, values_a
    if len(values_a) % 2 or len(values_a) * len(values_b) != size:
        return plain
    at = {(coords[j, dim_a], coords[j, dim_b]): j for j in plain}
    cycle = [at[(a, values_b[0])] for a in values_a]
    for row, a in enumerate(reversed(values_a)):
        columns = values_b[1:] if row % 2 == 0 else values_b[1:][::-1]
        cycle += [at[(a, b)] for b in columns]
    if sorted(cycle) != plain:
        return plain
    return cycle


def shift_all_gather(piece, axis_name):
    size = lax.axis_size(axis_name)
    rank = lax.axis_index(axis_name)
    by_offset = [piece] + [
        lax.ppermute(piece, axis_name, [(i, (i + s) % size) for i in range(size)])
        for s in range(1, size)
    ]
    return jnp.stack(by_offset[:1] + by_offset[1:][::-1], axis=0)


def shift_reduce_scatter(blocks, axis_name):
    size = lax.axis_size(axis_name)
    total = blocks[0].astype(jnp.float32)
    for s in range(1, size):
        moved = lax.ppermute(blocks[s], axis_name, [(i, (i + s) % size) for i in range(size)])
        total = total + moved.astype(jnp.float32)
    return total


def ring_all_gather(piece, axis_name, cycle):
    size = len(cycle)
    forward = [(cycle[i], cycle[(i + 1) % size]) for i in range(size)]
    backward = [(cycle[(i + 1) % size], cycle[i]) for i in range(size)]
    ahead = size // 2
    behind = size - 1 - ahead
    from_behind, from_ahead = [], []
    moving = piece
    for _ in range(ahead):
        moving = lax.ppermute(moving, axis_name, forward)
        from_behind.append(moving)
    moving = piece
    for _ in range(behind):
        moving = lax.ppermute(moving, axis_name, backward)
        from_ahead.append(moving)
    return jnp.stack([piece] + from_ahead + from_behind[::-1], axis=0)


def block_attention(ring_queries, keys, values_t, owner_offset, owner, valid, requests):
    blocks, block_size, width = keys.shape
    query_rows = ring_queries.shape[1]
    heads = width // HD
    scale = HD ** (-0.5)

    def kernel(offset_ref, owner_ref, valid_ref, q_ref, k_ref, v_ref, best_ref, total_ref, accum_ref):
        b = pl.program_id(0)

        @pl.when(b == 0)
        def _():
            best_ref[...] = jnp.full(best_ref.shape, NEG_FILL, jnp.float32)
            total_ref[...] = jnp.zeros(total_ref.shape, jnp.float32)
            accum_ref[...] = jnp.zeros(accum_ref.shape, jnp.float32)

        request = owner_ref[b]
        limit = valid_ref[b]
        row = lax.broadcasted_iota(jnp.int32, (block_size, query_rows), 0)
        for h in range(heads):
            q = q_ref[0, :, h * HD:(h + 1) * HD]
            k = k_ref[0, :, h * HD:(h + 1) * HD]
            scores = lax.dot_general(
                k, q, (((1,), (1,)), ((), ())), preferred_element_type=jnp.float32
            ) * scale
            scores = jnp.where(row < limit, scores, NEG_FILL)
            old_best = best_ref[request, h]
            new_best = jnp.maximum(old_best, jnp.max(scores, axis=0, keepdims=True))
            rescale = jnp.exp(old_best - new_best)
            weights = jnp.exp(scores - new_best)
            best_ref[request, h] = new_best
            total_ref[request, h] = total_ref[request, h] * rescale + jnp.sum(
                weights, axis=0, keepdims=True
            )
            v_t = v_ref[0, h * HD:(h + 1) * HD, :]
            accum_ref[request, h] = accum_ref[request, h] * rescale + jnp.dot(
                v_t, weights.astype(jnp.bfloat16), preferred_element_type=jnp.float32
            )

    grid_spec = pltpu.PrefetchScalarGridSpec(
        num_scalar_prefetch=3,
        grid=(blocks,),
        in_specs=[
            pl.BlockSpec((1, query_rows, width), lambda b, off, own, val: (off[b], 0, 0)),
            pl.BlockSpec((1, block_size, width), lambda b, off, own, val: (b, 0, 0)),
            pl.BlockSpec((1, width, block_size), lambda b, off, own, val: (b, 0, 0)),
        ],
        out_specs=[
            pl.BlockSpec((requests, heads, 1, query_rows), lambda b, off, own, val: (0, 0, 0, 0)),
            pl.BlockSpec((requests, heads, 1, query_rows), lambda b, off, own, val: (0, 0, 0, 0)),
            pl.BlockSpec((requests, heads, HD, query_rows), lambda b, off, own, val: (0, 0, 0, 0)),
        ],
    )
    resident = 2 * requests * heads * (HD + 16) * query_rows * 4
    return pl.pallas_call(
        kernel,
        grid_spec=grid_spec,
        out_shape=[
            jax.ShapeDtypeStruct((requests, heads, 1, query_rows), jnp.float32),
            jax.ShapeDtypeStruct((requests, heads, 1, query_rows), jnp.float32),
            jax.ShapeDtypeStruct((requests, heads, HD, query_rows), jnp.float32),
        ],
        compiler_params=pltpu.CompilerParams(
            dimension_semantics=("arbitrary",),
            vmem_limit_bytes=resident + 24 * 1024 * 1024,
        ),
    )(owner_offset, owner, valid, ring_queries, keys, values_t)


def per_device(
    cycle,
    hidden,
    norm_gain,
    router_weight,
    att_experts,
    q_weight,
    kv_weight,
    o_weight,
    kv_cache,
    cached_blocks,
    tail_trim,
    block_pool,
):
    head_count = lax.axis_size("heads")
    seq_rank = lax.axis_index("seq")
    block_size = kv_cache.shape[2]
    local_blocks = kv_cache.shape[1]
    local_heads = q_weight.shape[2] // HD
    scale_q = HD ** (-0.5)
    normed = normalize(hidden[0], norm_gain)
    gathered = shift_all_gather(normed, "heads").reshape(-1, normed.shape[1])
    new_count = gathered.shape[0]
    rows_each = new_count // head_count
    head_rank = lax.axis_index("heads")
    token_ids = (
        ((head_rank + jnp.arange(head_count, dtype=jnp.int32)[:, None]) % head_count) * rows_each
        + jnp.arange(rows_each, dtype=jnp.int32)[None, :]
    ).reshape(new_count)
    chosen = jnp.take(att_experts[0], token_ids, axis=0)
    cached_len = cached_blocks * block_size - tail_trim
    positions = cached_len[seq_rank] + token_ids
    onehot, gates = route(gathered, router_weight, chosen)
    every_q = jnp.einsum("nd,edc->enc", gathered, q_weight, preferred_element_type=jnp.float32)
    half_dim = HD // 2
    inverse = 10000.0 ** (-2.0 * jnp.arange(half_dim, dtype=jnp.float32) / HD)
    angles = positions.astype(jnp.float32)[:, None] * inverse[None, :]
    cosine = jnp.tile(jnp.cos(angles), (1, 2 * local_heads))
    signed_sine = jnp.tile(
        jnp.concatenate([-jnp.sin(angles), jnp.sin(angles)], axis=-1), (1, local_heads)
    )
    slot_tables = []
    for slot in range(chosen.shape[1]):
        slot_q = jnp.sum(onehot[:, slot, :].T[:, :, None] * every_q, axis=0)
        swapped = jnp.concatenate(
            [
                part
                for h in range(local_heads)
                for part in (
                    slot_q[:, h * HD + half_dim:(h + 1) * HD],
                    slot_q[:, h * HD:h * HD + half_dim],
                )
            ],
            axis=-1,
        )
        slot_tables.append((slot_q * cosine + swapped * signed_sine).astype(jnp.bfloat16))
    queries = jnp.stack(slot_tables, axis=1).reshape(new_count, 2, local_heads, HD)
    kv_input, slot_tables = lax.optimization_barrier((gathered, slot_tables))
    fresh = jnp.einsum("nd,sdc->snc", kv_input, kv_weight, preferred_element_type=jnp.float32)
    new_keys = rotate(fresh[0].reshape(new_count, local_heads, HD), positions).astype(jnp.bfloat16)
    new_values = fresh[1].reshape(new_count, local_heads, HD).astype(jnp.bfloat16)
    ring_queries = ring_all_gather(jnp.concatenate(slot_tables, axis=0), "seq", cycle)
    request_count = ring_queries.shape[0]
    ring_size = len(cycle)
    position_of = np.argsort(np.asarray(cycle))
    position = jnp.asarray(position_of, dtype=jnp.int32)[seq_rank]
    pool_size = block_pool.shape[0]

    global_ids = seq_rank * local_blocks + jnp.arange(local_blocks, dtype=jnp.int32)
    matches = block_pool[None, :] == global_ids[:, None]
    slot_of = jnp.sum(
        jnp.where(matches, jnp.arange(pool_size, dtype=jnp.int32)[None, :], 0), axis=1
    )
    starts = jnp.cumsum(cached_blocks) - cached_blocks
    owner = jnp.sum((starts[None, :] <= slot_of[:, None]).astype(jnp.int32), axis=1) - 1
    ordinal = slot_of - starts[owner]
    owns = owner[None, :] == jnp.arange(request_count, dtype=jnp.int32)[:, None]

    self_scores = (
        jnp.einsum("nkhc,thc->hnkt", queries, new_keys, preferred_element_type=jnp.float32)
        * scale_q
    )
    causal = token_ids[None, :] <= token_ids[:, None]
    self_scores = jnp.where(causal[None, :, None, :], self_scores, NEG_FILL)
    self_best = jnp.max(self_scores, axis=-1)
    self_weights = jnp.exp(self_scores - self_best[..., None])
    self_total = jnp.sum(self_weights, axis=-1)
    self_accum = jnp.einsum(
        "hnkt,thc->hnkc",
        self_weights.astype(jnp.bfloat16),
        new_values,
        preferred_element_type=jnp.float32,
    )
    ring_queries, self_best, self_total, self_accum = lax.optimization_barrier(
        (ring_queries, self_best, self_total, self_accum)
    )
    owner_offset = (jnp.asarray(position_of, dtype=jnp.int32)[owner] - position) % ring_size
    valid = jnp.clip(cached_len[owner] - ordinal * block_size, 0, block_size).astype(jnp.int32)
    query_rows = new_count * 2
    request_best, totals, accum = block_attention(
        ring_queries,
        kv_cache[0],
        jnp.swapaxes(kv_cache[1], 1, 2),
        owner_offset,
        owner,
        valid,
        request_count,
    )
    request_best = request_best[:, :, 0]
    best_hi, best_lo = split_bf16(request_best)
    request_ref = best_hi + best_lo
    present = request_best > 0.5 * NEG_FILL
    adjust = jnp.exp(jnp.where(present, request_best - request_ref, 0.0))
    totals = totals[:, :, 0] * adjust
    accum = accum * adjust[:, :, None, :]
    totals_hi, totals_lo = split_bf16(totals)
    stats = jnp.stack([best_hi, best_lo, totals_hi, totals_lo], axis=1).astype(jnp.bfloat16)
    payload = jnp.concatenate(
        [
            accum.astype(jnp.bfloat16).reshape(request_count, -1, query_rows),
            stats.reshape(request_count, -1, query_rows),
        ],
        axis=1,
    )
    received = lax.all_to_all(payload, "seq", 0, 0, tiled=True)
    acc_rows = local_heads * HD
    sources = received.shape[0]
    part_accum = received[:, :acc_rows].astype(jnp.float32).reshape(
        sources, local_heads, HD, query_rows
    )
    part_stats = received[:, acc_rows:].astype(jnp.float32).reshape(
        sources, 4, local_heads, query_rows
    )
    part_best = part_stats[:, 0] + part_stats[:, 1]
    part_totals = part_stats[:, 2] + part_stats[:, 3]
    cache_best = jnp.max(part_best, axis=0)
    share = jnp.exp(part_best - cache_best[None])
    cache_total = jnp.swapaxes(
        jnp.sum(part_totals * share, axis=0).reshape(local_heads, 2, new_count), 1, 2
    )
    cache_accum = jnp.transpose(
        jnp.sum(part_accum * share[:, :, None, :], axis=0).reshape(local_heads, HD, 2, new_count),
        (0, 3, 2, 1),
    )
    cache_best = jnp.swapaxes(cache_best.reshape(local_heads, 2, new_count), 1, 2)

    peak = jnp.maximum(cache_best, self_best)
    cache_share = jnp.exp(cache_best - peak)
    self_share = jnp.exp(self_best - peak)
    numerator = cache_accum * cache_share[..., None] + self_accum * self_share[..., None]
    denominator = cache_total * cache_share + self_total * self_share
    attended = (
        jnp.transpose((numerator / denominator[..., None]).astype(jnp.bfloat16), (1, 2, 0, 3))
        .reshape(new_count, 2, local_heads * HD)
    )
    output_blocks = []
    for block in list(range(1, head_count)) + [0]:
        rows = slice(block * rows_each, (block + 1) * rows_each)
        block_out = jnp.zeros((rows_each, o_weight.shape[2]), jnp.float32)
        for expert in range(o_weight.shape[0]):
            weight_expert = jnp.sum(onehot[rows, :, expert] * gates[rows], axis=1)
            picked = jnp.where(
                chosen[rows, 0:1] == expert,
                attended[rows, 0],
                jnp.where(
                    chosen[rows, 1:2] == expert, attended[rows, 1], jnp.zeros_like(attended[rows, 0])
                ),
            )
            block_out = block_out + weight_expert[:, None] * jnp.dot(
                picked, o_weight[expert], preferred_element_type=jnp.float32
            )
        block_out = block_out.astype(jnp.bfloat16)
        block_out, attended = lax.optimization_barrier((block_out, attended))
        output_blocks.append(block_out)
    summed = shift_reduce_scatter(output_blocks[-1:] + output_blocks[:-1], "heads")
    return summed[None].astype(jnp.bfloat16)


def solution(mesh):
    return jax.shard_map(
        functools.partial(per_device, tuple(seq_cycle(mesh))),
        mesh=mesh,
        in_specs=(
            P("seq", "heads", None),
            P(),
            P(),
            P("seq", None, None),
            P(None, None, "heads"),
            P(None, None, "heads"),
            P(None, "heads", None),
            P(None, "seq", None, "heads"),
            P(),
            P(),
            P(),
        ),
        out_specs=P("seq", "heads", None),
        check_vma=False,
    )
```

```python
import functools

import numpy as np
import jax
import jax.numpy as jnp
from jax import lax
from jax.experimental import pallas as pl
from jax.experimental.pallas import tpu as pltpu
from jax.sharding import PartitionSpec as P

HD = 128


NEG_FILL = -1e30


def rotate(values, positions):
    half_dim = values.shape[-1] // 2
    inverse = 10000.0 ** (-2.0 * jnp.arange(half_dim, dtype=jnp.float32) / values.shape[-1])
    angles = positions.astype(jnp.float32)[:, None] * inverse[None, :]
    target = (values.shape[0],) + (1,) * (values.ndim - 2) + (half_dim,)
    cosine = jnp.cos(angles).reshape(target)
    sine_part = jnp.sin(angles).reshape(target)
    leading_part = values[..., :half_dim]
    trailing_part = values[..., half_dim:]
    return jnp.concatenate(
        [
            leading_part * cosine - trailing_part * sine_part,
            trailing_part * cosine + leading_part * sine_part,
        ],
        axis=-1,
    )


def normalize(rows, norm_gain):
    wide_rows = rows.astype(jnp.float32)
    scaled = wide_rows * lax.rsqrt(jnp.mean(wide_rows * wide_rows, axis=-1, keepdims=True) + 1e-05)
    return (scaled * norm_gain.astype(jnp.float32)).astype(jnp.bfloat16)


def route(normed, router_weight, chosen):
    logits = jnp.dot(normed, router_weight, preferred_element_type=jnp.float32)
    experts_all = router_weight.shape[1]
    onehot = (chosen[:, :, None] == jnp.arange(experts_all, dtype=jnp.int32)[None, None, :]).astype(
        jnp.float32
    )
    picked = jnp.sum(onehot * logits[:, None, :], axis=-1)
    return (onehot, jax.nn.softmax(picked, axis=-1))


def split_bf16(x):
    hi = lax.reduce_precision(x, exponent_bits=8, mantissa_bits=7)
    lo = lax.reduce_precision(x - hi, exponent_bits=8, mantissa_bits=7)
    return hi, lo


def seq_cycle(mesh):
    size = mesh.shape["seq"]
    plain = list(range(size))
    try:
        devices = np.moveaxis(np.asarray(mesh.devices), mesh.axis_names.index("seq"), -1)
        line = devices.reshape(-1, size)[0]
        coords = np.array([list(d.coords) for d in line])
    except Exception:
        return plain
    varying = [k for k in range(coords.shape[1]) if len(set(coords[:, k])) > 1]
    if len(varying) == 1:
        order = sorted(plain, key=lambda j: coords[j, varying[0]])
        return order[0::2] + order[1::2][::-1]
    if len(varying) != 2:
        return plain
    dim_a, dim_b = varying
    values_a = sorted(set(coords[:, dim_a]))
    values_b = sorted(set(coords[:, dim_b]))
    if len(values_a) % 2:
        dim_a, dim_b, values_a, values_b = dim_b, dim_a, values_b, values_a
    if len(values_a) % 2 or len(values_a) * len(values_b) != size:
        return plain
    at = {(coords[j, dim_a], coords[j, dim_b]): j for j in plain}
    cycle = [at[(a, values_b[0])] for a in values_a]
    for row, a in enumerate(reversed(values_a)):
        columns = values_b[1:] if row % 2 == 0 else values_b[1:][::-1]
        cycle += [at[(a, b)] for b in columns]
    if sorted(cycle) != plain:
        return plain
    return cycle


def shift_all_gather(piece, axis_name):
    size = lax.axis_size(axis_name)
    rank = lax.axis_index(axis_name)
    copies = jnp.broadcast_to(piece[None], (size,) + piece.shape)
    everyone = lax.all_to_all(copies, axis_name, 0, 0, tiled=True)
    return jnp.take(everyone, (rank + jnp.arange(size, dtype=jnp.int32)) % size, axis=0)


def shift_reduce_scatter(blocks, axis_name):
    size = lax.axis_size(axis_name)
    total = blocks[0].astype(jnp.float32)
    for s in range(1, size):
        moved = lax.ppermute(blocks[s], axis_name, [(i, (i + s) % size) for i in range(size)])
        total = total + moved.astype(jnp.float32)
    return total


def ring_all_gather(piece, axis_name, cycle):
    size = len(cycle)
    forward = [(cycle[i], cycle[(i + 1) % size]) for i in range(size)]
    backward = [(cycle[(i + 1) % size], cycle[i]) for i in range(size)]
    ahead = size // 2
    behind = size - 1 - ahead
    from_behind, from_ahead = [], []
    moving = piece
    for _ in range(ahead):
        moving = lax.ppermute(moving, axis_name, forward)
        from_behind.append(moving)
    moving = piece
    for _ in range(behind):
        moving = lax.ppermute(moving, axis_name, backward)
        from_ahead.append(moving)
    return jnp.stack([piece] + from_ahead + from_behind[::-1], axis=0)


def block_attention(ring_queries, keys, values_t, owner_offset, owner, valid, requests):
    blocks, block_size, width = keys.shape
    query_rows = ring_queries.shape[1]
    heads = width // HD
    scale = HD ** (-0.5)

    def kernel(offset_ref, owner_ref, valid_ref, q_ref, k_ref, v_ref, best_ref, total_ref, accum_ref):
        b = pl.program_id(0)

        @pl.when(b == 0)
        def _():
            best_ref[...] = jnp.full(best_ref.shape, NEG_FILL, jnp.float32)
            total_ref[...] = jnp.zeros(total_ref.shape, jnp.float32)
            accum_ref[...] = jnp.zeros(accum_ref.shape, jnp.float32)

        request = owner_ref[b]
        limit = valid_ref[b]
        row = lax.broadcasted_iota(jnp.int32, (block_size, query_rows), 0)
        for h in range(heads):
            q = q_ref[0, :, h * HD:(h + 1) * HD]
            k = k_ref[0, :, h * HD:(h + 1) * HD]
            scores = lax.dot_general(
                k, q, (((1,), (1,)), ((), ())), preferred_element_type=jnp.float32
            ) * scale
            scores = jnp.where(row < limit, scores, NEG_FILL)
            old_best = best_ref[request, h]
            new_best = jnp.maximum(old_best, jnp.max(scores, axis=0, keepdims=True))
            rescale = jnp.exp(old_best - new_best)
            weights = jnp.exp(scores - new_best)
            best_ref[request, h] = new_best
            total_ref[request, h] = total_ref[request, h] * rescale + jnp.sum(
                weights, axis=0, keepdims=True
            )
            v_t = v_ref[0, h * HD:(h + 1) * HD, :]
            accum_ref[request, h] = accum_ref[request, h] * rescale + jnp.dot(
                v_t, weights.astype(jnp.bfloat16), preferred_element_type=jnp.float32
            )

    grid_spec = pltpu.PrefetchScalarGridSpec(
        num_scalar_prefetch=3,
        grid=(blocks,),
        in_specs=[
            pl.BlockSpec((1, query_rows, width), lambda b, off, own, val: (off[b], 0, 0)),
            pl.BlockSpec((1, block_size, width), lambda b, off, own, val: (b, 0, 0)),
            pl.BlockSpec((1, width, block_size), lambda b, off, own, val: (b, 0, 0)),
        ],
        out_specs=[
            pl.BlockSpec((requests, heads, 1, query_rows), lambda b, off, own, val: (0, 0, 0, 0)),
            pl.BlockSpec((requests, heads, 1, query_rows), lambda b, off, own, val: (0, 0, 0, 0)),
            pl.BlockSpec((requests, heads, HD, query_rows), lambda b, off, own, val: (0, 0, 0, 0)),
        ],
    )
    resident = 2 * requests * heads * (HD + 16) * query_rows * 4
    return pl.pallas_call(
        kernel,
        grid_spec=grid_spec,
        out_shape=[
            jax.ShapeDtypeStruct((requests, heads, 1, query_rows), jnp.float32),
            jax.ShapeDtypeStruct((requests, heads, 1, query_rows), jnp.float32),
            jax.ShapeDtypeStruct((requests, heads, HD, query_rows), jnp.float32),
        ],
        compiler_params=pltpu.CompilerParams(
            dimension_semantics=("arbitrary",),
            vmem_limit_bytes=resident + 24 * 1024 * 1024,
        ),
    )(owner_offset, owner, valid, ring_queries, keys, values_t)


def per_device(
    cycle,
    hidden,
    norm_gain,
    router_weight,
    att_experts,
    q_weight,
    kv_weight,
    o_weight,
    kv_cache,
    cached_blocks,
    tail_trim,
    block_pool,
):
    head_count = lax.axis_size("heads")
    seq_rank = lax.axis_index("seq")
    block_size = kv_cache.shape[2]
    local_blocks = kv_cache.shape[1]
    local_heads = q_weight.shape[2] // HD
    scale_q = HD ** (-0.5)
    normed = normalize(hidden[0], norm_gain)
    gathered = shift_all_gather(normed, "heads").reshape(-1, normed.shape[1])
    new_count = gathered.shape[0]
    rows_each = new_count // head_count
    head_rank = lax.axis_index("heads")
    token_ids = (
        ((head_rank + jnp.arange(head_count, dtype=jnp.int32)[:, None]) % head_count) * rows_each
        + jnp.arange(rows_each, dtype=jnp.int32)[None, :]
    ).reshape(new_count)
    chosen = jnp.take(att_experts[0], token_ids, axis=0)
    cached_len = cached_blocks * block_size - tail_trim
    positions = cached_len[seq_rank] + token_ids
    onehot, gates = route(gathered, router_weight, chosen)
    every_q = jnp.einsum("nd,edc->enc", gathered, q_weight, preferred_element_type=jnp.float32)
    half_dim = HD // 2
    inverse = 10000.0 ** (-2.0 * jnp.arange(half_dim, dtype=jnp.float32) / HD)
    angles = positions.astype(jnp.float32)[:, None] * inverse[None, :]
    cosine = jnp.tile(jnp.cos(angles), (1, 2 * local_heads))
    signed_sine = jnp.tile(
        jnp.concatenate([-jnp.sin(angles), jnp.sin(angles)], axis=-1), (1, local_heads)
    )
    slot_tables = []
    for slot in range(chosen.shape[1]):
        slot_q = jnp.sum(onehot[:, slot, :].T[:, :, None] * every_q, axis=0)
        swapped = jnp.concatenate(
            [
                part
                for h in range(local_heads)
                for part in (
                    slot_q[:, h * HD + half_dim:(h + 1) * HD],
                    slot_q[:, h * HD:h * HD + half_dim],
                )
            ],
            axis=-1,
        )
        slot_tables.append((slot_q * cosine + swapped * signed_sine).astype(jnp.bfloat16))
    queries = jnp.stack(slot_tables, axis=1).reshape(new_count, 2, local_heads, HD)
    fresh = jnp.einsum("nd,sdc->snc", gathered, kv_weight, preferred_element_type=jnp.float32)
    new_keys = rotate(fresh[0].reshape(new_count, local_heads, HD), positions).astype(jnp.bfloat16)
    new_values = fresh[1].reshape(new_count, local_heads, HD).astype(jnp.bfloat16)
    ring_queries = ring_all_gather(jnp.concatenate(slot_tables, axis=0), "seq", cycle)
    request_count = ring_queries.shape[0]
    ring_size = len(cycle)
    position_of = np.argsort(np.asarray(cycle))
    position = jnp.asarray(position_of, dtype=jnp.int32)[seq_rank]
    pool_size = block_pool.shape[0]

    global_ids = seq_rank * local_blocks + jnp.arange(local_blocks, dtype=jnp.int32)
    matches = block_pool[None, :] == global_ids[:, None]
    slot_of = jnp.sum(
        jnp.where(matches, jnp.arange(pool_size, dtype=jnp.int32)[None, :], 0), axis=1
    )
    starts = jnp.cumsum(cached_blocks) - cached_blocks
    owner = jnp.sum((starts[None, :] <= slot_of[:, None]).astype(jnp.int32), axis=1) - 1
    ordinal = slot_of - starts[owner]
    owns = owner[None, :] == jnp.arange(request_count, dtype=jnp.int32)[:, None]

    self_scores = (
        jnp.einsum("nkhc,thc->hnkt", queries, new_keys, preferred_element_type=jnp.float32)
        * scale_q
    )
    causal = token_ids[None, :] <= token_ids[:, None]
    self_scores = jnp.where(causal[None, :, None, :], self_scores, NEG_FILL)
    self_best = jnp.max(self_scores, axis=-1)
    self_weights = jnp.exp(self_scores - self_best[..., None])
    self_total = jnp.sum(self_weights, axis=-1)
    self_accum = jnp.einsum(
        "hnkt,thc->hnkc",
        self_weights.astype(jnp.bfloat16),
        new_values,
        preferred_element_type=jnp.float32,
    )
    ring_queries, self_best, self_total, self_accum = lax.optimization_barrier(
        (ring_queries, self_best, self_total, self_accum)
    )
    owner_offset = (jnp.asarray(position_of, dtype=jnp.int32)[owner] - position) % ring_size
    valid = jnp.clip(cached_len[owner] - ordinal * block_size, 0, block_size).astype(jnp.int32)
    query_rows = new_count * 2
    request_best, totals, accum = block_attention(
        ring_queries,
        kv_cache[0],
        jnp.swapaxes(kv_cache[1], 1, 2),
        owner_offset,
        owner,
        valid,
        request_count,
    )
    request_best = request_best[:, :, 0]
    best_hi, best_lo = split_bf16(request_best)
    request_ref = best_hi + best_lo
    present = request_best > 0.5 * NEG_FILL
    adjust = jnp.exp(jnp.where(present, request_best - request_ref, 0.0))
    totals = totals[:, :, 0] * adjust
    accum = accum * adjust[:, :, None, :]
    totals_hi, totals_lo = split_bf16(totals)
    stats = jnp.stack([best_hi, best_lo, totals_hi, totals_lo], axis=1).astype(jnp.bfloat16)
    payload = jnp.concatenate(
        [
            accum.astype(jnp.bfloat16).reshape(request_count, -1, query_rows),
            stats.reshape(request_count, -1, query_rows),
        ],
        axis=1,
    )
    received = lax.all_to_all(payload, "seq", 0, 0, tiled=True)
    acc_rows = local_heads * HD
    sources = received.shape[0]
    part_accum = received[:, :acc_rows].astype(jnp.float32).reshape(
        sources, local_heads, HD, query_rows
    )
    part_stats = received[:, acc_rows:].astype(jnp.float32).reshape(
        sources, 4, local_heads, query_rows
    )
    part_best = part_stats[:, 0] + part_stats[:, 1]
    part_totals = part_stats[:, 2] + part_stats[:, 3]
    cache_best = jnp.max(part_best, axis=0)
    share = jnp.exp(part_best - cache_best[None])
    cache_total = jnp.swapaxes(
        jnp.sum(part_totals * share, axis=0).reshape(local_heads, 2, new_count), 1, 2
    )
    cache_accum = jnp.transpose(
        jnp.sum(part_accum * share[:, :, None, :], axis=0).reshape(local_heads, HD, 2, new_count),
        (0, 3, 2, 1),
    )
    cache_best = jnp.swapaxes(cache_best.reshape(local_heads, 2, new_count), 1, 2)

    peak = jnp.maximum(cache_best, self_best)
    cache_share = jnp.exp(cache_best - peak)
    self_share = jnp.exp(self_best - peak)
    numerator = cache_accum * cache_share[..., None] + self_accum * self_share[..., None]
    denominator = cache_total * cache_share + self_total * self_share
    attended = (
        jnp.transpose((numerator / denominator[..., None]).astype(jnp.bfloat16), (1, 2, 0, 3))
        .reshape(new_count, 2, local_heads * HD)
    )
    output_blocks = []
    for block in list(range(1, head_count)) + [0]:
        rows = slice(block * rows_each, (block + 1) * rows_each)
        block_out = jnp.zeros((rows_each, o_weight.shape[2]), jnp.float32)
        for expert in range(o_weight.shape[0]):
            weight_expert = jnp.sum(onehot[rows, :, expert] * gates[rows], axis=1)
            picked = jnp.where(
                chosen[rows, 0:1] == expert,
                attended[rows, 0],
                jnp.where(
                    chosen[rows, 1:2] == expert, attended[rows, 1], jnp.zeros_like(attended[rows, 0])
                ),
            )
            block_out = block_out + weight_expert[:, None] * jnp.dot(
                picked, o_weight[expert], preferred_element_type=jnp.float32
            )
        block_out = block_out.astype(jnp.bfloat16)
        block_out, attended = lax.optimization_barrier((block_out, attended))
        output_blocks.append(block_out)
    summed = shift_reduce_scatter(output_blocks[-1:] + output_blocks[:-1], "heads")
    return summed[None].astype(jnp.bfloat16)


def solution(mesh):
    return jax.shard_map(
        functools.partial(per_device, tuple(seq_cycle(mesh))),
        mesh=mesh,
        in_specs=(
            P("seq", "heads", None),
            P(),
            P(),
            P("seq", None, None),
            P(None, None, "heads"),
            P(None, None, "heads"),
            P(None, "heads", None),
            P(None, "seq", None, "heads"),
            P(),
            P(),
            P(),
        ),
        out_specs=P("seq", "heads", None),
        check_vma=False,
    )
```
